32 devices in a mesh: az: 8 (over z, y), ax: 4 (over x, core).
Axes of the slice: x: 2, y: 2, z: 4, core: 2. Of those that a mesh axis runs over, the one named last changes fastest.
Arguments:
- acoustic: float32 [4, 64, 64, 128], P(None, 'az', 'ax'), may hold values from -6 to 6
- mean_flow: float32 [4, 64, 64, 128], P(None, 'az', 'ax'), may hold values from -0.4 to 2, as said below
- adjoint_in: float32 [4, 64, 64, 128], P(None, 'az', 'ax'), may hold values from -6 to 6
- admittance: float32 [64], replicated, may hold values from 0.2 to 2
- segment_id: int32 [64, 64], P('az', 'ax'), may hold values from 0 to 63, as said below
- noise_code: int32 [64, 64], P('az', 'ax'), may hold values from 0 to 63
- noise_table: float32 [64], replicated, may hold values from -4 to 4
- mic_az: int32 [512], replicated, may hold values from 0 to 63, as said below
- mic_ax: int32 [512], replicated, may hold values from 0 to 63
- measured: float32 [512], replicated, may hold values from -17 to 17
Outputs:
- adjoint_out: float32 [4, 64, 64, 128], P(None, 'az', 'ax')
- liner_grad: float32 [64], replicated
- misfit: float32 [], replicated
The draws below stay inside these ranges and needn't reach their ends.
Inputs may be any that keep to these rules, and one draw needn't show every extreme that they name: `mean_flow`: component 0 lies in 0.2 to 0.6, component 1 in -0.4 to 0.4, component 2 in 0.5 to 2, component 3 in 0.7 to 1.4. segment_id = sector * 4 + band, where the 16 sectors are runs of contiguous azimuthal cells (wrapping) and the 4 bands runs of contiguous axial cells; every segment has cells. `mic_az`: microphones sit on casing cells; several may share a cell.
All inputs are finite; a program needn't handle non-finite values.
Results may differ from the reference program's by a relative error of at most 0.000086.
Values sent between devices are 32-bit elements; how exact they have to be, the bound alone decides.
No kernel may reach another device: no remote copies, remote signals or barrier semaphores. Data moves between devices by JAX's collectives and lax.ppermute only.
A program may use at most 128 MiB of HBM per device.

```python
import math
import jax
import jax.numpy as jnp
from jax import lax

NR = 128
SECTORS = 16
BANDS = 4
NTAB = 64
NA = 64
NX = 64
NSEG = 64
NMIC = 512


def draw_mean_flow(key, part):
    grid_shape = (NA, NX, NR)
    axial_flow = jax.random.uniform(jax.random.fold_in(key, 31), grid_shape, jnp.float32, 0.2, 0.6)
    swirl_flow = jax.random.uniform(jax.random.fold_in(key, 32), grid_shape, jnp.float32, -0.4, 0.4)
    density = jnp.exp(jax.random.uniform(jax.random.fold_in(key, 33), grid_shape, jnp.float32, math.log(0.5), math.log(2.0)))
    sound_speed = jax.random.uniform(jax.random.fold_in(key, 34), grid_shape, jnp.float32, 0.7, 1.4)
    return jnp.stack([axial_flow, swirl_flow, density, sound_speed])


def draw_segment_id(key, part):
    shift_az = jax.random.randint(jax.random.fold_in(key, 21), (), 0, NA)
    shift_ax = jax.random.randint(jax.random.fold_in(key, 22), (), 0, NX // BANDS)
    az_index = lax.broadcasted_iota(jnp.int32, (NA, NX), 0)
    ax_index = lax.broadcasted_iota(jnp.int32, (NA, NX), 1)
    sector = (az_index + shift_az) % NA * SECTORS // NA
    band = jnp.minimum((ax_index + shift_ax) * BANDS // NX, BANDS - 1)
    return (sector * BANDS + band).astype(jnp.int32)


def mic_spots(key):
    return jax.random.randint(jax.random.fold_in(key, 11), (NMIC,), 0, NA)


def draw_mic_az(key, part):
    return mic_spots(key).astype(jnp.int32)


def draw_measured(key, part):
    spots = mic_spots(key).astype(jnp.float32)
    rising = 1.0 + 2.0 * spots / NA
    level = jnp.clip(jax.random.normal(jax.random.fold_in(key, 12), (NMIC,), jnp.float32), -4.0, 4.0)
    return level * rising


def set_ends(array, stream_key, smallest, top_value):
    dims = array.shape
    place = [jax.random.randint(jax.random.fold_in(stream_key, axis), (), 0, dims[axis]) for axis in range(len(dims))]
    array = array.at[tuple(place)].set(smallest)
    longest = dims.index(max(dims))
    place[longest] = (place[longest] + 1) % dims[longest]
    return array.at[tuple(place)].set(top_value)


def block_levels(stream_key, shape, cuts, low, top_value):
    def one(dim, shards_of):
        steps = jax.random.uniform(jax.random.fold_in(jax.random.fold_in(stream_key, 6), dim), (shards_of,), jnp.float32, low / len(cuts), top_value / len(cuts))
        return jnp.repeat(jnp.exp(steps), shape[dim] // shards_of).reshape((-1,) + (1,) * (len(shape) - dim - 1))

    loudness = one(*cuts[0])
    for cut in cuts[1:]:
        loudness = loudness * one(*cut)
    return loudness


def bell_draw(own_key, shape, deviation, reach, split=(), kind=jnp.bfloat16):
    entries = deviation * jax.random.normal(own_key, shape, jnp.float32)
    if split:
        entries = entries * block_levels(own_key, shape, split, -0.22, 0.18)
    return jnp.clip(entries, -reach, reach).astype(kind)


def setup_inputs(seed: int = 0) -> dict:
    key_list = jax.random.split(jax.random.key(seed), 11)
    return {
        "acoustic": bell_draw(key_list[0], (4, NA, NX, NR), 1.0, 6.0, ((1, 8), (2, 4)), jnp.float32),
        "mean_flow": draw_mean_flow(jax.random.fold_in(key_list[10], 71), 0),
        "adjoint_in": bell_draw(key_list[2], (4, NA, NX, NR), 1.0, 6.0, ((1, 8), (2, 4)), jnp.float32),
        "admittance": jnp.clip(jnp.exp(jax.random.uniform(key_list[3], (NSEG,), jnp.float32, math.log(0.2), math.log(2.0))), 0.2, 2.0),
        "segment_id": draw_segment_id(jax.random.fold_in(key_list[10], 71), 0),
        "noise_code": set_ends(jax.random.randint(key_list[5], (NA, NX), 0, NTAB), jax.random.fold_in(key_list[5], 1), 0, NTAB - 1).astype(jnp.int32),
        "noise_table": bell_draw(key_list[6], (NTAB,), 1.0, 4.0, (), jnp.float32),
        "mic_az": draw_mic_az(jax.random.fold_in(key_list[10], 71), 0),
        "mic_ax": set_ends(jax.random.randint(key_list[8], (NMIC,), 0, NX), jax.random.fold_in(key_list[8], 1), 0, NX - 1).astype(jnp.int32),
        "measured": draw_measured(jax.random.fold_in(key_list[10], 71), 0),
    }


step_dt = 0.25
epsilon = 1e-06

def cycle_shift(values, offset):
    return jnp.roll(values, -offset, axis=-3)

def axial_shift(values, offset):
    blank_edge = jnp.zeros_like(values[..., :1, :])
    if offset > 0:
        return jnp.concatenate([values[..., 1:, :], blank_edge], axis=-2)
    return jnp.concatenate([blank_edge, values[..., :-1, :]], axis=-2)

def radial_shift(values, offset):
    blank_edge = jnp.zeros_like(values[..., :1])
    if offset > 0:
        return jnp.concatenate([values[..., 1:], blank_edge], axis=-1)
    return jnp.concatenate([blank_edge, values[..., :-1]], axis=-1)

def step_forward(acoustic, admittance, mean_flow, segment_id, source):
    pressure, vel_az, vel_ax, vel_rad = (acoustic[0], acoustic[1], acoustic[2], acoustic[3])
    axial_flow, swirl_flow = (mean_flow[0], mean_flow[1])
    buoyancy = 1.0 / mean_flow[2]
    stiffness = mean_flow[2] * mean_flow[3] * mean_flow[3]

    def advect(values):
        return axial_flow * (axial_shift(values, 1) - axial_shift(values, -1)) * 0.5 + swirl_flow * (cycle_shift(values, 1) - cycle_shift(values, -1)) * 0.5
    casing = lax.broadcasted_iota(jnp.int32, pressure.shape, 2) == NR - 1
    wall_admit = admittance[segment_id][:, :, None]
    new_az = vel_az - step_dt * (advect(vel_az) + buoyancy * (cycle_shift(pressure, 1) - pressure))
    new_ax = vel_ax - step_dt * (advect(vel_ax) + buoyancy * (axial_shift(pressure, 1) - pressure))
    new_rad = jnp.where(casing, wall_admit * pressure, vel_rad - step_dt * (advect(vel_rad) + buoyancy * (radial_shift(pressure, 1) - pressure)))
    spread = new_az - cycle_shift(new_az, -1) + (new_ax - axial_shift(new_ax, -1)) + (new_rad - radial_shift(new_rad, -1))
    new_press = pressure - step_dt * (advect(pressure) + stiffness * spread) + step_dt * source
    return jnp.stack([new_press, new_az, new_ax, new_rad])

def reference(acoustic, mean_flow, adjoint_in, admittance, segment_id, noise_code, noise_table, mic_az, mic_ax, measured):
    profile = (jnp.arange(NR, dtype=jnp.float32) + 0.5) / NR
    source = noise_table[noise_code][:, :, None] * profile

    def advance(state_now, admit_now):
        return step_forward(state_now, admit_now, mean_flow, segment_id, source)
    stepped, pullback = jax.vjp(advance, acoustic, admittance)
    misses = stepped[0][mic_az, mic_ax, NR - 1] - measured
    mean_sq = jnp.sum(misses * misses) / NMIC + epsilon
    placed = jnp.zeros((NA, NX), jnp.float32).at[mic_az, mic_ax].add(misses / mean_sq)
    casing = lax.broadcasted_iota(jnp.int32, (NA, NX, NR), 2) == NR - 1
    seed_press = adjoint_in[0] + jnp.where(casing, placed[:, :, None], 0.0)
    cotangent = jnp.concatenate([seed_press[None], adjoint_in[1:]], axis=0)
    adjoint_out, wall_grad = pullback(cotangent)
    liner_grad = wall_grad * (NA * NX / NSEG) ** (-0.5)
    misfit = 0.5 * jnp.log(mean_sq)
    return (adjoint_out, liner_grad, misfit)
```

```python
import jax
import jax.numpy as jnp
from jax import lax
from jax.sharding import PartitionSpec as P

step_dt = 0.25
epsilon = 1e-06


def with_halo(array, axis, dim, before, after, wrap):
    size, length = (lax.axis_size(axis), array.shape[dim])
    up = [(i, (i + 1) % size) for i in range(size if wrap else size - 1)]
    down = [(j, i) for i, j in up]
    parts = []
    if before:
        parts.append(lax.ppermute(lax.slice_in_dim(array, length - before, length, axis=dim), axis, up))
    parts.append(array)
    if after:
        parts.append(lax.ppermute(lax.slice_in_dim(array, 0, after, axis=dim), axis, down))
    return jnp.concatenate(parts, axis=dim)


def exchange(array, before, after):
    widened = with_halo(array, "ax", 2, before, after, False)
    return with_halo(widened, "az", 1, before, after, True)


def win(values, origin, da, dx, na, nx):
    a0, x0 = origin[0] + da, origin[1] + dx
    return values[a0 : a0 + na, x0 : x0 + nx]


def rad_next(values):
    return jnp.concatenate([values[..., 1:], jnp.zeros_like(values[..., :1])], axis=-1)


def rad_prev(values):
    return jnp.concatenate([jnp.zeros_like(values[..., :1]), values[..., :-1]], axis=-1)


def casing_mask(shape):
    return lax.broadcasted_iota(jnp.int32, shape, len(shape) - 1) == shape[-1] - 1


def advect_back(carried_ax, carried_az, na, nx):
    return 0.5 * (carried_ax[..., 1 : 1 + na, 0:nx] - carried_ax[..., 1 : 1 + na, 2 : 2 + nx]) + 0.5 * (
        carried_az[..., 0:na, 1 : 1 + nx] - carried_az[..., 2 : 2 + na, 1 : 1 + nx]
    )


def advect_back4(carried_ax, carried_az, na, nx):
    return 0.5 * (carried_ax[:, 1 : 1 + na, 0:nx, :] - carried_ax[:, 1 : 1 + na, 2 : 2 + nx, :]) + 0.5 * (
        carried_az[:, 0:na, 1 : 1 + nx, :] - carried_az[:, 2 : 2 + na, 1 : 1 + nx, :]
    )


def butterfly_sum(values, axes):
    for axis in axes:
        size = lax.axis_size(axis)
        if size & (size - 1):
            values = lax.psum(values, axis)
            continue
        step = 1
        while step < size:
            values = values + lax.ppermute(values, axis, [(i, i ^ step) for i in range(size)])
            step *= 2
    return values


def shards(
    acoustic,
    mean_flow,
    adjoint_in,
    admittance,
    segment_id,
    noise_code,
    noise_table,
    mic_az,
    mic_ax,
    measured,
):
    na, nx, nr = (acoustic.shape[1], acoustic.shape[2], acoustic.shape[3])
    nseg = admittance.shape[0]
    buoyancy = 1.0 / mean_flow[2]
    stiffness = mean_flow[2] * mean_flow[3] * mean_flow[3]
    axial_flow, swirl_flow = (mean_flow[0], mean_flow[1])

    segment_hot = segment_id[:, :, None] == lax.broadcasted_iota(jnp.int32, (1, 1, nseg), 2)
    wall = jnp.sum(jnp.where(segment_hot, admittance, 0.0), axis=2)
    noise_hot = noise_code[:, :, None] == lax.broadcasted_iota(jnp.int32, (1, 1, noise_table.shape[0]), 2)
    top_profile = (nr - 1 + 0.5) / nr
    source_top = jnp.sum(jnp.where(noise_hot, noise_table, 0.0), axis=2) * top_profile

    a0 = adjoint_in[0]
    push = -step_dt * stiffness * a0
    stack_f = jnp.stack([a0, adjoint_in[1], adjoint_in[2], adjoint_in[3], axial_flow, swirl_flow, buoyancy, push])
    top, below = nr - 1, nr - 2
    planes = [
        acoustic[0, :, :, top],
        acoustic[0, :, :, below],
        acoustic[1, :, :, top],
        acoustic[2, :, :, top],
        acoustic[3, :, :, below],
        axial_flow[:, :, top],
        axial_flow[:, :, below],
        swirl_flow[:, :, top],
        swirl_flow[:, :, below],
        buoyancy[:, :, top],
        buoyancy[:, :, below],
        stiffness[:, :, top],
        wall,
        source_top,
    ]
    stack_c = jnp.stack(planes)

    wide_f = exchange(stack_f, 1, 2)
    wide_c = exchange(stack_c, 3, 3)

    oc = (3, 3)
    p_t, p_b, va_t, vx_t, vr_b, u_t, u_b, w_t, w_b, b_t, b_b, s_t, wall_c, src_c = [wide_c[i] for i in range(14)]
    ea, ex = na + 3, nx + 3

    def c(f, da, dx, la, lx):
        return win(f, oc, da, dx, la, lx)

    def advect_c(f, u, w, da, dx, la, lx):
        return c(u, da, dx, la, lx) * (c(f, da, dx + 1, la, lx) - c(f, da, dx - 1, la, lx)) * 0.5 + c(
            w, da, dx, la, lx
        ) * (c(f, da + 1, dx, la, lx) - c(f, da - 1, dx, la, lx)) * 0.5

    new_az = c(va_t, -2, -1, ea + 1, ex) - step_dt * (
        advect_c(va_t, u_t, w_t, -2, -1, ea + 1, ex)
        + c(b_t, -2, -1, ea + 1, ex) * (c(p_t, -1, -1, ea + 1, ex) - c(p_t, -2, -1, ea + 1, ex))
    )
    new_ax = c(vx_t, -1, -2, ea, ex + 1) - step_dt * (
        advect_c(vx_t, u_t, w_t, -1, -2, ea, ex + 1)
        + c(b_t, -1, -2, ea, ex + 1) * (c(p_t, -1, -1, ea, ex + 1) - c(p_t, -1, -2, ea, ex + 1))
    )
    rad_top = c(wall_c, -1, -1, ea, ex) * c(p_t, -1, -1, ea, ex)
    rad_below = c(vr_b, -1, -1, ea, ex) - step_dt * (
        advect_c(vr_b, u_b, w_b, -1, -1, ea, ex)
        + c(b_b, -1, -1, ea, ex) * (c(p_t, -1, -1, ea, ex) - c(p_b, -1, -1, ea, ex))
    )
    spread = (new_az[1:] - new_az[:-1]) + (new_ax[:, 1:] - new_ax[:, :-1]) + (rad_top - rad_below)
    press_ring = (
        c(p_t, -1, -1, ea, ex)
        - step_dt * (advect_c(p_t, u_t, w_t, -1, -1, ea, ex) + c(s_t, -1, -1, ea, ex) * spread)
        + step_dt * c(src_c, -1, -1, ea, ex)
    )

    total_az = na * lax.axis_size("az")
    first_az = lax.axis_index("az") * na
    first_ax = lax.axis_index("ax") * nx
    ring_az = jnp.remainder(mic_az - first_az + 1, total_az)
    ring_ax = mic_ax - first_ax + 1
    on_ring = (ring_az < ea) & (ring_ax >= 0) & (ring_ax < ex)
    owned = (ring_az >= 1) & (ring_az <= na) & (ring_ax >= 1) & (ring_ax <= nx)
    ring_cell = jnp.where(on_ring, ring_az * ex + ring_ax, -1)
    cell_hot = ring_cell[:, None] == lax.broadcasted_iota(jnp.int32, (1, ea * ex), 1)
    heard = jnp.sum(jnp.where(cell_hot, press_ring.reshape(1, ea * ex), 0.0), axis=1)
    misses = heard - measured
    square_sum = jnp.sum(jnp.where(owned, misses * misses, 0.0))
    placed = jnp.sum(jnp.where(cell_hot, misses[:, None], 0.0), axis=0).reshape(ea, ex)

    push_e = -step_dt * c(s_t, -1, -1, ea, ex) * placed
    r1a, r1x = na + 2, nx + 2
    head_az_e = push_e[:r1a, :r1x] - push_e[1 : 1 + r1a, :r1x]
    head_ax_e = push_e[:r1a, :r1x] - push_e[:r1a, 1 : 1 + r1x]
    head_rad_e = -push_e[:r1a, :r1x]
    u_t1, w_t1 = c(u_t, -1, -1, r1a, r1x), c(w_t, -1, -1, r1a, r1x)
    u_b1, w_b1 = c(u_b, -1, -1, r1a, r1x), c(w_b, -1, -1, r1a, r1x)
    b_t1 = c(b_t, -1, -1, r1a, r1x)
    own_e = (slice(1, 1 + na), slice(1, 1 + nx))
    back_press_t = (
        placed[1 : 1 + na, 1 : 1 + nx]
        - step_dt * advect_back(u_t1 * placed[:r1a, :r1x], w_t1 * placed[:r1a, :r1x], na, nx)
    )
    shove_az = step_dt * b_t1 * head_az_e
    shove_ax = step_dt * b_t1 * head_ax_e
    b_b0, wall_0, push_0 = c(b_b, 0, 0, na, nx), c(wall_c, 0, 0, na, nx), push_e[own_e]
    back_press_t = (
        back_press_t
        + (shove_az[own_e] - shove_az[0:na, 1 : 1 + nx])
        + (shove_ax[own_e] - shove_ax[1 : 1 + na, 0:nx])
        + step_dt * b_b0 * push_0
        + wall_0 * push_0
    )
    back_press_b = -step_dt * b_b0 * push_0
    back_az_t = head_az_e[own_e] - step_dt * advect_back(u_t1 * head_az_e, w_t1 * head_az_e, na, nx)
    back_ax_t = head_ax_e[own_e] - step_dt * advect_back(u_t1 * head_ax_e, w_t1 * head_ax_e, na, nx)
    back_rad_b = head_rad_e[own_e] - step_dt * advect_back(u_b1 * head_rad_e, w_b1 * head_rad_e, na, nx)
    zero = jnp.zeros_like(back_press_b)
    extra = jnp.stack(
        [
            jnp.stack([back_press_b, back_press_t], axis=-1),
            jnp.stack([zero, back_az_t], axis=-1),
            jnp.stack([zero, back_ax_t], axis=-1),
            jnp.stack([back_rad_b, zero], axis=-1),
        ]
    )

    of = (1, 1)
    g_a0, g_a1, g_a2, g_a3, g_u, g_w, g_b, g_push = [wide_f[i] for i in range(8)]
    head_az = win(g_a1, of, -1, -1, r1a, r1x) + win(g_push, of, -1, -1, r1a, r1x) - win(g_push, of, 0, -1, r1a, r1x)
    head_ax = win(g_a2, of, -1, -1, r1a, r1x) + win(g_push, of, -1, -1, r1a, r1x) - win(g_push, of, -1, 0, r1a, r1x)
    push_1 = win(g_push, of, -1, -1, r1a, r1x)
    head_rad = win(g_a3, of, -1, -1, r1a, r1x) + push_1 - rad_next(push_1)
    casing = casing_mask(head_rad.shape)
    head_masked = jnp.where(casing, 0.0, head_rad)
    heads = jnp.stack([head_az, head_ax, head_masked])
    u1, w1, b1 = win(g_u, of, -1, -1, r1a, r1x), win(g_w, of, -1, -1, r1a, r1x), win(g_b, of, -1, -1, r1a, r1x)
    backs = heads[:, 1 : 1 + na, 1 : 1 + nx, :] - step_dt * advect_back4(u1 * heads, w1 * heads, na, nx)
    seed_1 = win(g_a0, of, -1, -1, r1a, r1x)
    back_press = (
        seed_1[1 : 1 + na, 1 : 1 + nx]
        - step_dt * advect_back4((u1 * seed_1)[None], (w1 * seed_1)[None], na, nx)[0]
    )
    shoves = step_dt * b1 * heads
    own = (slice(1, 1 + na), slice(1, 1 + nx))
    shove_r = shoves[2][own]
    back_press = (
        back_press
        + (shoves[0][own] - shoves[0][0:na, 1 : 1 + nx])
        + (shoves[1][own] - shoves[1][1 : 1 + na, 0:nx])
        + (shove_r - rad_prev(shove_r))
    )
    head_rad_own = head_rad[own]
    back_press = back_press + jnp.where(casing_mask(head_rad_own.shape), wall[:, :, None] * head_rad_own, 0.0)
    base = jnp.concatenate([back_press[None], backs], axis=0)

    press_top = acoustic[0, :, :, top]
    sens_base = press_top * head_rad_own[:, :, top]
    sens_placed = press_top * push_0
    seg_base = jnp.sum(jnp.where(segment_hot, sens_base[:, :, None], 0.0), axis=(0, 1))
    seg_placed = jnp.sum(jnp.where(segment_hot, sens_placed[:, :, None], 0.0), axis=(0, 1))

    totals = butterfly_sum(jnp.concatenate([square_sum[None], seg_base, seg_placed]), ("ax", "az"))
    mean_sq = totals[0] / mic_az.shape[0] + epsilon
    grad_scale = (na * lax.axis_size("az") * nx * lax.axis_size("ax") / nseg) ** (-0.5)
    liner_grad = (totals[1 : 1 + nseg] + totals[1 + nseg :] / mean_sq) * grad_scale
    misfit = 0.5 * jnp.log(mean_sq)
    adjoint_out = jnp.concatenate([base[..., : nr - 2], base[..., nr - 2 :] + extra / mean_sq], axis=-1)
    return (adjoint_out, liner_grad, misfit)


def solution(mesh):
    placed = (
        P(None, "az", "ax", None),
        P(None, "az", "ax", None),
        P(None, "az", "ax", None),
        P(),
        P("az", "ax"),
        P("az", "ax"),
        P(),
        P(),
        P(),
        P(),
    )
    return jax.shard_map(
        shards,
        mesh=mesh,
        in_specs=placed,
        out_specs=(P(None, "az", "ax", None), P(), P()),
        check_vma=False,
    )
```

```python
import jax
import jax.numpy as jnp
from jax import lax
from jax.sharding import PartitionSpec as P

step_dt = 0.25
epsilon = 1e-06


def with_halo(array, axis, dim, before, after, wrap):
    size, length = (lax.axis_size(axis), array.shape[dim])
    up = [(i, (i + 1) % size) for i in range(size if wrap else size - 1)]
    down = [(j, i) for i, j in up]
    parts = []
    if before:
        parts.append(lax.ppermute(lax.slice_in_dim(array, length - before, length, axis=dim), axis, up))
    parts.append(array)
    if after:
        parts.append(lax.ppermute(lax.slice_in_dim(array, 0, after, axis=dim), axis, down))
    return jnp.concatenate(parts, axis=dim)


def exchange(array, before, after, ax_before=None, ax_after=None):
    ax_before = before if ax_before is None else ax_before
    ax_after = after if ax_after is None else ax_after
    widened = with_halo(array, "ax", 2, ax_before, ax_after, False)
    return with_halo(widened, "az", 1, before, after, True)


def win(values, origin, da, dx, na, nx):
    a0, x0 = origin[0] + da, origin[1] + dx
    return values[a0 : a0 + na, x0 : x0 + nx]


def rad_next(values):
    return jnp.concatenate([values[..., 1:], jnp.zeros_like(values[..., :1])], axis=-1)


def rad_prev(values):
    return jnp.concatenate([jnp.zeros_like(values[..., :1]), values[..., :-1]], axis=-1)


def casing_mask(shape):
    return lax.broadcasted_iota(jnp.int32, shape, len(shape) - 1) == shape[-1] - 1


def advect_back(carried_ax, carried_az, na, nx):
    return 0.5 * (carried_ax[..., 1 : 1 + na, 0:nx] - carried_ax[..., 1 : 1 + na, 2 : 2 + nx]) + 0.5 * (
        carried_az[..., 0:na, 1 : 1 + nx] - carried_az[..., 2 : 2 + na, 1 : 1 + nx]
    )


def advect_back4(carried_ax, carried_az, na, nx):
    return 0.5 * (carried_ax[:, 1 : 1 + na, 0:nx, :] - carried_ax[:, 1 : 1 + na, 2 : 2 + nx, :]) + 0.5 * (
        carried_az[:, 0:na, 1 : 1 + nx, :] - carried_az[:, 2 : 2 + na, 1 : 1 + nx, :]
    )


def butterfly_sum(values, axes):
    for axis in axes:
        size = lax.axis_size(axis)
        if size & (size - 1):
            values = lax.psum(values, axis)
            continue
        step = 1
        while step < size:
            values = values + lax.ppermute(values, axis, [(i, i ^ step) for i in range(size)])
            step *= 2
    return values


def shards(
    acoustic,
    mean_flow,
    adjoint_in,
    admittance,
    segment_id,
    noise_code,
    noise_table,
    mic_az,
    mic_ax,
    measured,
):
    na, nx, nr = (acoustic.shape[1], acoustic.shape[2], acoustic.shape[3])
    nseg = admittance.shape[0]
    buoyancy = 1.0 / mean_flow[2]
    stiffness = mean_flow[2] * mean_flow[3] * mean_flow[3]
    axial_flow, swirl_flow = (mean_flow[0], mean_flow[1])

    segment_hot = segment_id[:, :, None] == lax.broadcasted_iota(jnp.int32, (1, 1, nseg), 2)
    wall = jnp.sum(jnp.where(segment_hot, admittance, 0.0), axis=2)
    noise_hot = noise_code[:, :, None] == lax.broadcasted_iota(jnp.int32, (1, 1, noise_table.shape[0]), 2)
    top_profile = (nr - 1 + 0.5) / nr
    source_top = jnp.sum(jnp.where(noise_hot, noise_table, 0.0), axis=2) * top_profile

    a0 = adjoint_in[0]
    push = -step_dt * stiffness * a0
    stack_f = jnp.stack([a0, adjoint_in[1], adjoint_in[2], adjoint_in[3], axial_flow, swirl_flow, buoyancy, push])
    top, below = nr - 1, nr - 2
    planes = [
        acoustic[0, :, :, top],
        acoustic[0, :, :, below],
        acoustic[1, :, :, top],
        acoustic[2, :, :, top],
        acoustic[3, :, :, below],
        axial_flow[:, :, top],
        axial_flow[:, :, below],
        swirl_flow[:, :, top],
        swirl_flow[:, :, below],
        buoyancy[:, :, top],
        buoyancy[:, :, below],
        stiffness[:, :, top],
        wall,
        source_top,
    ]
    stack_c = jnp.stack(planes)

    tile = 8
    wide_f = exchange(stack_f, 1, 2, tile, tile)
    wide_c = exchange(stack_c, 3, 3)

    oc = (3, 3)
    p_t, p_b, va_t, vx_t, vr_b, u_t, u_b, w_t, w_b, b_t, b_b, s_t, wall_c, src_c = [wide_c[i] for i in range(14)]
    ea, ex = na + 3, nx + 3

    def c(f, da, dx, la, lx):
        return win(f, oc, da, dx, la, lx)

    def advect_c(f, u, w, da, dx, la, lx):
        return c(u, da, dx, la, lx) * (c(f, da, dx + 1, la, lx) - c(f, da, dx - 1, la, lx)) * 0.5 + c(
            w, da, dx, la, lx
        ) * (c(f, da + 1, dx, la, lx) - c(f, da - 1, dx, la, lx)) * 0.5

    new_az = c(va_t, -2, -1, ea + 1, ex) - step_dt * (
        advect_c(va_t, u_t, w_t, -2, -1, ea + 1, ex)
        + c(b_t, -2, -1, ea + 1, ex) * (c(p_t, -1, -1, ea + 1, ex) - c(p_t, -2, -1, ea + 1, ex))
    )
    new_ax = c(vx_t, -1, -2, ea, ex + 1) - step_dt * (
        advect_c(vx_t, u_t, w_t, -1, -2, ea, ex + 1)
        + c(b_t, -1, -2, ea, ex + 1) * (c(p_t, -1, -1, ea, ex + 1) - c(p_t, -1, -2, ea, ex + 1))
    )
    rad_top = c(wall_c, -1, -1, ea, ex) * c(p_t, -1, -1, ea, ex)
    rad_below = c(vr_b, -1, -1, ea, ex) - step_dt * (
        advect_c(vr_b, u_b, w_b, -1, -1, ea, ex)
        + c(b_b, -1, -1, ea, ex) * (c(p_t, -1, -1, ea, ex) - c(p_b, -1, -1, ea, ex))
    )
    spread = (new_az[1:] - new_az[:-1]) + (new_ax[:, 1:] - new_ax[:, :-1]) + (rad_top - rad_below)
    press_ring = (
        c(p_t, -1, -1, ea, ex)
        - step_dt * (advect_c(p_t, u_t, w_t, -1, -1, ea, ex) + c(s_t, -1, -1, ea, ex) * spread)
        + step_dt * c(src_c, -1, -1, ea, ex)
    )

    total_az = na * lax.axis_size("az")
    first_az = lax.axis_index("az") * na
    first_ax = lax.axis_index("ax") * nx
    ring_az = jnp.remainder(mic_az - first_az + 1, total_az)
    ring_ax = mic_ax - first_ax + 1
    on_ring = (ring_az < ea) & (ring_ax >= 0) & (ring_ax < ex)
    owned = (ring_az >= 1) & (ring_az <= na) & (ring_ax >= 1) & (ring_ax <= nx)
    ring_cell = jnp.where(on_ring, ring_az * ex + ring_ax, -1)
    cell_hot = ring_cell[:, None] == lax.broadcasted_iota(jnp.int32, (1, ea * ex), 1)
    heard = jnp.sum(jnp.where(cell_hot, press_ring.reshape(1, ea * ex), 0.0), axis=1)
    misses = heard - measured
    square_sum = jnp.sum(jnp.where(owned, misses * misses, 0.0))
    placed = jnp.sum(jnp.where(cell_hot, misses[:, None], 0.0), axis=0).reshape(ea, ex)

    push_e = -step_dt * c(s_t, -1, -1, ea, ex) * placed
    r1a, r1x = na + 2, nx + 2
    head_az_e = push_e[:r1a, :r1x] - push_e[1 : 1 + r1a, :r1x]
    head_ax_e = push_e[:r1a, :r1x] - push_e[:r1a, 1 : 1 + r1x]
    head_rad_e = -push_e[:r1a, :r1x]
    u_t1, w_t1 = c(u_t, -1, -1, r1a, r1x), c(w_t, -1, -1, r1a, r1x)
    u_b1, w_b1 = c(u_b, -1, -1, r1a, r1x), c(w_b, -1, -1, r1a, r1x)
    b_t1 = c(b_t, -1, -1, r1a, r1x)
    own_e = (slice(1, 1 + na), slice(1, 1 + nx))
    back_press_t = (
        placed[1 : 1 + na, 1 : 1 + nx]
        - step_dt * advect_back(u_t1 * placed[:r1a, :r1x], w_t1 * placed[:r1a, :r1x], na, nx)
    )
    shove_az = step_dt * b_t1 * head_az_e
    shove_ax = step_dt * b_t1 * head_ax_e
    b_b0, wall_0, push_0 = c(b_b, 0, 0, na, nx), c(wall_c, 0, 0, na, nx), push_e[own_e]
    back_press_t = (
        back_press_t
        + (shove_az[own_e] - shove_az[0:na, 1 : 1 + nx])
        + (shove_ax[own_e] - shove_ax[1 : 1 + na, 0:nx])
        + step_dt * b_b0 * push_0
        + wall_0 * push_0
    )
    back_press_b = -step_dt * b_b0 * push_0
    back_az_t = head_az_e[own_e] - step_dt * advect_back(u_t1 * head_az_e, w_t1 * head_az_e, na, nx)
    back_ax_t = head_ax_e[own_e] - step_dt * advect_back(u_t1 * head_ax_e, w_t1 * head_ax_e, na, nx)
    back_rad_b = head_rad_e[own_e] - step_dt * advect_back(u_b1 * head_rad_e, w_b1 * head_rad_e, na, nx)
    zero = jnp.zeros_like(back_press_b)
    extra = jnp.stack(
        [
            jnp.stack([back_press_b, back_press_t], axis=-1),
            jnp.stack([zero, back_az_t], axis=-1),
            jnp.stack([zero, back_ax_t], axis=-1),
            jnp.stack([back_rad_b, zero], axis=-1),
        ]
    )

    of = (1, tile)
    g_a0, g_a1, g_a2, g_a3, g_u, g_w, g_b, g_push = [wide_f[i] for i in range(8)]
    head_az = win(g_a1, of, -1, -1, r1a, r1x) + win(g_push, of, -1, -1, r1a, r1x) - win(g_push, of, 0, -1, r1a, r1x)
    head_ax = win(g_a2, of, -1, -1, r1a, r1x) + win(g_push, of, -1, -1, r1a, r1x) - win(g_push, of, -1, 0, r1a, r1x)
    push_1 = win(g_push, of, -1, -1, r1a, r1x)
    head_rad = win(g_a3, of, -1, -1, r1a, r1x) + push_1 - rad_next(push_1)
    casing = casing_mask(head_rad.shape)
    head_masked = jnp.where(casing, 0.0, head_rad)
    heads = jnp.stack([head_az, head_ax, head_masked])
    u1, w1, b1 = win(g_u, of, -1, -1, r1a, r1x), win(g_w, of, -1, -1, r1a, r1x), win(g_b, of, -1, -1, r1a, r1x)
    backs = heads[:, 1 : 1 + na, 1 : 1 + nx, :] - step_dt * advect_back4(u1 * heads, w1 * heads, na, nx)
    seed_1 = win(g_a0, of, -1, -1, r1a, r1x)
    back_press = (
        seed_1[1 : 1 + na, 1 : 1 + nx]
        - step_dt * advect_back4((u1 * seed_1)[None], (w1 * seed_1)[None], na, nx)[0]
    )
    shoves = step_dt * b1 * heads
    own = (slice(1, 1 + na), slice(1, 1 + nx))
    shove_r = shoves[2][own]
    back_press = (
        back_press
        + (shoves[0][own] - shoves[0][0:na, 1 : 1 + nx])
        + (shoves[1][own] - shoves[1][1 : 1 + na, 0:nx])
        + (shove_r - rad_prev(shove_r))
    )
    head_rad_own = head_rad[own]
    back_press = back_press + jnp.where(casing_mask(head_rad_own.shape), wall[:, :, None] * head_rad_own, 0.0)
    base = jnp.concatenate([back_press[None], backs], axis=0)

    press_top = acoustic[0, :, :, top]
    sens_base = press_top * head_rad_own[:, :, top]
    sens_placed = press_top * push_0
    seg_base = jnp.sum(jnp.where(segment_hot, sens_base[:, :, None], 0.0), axis=(0, 1))
    seg_placed = jnp.sum(jnp.where(segment_hot, sens_placed[:, :, None], 0.0), axis=(0, 1))

    totals = butterfly_sum(jnp.concatenate([square_sum[None], seg_base, seg_placed]), ("ax", "az"))
    mean_sq = totals[0] / mic_az.shape[0] + epsilon
    grad_scale = (na * lax.axis_size("az") * nx * lax.axis_size("ax") / nseg) ** (-0.5)
    liner_grad = (totals[1 : 1 + nseg] + totals[1 + nseg :] / mean_sq) * grad_scale
    misfit = 0.5 * jnp.log(mean_sq)
    adjoint_out = jnp.concatenate([base[..., : nr - 2], base[..., nr - 2 :] + extra / mean_sq], axis=-1)
    return (adjoint_out, liner_grad, misfit)


def solution(mesh):
    placed = (
        P(None, "az", "ax", None),
        P(None, "az", "ax", None),
        P(None, "az", "ax", None),
        P(),
        P("az", "ax"),
        P("az", "ax"),
        P(),
        P(),
        P(),
        P(),
    )
    return jax.shard_map(
        shards,
        mesh=mesh,
        in_specs=placed,
        out_specs=(P(None, "az", "ax", None), P(), P()),
        check_vma=False,
    )
```

```python
import jax
import jax.numpy as jnp
from jax import lax
from jax.sharding import PartitionSpec as P

step_dt = 0.25
epsilon = 1e-06


def with_halo(array, axis, dim, before, after, wrap):
    size, length = (lax.axis_size(axis), array.shape[dim])
    up = [(i, (i + 1) % size) for i in range(size if wrap else size - 1)]
    down = [(j, i) for i, j in up]
    parts = []
    if before:
        parts.append(lax.ppermute(lax.slice_in_dim(array, length - before, length, axis=dim), axis, up))
    parts.append(array)
    if after:
        parts.append(lax.ppermute(lax.slice_in_dim(array, 0, after, axis=dim), axis, down))
    return jnp.concatenate(parts, axis=dim)


def exchange(array, before, after, ax_before=None, ax_after=None):
    ax_before = before if ax_before is None else ax_before
    ax_after = after if ax_after is None else ax_after
    widened = with_halo(array, "ax", 2, ax_before, ax_after, False)
    return with_halo(widened, "az", 1, before, after, True)


def exchange_once(array, a_lo, a_hi, x_lo, x_hi):
    n_az, n_ax = (lax.axis_size("az"), lax.axis_size("ax"))
    length_a, length_x = (array.shape[1], array.shape[2])

    def pairs(da, dx):
        found = []
        for az in range(n_az):
            for ax in range(n_ax):
                to_ax = ax - dx
                if 0 <= to_ax < n_ax:
                    found.append((az * n_ax + ax, ((az - da) % n_az) * n_ax + to_ax))
        return found

    rows = {-1: (length_a - a_lo, length_a), 0: (0, length_a), 1: (0, a_hi)}
    cols = {-1: (length_x - x_lo, length_x), 0: (0, length_x), 1: (0, x_hi)}
    bands = []
    for da in (-1, 0, 1):
        if (da == -1 and not a_lo) or (da == 1 and not a_hi):
            continue
        pieces = []
        for dx in (-1, 0, 1):
            if (dx == -1 and not x_lo) or (dx == 1 and not x_hi):
                continue
            piece = lax.slice_in_dim(lax.slice_in_dim(array, *rows[da], axis=1), *cols[dx], axis=2)
            if da or dx:
                piece = lax.ppermute(piece, ("az", "ax"), pairs(da, dx))
            pieces.append(piece)
        bands.append(jnp.concatenate(pieces, axis=2))
    return jnp.concatenate(bands, axis=1)


def win(values, origin, da, dx, na, nx):
    a0, x0 = origin[0] + da, origin[1] + dx
    return values[a0 : a0 + na, x0 : x0 + nx]


def rad_next(values):
    return jnp.concatenate([values[..., 1:], jnp.zeros_like(values[..., :1])], axis=-1)


def rad_prev(values):
    return jnp.concatenate([jnp.zeros_like(values[..., :1]), values[..., :-1]], axis=-1)


def casing_mask(shape):
    return lax.broadcasted_iota(jnp.int32, shape, len(shape) - 1) == shape[-1] - 1


def advect_back(carried_ax, carried_az, na, nx):
    return 0.5 * (carried_ax[..., 1 : 1 + na, 0:nx] - carried_ax[..., 1 : 1 + na, 2 : 2 + nx]) + 0.5 * (
        carried_az[..., 0:na, 1 : 1 + nx] - carried_az[..., 2 : 2 + na, 1 : 1 + nx]
    )


def advect_back4(carried_ax, carried_az, na, nx):
    return 0.5 * (carried_ax[:, 1 : 1 + na, 0:nx, :] - carried_ax[:, 1 : 1 + na, 2 : 2 + nx, :]) + 0.5 * (
        carried_az[:, 0:na, 1 : 1 + nx, :] - carried_az[:, 2 : 2 + na, 1 : 1 + nx, :]
    )


def butterfly_sum(values, axes):
    for axis in axes:
        size = lax.axis_size(axis)
        if size & (size - 1):
            values = lax.psum(values, axis)
            continue
        step = 1
        while step < size:
            values = values + lax.ppermute(values, axis, [(i, i ^ step) for i in range(size)])
            step *= 2
    return values


def shards(
    acoustic,
    mean_flow,
    adjoint_in,
    admittance,
    segment_id,
    noise_code,
    noise_table,
    mic_az,
    mic_ax,
    measured,
):
    na, nx, nr = (acoustic.shape[1], acoustic.shape[2], acoustic.shape[3])
    nseg = admittance.shape[0]
    buoyancy = 1.0 / mean_flow[2]
    stiffness = mean_flow[2] * mean_flow[3] * mean_flow[3]
    axial_flow, swirl_flow = (mean_flow[0], mean_flow[1])

    segment_hot = segment_id[:, :, None] == lax.broadcasted_iota(jnp.int32, (1, 1, nseg), 2)
    wall = jnp.sum(jnp.where(segment_hot, admittance, 0.0), axis=2)
    noise_hot = noise_code[:, :, None] == lax.broadcasted_iota(jnp.int32, (1, 1, noise_table.shape[0]), 2)
    top_profile = (nr - 1 + 0.5) / nr
    source_top = jnp.sum(jnp.where(noise_hot, noise_table, 0.0), axis=2) * top_profile

    a0 = adjoint_in[0]
    push = -step_dt * stiffness * a0
    stack_f = jnp.stack([a0, adjoint_in[1], adjoint_in[2], adjoint_in[3], axial_flow, swirl_flow, buoyancy, push])
    top, below = nr - 1, nr - 2
    planes = [
        acoustic[0, :, :, top],
        acoustic[0, :, :, below],
        acoustic[1, :, :, top],
        acoustic[2, :, :, top],
        acoustic[3, :, :, below],
        axial_flow[:, :, top],
        axial_flow[:, :, below],
        swirl_flow[:, :, top],
        swirl_flow[:, :, below],
        buoyancy[:, :, top],
        buoyancy[:, :, below],
        stiffness[:, :, top],
        wall,
        source_top,
    ]
    stack_c = jnp.stack(planes)

    tile = 8
    wide_f = exchange_once(stack_f, 1, 2, tile, tile)
    wide_c = exchange_once(stack_c, 3, 3, 3, 3)

    oc = (3, 3)
    p_t, p_b, va_t, vx_t, vr_b, u_t, u_b, w_t, w_b, b_t, b_b, s_t, wall_c, src_c = [wide_c[i] for i in range(14)]
    ea, ex = na + 3, nx + 3

    def c(f, da, dx, la, lx):
        return win(f, oc, da, dx, la, lx)

    def advect_c(f, u, w, da, dx, la, lx):
        return c(u, da, dx, la, lx) * (c(f, da, dx + 1, la, lx) - c(f, da, dx - 1, la, lx)) * 0.5 + c(
            w, da, dx, la, lx
        ) * (c(f, da + 1, dx, la, lx) - c(f, da - 1, dx, la, lx)) * 0.5

    new_az = c(va_t, -2, -1, ea + 1, ex) - step_dt * (
        advect_c(va_t, u_t, w_t, -2, -1, ea + 1, ex)
        + c(b_t, -2, -1, ea + 1, ex) * (c(p_t, -1, -1, ea + 1, ex) - c(p_t, -2, -1, ea + 1, ex))
    )
    new_ax = c(vx_t, -1, -2, ea, ex + 1) - step_dt * (
        advect_c(vx_t, u_t, w_t, -1, -2, ea, ex + 1)
        + c(b_t, -1, -2, ea, ex + 1) * (c(p_t, -1, -1, ea, ex + 1) - c(p_t, -1, -2, ea, ex + 1))
    )
    rad_top = c(wall_c, -1, -1, ea, ex) * c(p_t, -1, -1, ea, ex)
    rad_below = c(vr_b, -1, -1, ea, ex) - step_dt * (
        advect_c(vr_b, u_b, w_b, -1, -1, ea, ex)
        + c(b_b, -1, -1, ea, ex) * (c(p_t, -1, -1, ea, ex) - c(p_b, -1, -1, ea, ex))
    )
    spread = (new_az[1:] - new_az[:-1]) + (new_ax[:, 1:] - new_ax[:, :-1]) + (rad_top - rad_below)
    press_ring = (
        c(p_t, -1, -1, ea, ex)
        - step_dt * (advect_c(p_t, u_t, w_t, -1, -1, ea, ex) + c(s_t, -1, -1, ea, ex) * spread)
        + step_dt * c(src_c, -1, -1, ea, ex)
    )

    total_az = na * lax.axis_size("az")
    first_az = lax.axis_index("az") * na
    first_ax = lax.axis_index("ax") * nx
    ring_az = jnp.remainder(mic_az - first_az + 1, total_az)
    ring_ax = mic_ax - first_ax + 1
    on_ring = (ring_az < ea) & (ring_ax >= 0) & (ring_ax < ex)
    owned = (ring_az >= 1) & (ring_az <= na) & (ring_ax >= 1) & (ring_ax <= nx)
    ring_cell = jnp.where(on_ring, ring_az * ex + ring_ax, -1)
    cell_hot = ring_cell[:, None] == lax.broadcasted_iota(jnp.int32, (1, ea * ex), 1)
    heard = jnp.sum(jnp.where(cell_hot, press_ring.reshape(1, ea * ex), 0.0), axis=1)
    misses = heard - measured
    square_sum = jnp.sum(jnp.where(owned, misses * misses, 0.0))
    placed = jnp.sum(jnp.where(cell_hot, misses[:, None], 0.0), axis=0).reshape(ea, ex)

    push_e = -step_dt * c(s_t, -1, -1, ea, ex) * placed
    r1a, r1x = na + 2, nx + 2
    head_az_e = push_e[:r1a, :r1x] - push_e[1 : 1 + r1a, :r1x]
    head_ax_e = push_e[:r1a, :r1x] - push_e[:r1a, 1 : 1 + r1x]
    head_rad_e = -push_e[:r1a, :r1x]
    u_t1, w_t1 = c(u_t, -1, -1, r1a, r1x), c(w_t, -1, -1, r1a, r1x)
    u_b1, w_b1 = c(u_b, -1, -1, r1a, r1x), c(w_b, -1, -1, r1a, r1x)
    b_t1 = c(b_t, -1, -1, r1a, r1x)
    own_e = (slice(1, 1 + na), slice(1, 1 + nx))
    back_press_t = (
        placed[1 : 1 + na, 1 : 1 + nx]
        - step_dt * advect_back(u_t1 * placed[:r1a, :r1x], w_t1 * placed[:r1a, :r1x], na, nx)
    )
    shove_az = step_dt * b_t1 * head_az_e
    shove_ax = step_dt * b_t1 * head_ax_e
    b_b0, wall_0, push_0 = c(b_b, 0, 0, na, nx), c(wall_c, 0, 0, na, nx), push_e[own_e]
    back_press_t = (
        back_press_t
        + (shove_az[own_e] - shove_az[0:na, 1 : 1 + nx])
        + (shove_ax[own_e] - shove_ax[1 : 1 + na, 0:nx])
        + step_dt * b_b0 * push_0
        + wall_0 * push_0
    )
    back_press_b = -step_dt * b_b0 * push_0
    back_az_t = head_az_e[own_e] - step_dt * advect_back(u_t1 * head_az_e, w_t1 * head_az_e, na, nx)
    back_ax_t = head_ax_e[own_e] - step_dt * advect_back(u_t1 * head_ax_e, w_t1 * head_ax_e, na, nx)
    back_rad_b = head_rad_e[own_e] - step_dt * advect_back(u_b1 * head_rad_e, w_b1 * head_rad_e, na, nx)
    zero = jnp.zeros_like(back_press_b)
    extra = jnp.stack(
        [
            jnp.stack([back_press_b, back_press_t], axis=-1),
            jnp.stack([zero, back_az_t], axis=-1),
            jnp.stack([zero, back_ax_t], axis=-1),
            jnp.stack([back_rad_b, zero], axis=-1),
        ]
    )

    of = (1, tile)
    g_a0, g_a1, g_a2, g_a3, g_u, g_w, g_b, g_push = [wide_f[i] for i in range(8)]
    head_az = win(g_a1, of, -1, -1, r1a, r1x) + win(g_push, of, -1, -1, r1a, r1x) - win(g_push, of, 0, -1, r1a, r1x)
    head_ax = win(g_a2, of, -1, -1, r1a, r1x) + win(g_push, of, -1, -1, r1a, r1x) - win(g_push, of, -1, 0, r1a, r1x)
    push_1 = win(g_push, of, -1, -1, r1a, r1x)
    head_rad = win(g_a3, of, -1, -1, r1a, r1x) + push_1 - rad_next(push_1)
    casing = casing_mask(head_rad.shape)
    head_masked = jnp.where(casing, 0.0, head_rad)
    heads = jnp.stack([head_az, head_ax, head_masked])
    u1, w1, b1 = win(g_u, of, -1, -1, r1a, r1x), win(g_w, of, -1, -1, r1a, r1x), win(g_b, of, -1, -1, r1a, r1x)
    backs = heads[:, 1 : 1 + na, 1 : 1 + nx, :] - step_dt * advect_back4(u1 * heads, w1 * heads, na, nx)
    seed_1 = win(g_a0, of, -1, -1, r1a, r1x)
    back_press = (
        seed_1[1 : 1 + na, 1 : 1 + nx]
        - step_dt * advect_back4((u1 * seed_1)[None], (w1 * seed_1)[None], na, nx)[0]
    )
    shoves = step_dt * b1 * heads
    own = (slice(1, 1 + na), slice(1, 1 + nx))
    shove_r = shoves[2][own]
    back_press = (
        back_press
        + (shoves[0][own] - shoves[0][0:na, 1 : 1 + nx])
        + (shoves[1][own] - shoves[1][1 : 1 + na, 0:nx])
        + (shove_r - rad_prev(shove_r))
    )
    head_rad_own = head_rad[own]
    back_press = back_press + jnp.where(casing_mask(head_rad_own.shape), wall[:, :, None] * head_rad_own, 0.0)
    base = jnp.concatenate([back_press[None], backs], axis=0)

    press_top = acoustic[0, :, :, top]
    sens_base = press_top * head_rad_own[:, :, top]
    sens_placed = press_top * push_0
    seg_base = jnp.sum(jnp.where(segment_hot, sens_base[:, :, None], 0.0), axis=(0, 1))
    seg_placed = jnp.sum(jnp.where(segment_hot, sens_placed[:, :, None], 0.0), axis=(0, 1))

    totals = butterfly_sum(jnp.concatenate([square_sum[None], seg_base, seg_placed]), ("ax", "az"))
    mean_sq = totals[0] / mic_az.shape[0] + epsilon
    grad_scale = (na * lax.axis_size("az") * nx * lax.axis_size("ax") / nseg) ** (-0.5)
    liner_grad = (totals[1 : 1 + nseg] + totals[1 + nseg :] / mean_sq) * grad_scale
    misfit = 0.5 * jnp.log(mean_sq)
    adjoint_out = jnp.concatenate([base[..., : nr - 2], base[..., nr - 2 :] + extra / mean_sq], axis=-1)
    return (adjoint_out, liner_grad, misfit)


def solution(mesh):
    placed = (
        P(None, "az", "ax", None),
        P(None, "az", "ax", None),
        P(None, "az", "ax", None),
        P(),
        P("az", "ax"),
        P("az", "ax"),
        P(),
        P(),
        P(),
        P(),
    )
    return jax.shard_map(
        shards,
        mesh=mesh,
        in_specs=placed,
        out_specs=(P(None, "az", "ax", None), P(), P()),
        check_vma=False,
    )
```

```python
import jax
import jax.numpy as jnp
from jax import lax
from jax.sharding import PartitionSpec as P

step_dt = 0.25
epsilon = 1e-06


def with_halo(array, axis, dim, before, after, wrap):
    size, length = (lax.axis_size(axis), array.shape[dim])
    up = [(i, (i + 1) % size) for i in range(size if wrap else size - 1)]
    down = [(j, i) for i, j in up]
    parts = []
    if before:
        parts.append(lax.ppermute(lax.slice_in_dim(array, length - before, length, axis=dim), axis, up))
    parts.append(array)
    if after:
        parts.append(lax.ppermute(lax.slice_in_dim(array, 0, after, axis=dim), axis, down))
    return jnp.concatenate(parts, axis=dim)


def exchange(array, before, after, ax_before=None, ax_after=None):
    ax_before = before if ax_before is None else ax_before
    ax_after = after if ax_after is None else ax_after
    widened = with_halo(array, "ax", 2, ax_before, ax_after, False)
    return with_halo(widened, "az", 1, before, after, True)


def win(values, origin, da, dx, na, nx):
    a0, x0 = origin[0] + da, origin[1] + dx
    return values[a0 : a0 + na, x0 : x0 + nx]


def rad_next(values):
    return jnp.concatenate([values[..., 1:], jnp.zeros_like(values[..., :1])], axis=-1)


def rad_prev(values):
    return jnp.concatenate([jnp.zeros_like(values[..., :1]), values[..., :-1]], axis=-1)


def casing_mask(shape):
    return lax.broadcasted_iota(jnp.int32, shape, len(shape) - 1) == shape[-1] - 1


def advect_back(carried_ax, carried_az, na, nx):
    return 0.5 * (carried_ax[..., 1 : 1 + na, 0:nx] - carried_ax[..., 1 : 1 + na, 2 : 2 + nx]) + 0.5 * (
        carried_az[..., 0:na, 1 : 1 + nx] - carried_az[..., 2 : 2 + na, 1 : 1 + nx]
    )


def advect_back4(carried_ax, carried_az, na, nx):
    return 0.5 * (carried_ax[:, 1 : 1 + na, 0:nx, :] - carried_ax[:, 1 : 1 + na, 2 : 2 + nx, :]) + 0.5 * (
        carried_az[:, 0:na, 1 : 1 + nx, :] - carried_az[:, 2 : 2 + na, 1 : 1 + nx, :]
    )


def butterfly_sum(values, axes):
    for axis in axes:
        size = lax.axis_size(axis)
        if size & (size - 1):
            values = lax.psum(values, axis)
            continue
        step = 1
        while step < size:
            values = values + lax.ppermute(values, axis, [(i, i ^ step) for i in range(size)])
            step *= 2
    return values


def shards(
    acoustic,
    mean_flow,
    adjoint_in,
    admittance,
    segment_id,
    noise_code,
    noise_table,
    mic_az,
    mic_ax,
    measured,
):
    na, nx, nr = (acoustic.shape[1], acoustic.shape[2], acoustic.shape[3])
    nseg = admittance.shape[0]
    buoyancy = 1.0 / mean_flow[2]
    stiffness = mean_flow[2] * mean_flow[3] * mean_flow[3]
    axial_flow, swirl_flow = (mean_flow[0], mean_flow[1])

    segment_hot = segment_id[:, :, None] == lax.broadcasted_iota(jnp.int32, (1, 1, nseg), 2)
    wall = jnp.sum(jnp.where(segment_hot, admittance, 0.0), axis=2)
    noise_hot = noise_code[:, :, None] == lax.broadcasted_iota(jnp.int32, (1, 1, noise_table.shape[0]), 2)
    top_profile = (nr - 1 + 0.5) / nr
    source_top = jnp.sum(jnp.where(noise_hot, noise_table, 0.0), axis=2) * top_profile

    a0 = adjoint_in[0]
    push = -step_dt * stiffness * a0
    stack_f = jnp.stack([a0, adjoint_in[1], adjoint_in[2], adjoint_in[3], axial_flow, swirl_flow, buoyancy, push])
    top, below = nr - 1, nr - 2
    planes = [
        acoustic[0, :, :, top],
        acoustic[0, :, :, below],
        acoustic[1, :, :, top],
        acoustic[2, :, :, top],
        acoustic[3, :, :, below],
        axial_flow[:, :, top],
        axial_flow[:, :, below],
        swirl_flow[:, :, top],
        swirl_flow[:, :, below],
        buoyancy[:, :, top],
        buoyancy[:, :, below],
        stiffness[:, :, top],
        wall,
        source_top,
    ]
    stack_c = jnp.stack(planes)

    tile = 8
    wide_f = exchange(stack_f, 1, 2, tile, tile)
    wide_c = exchange(stack_c, 3, 3)

    oc = (3, 3)
    p_t, p_b, va_t, vx_t, vr_b, u_t, u_b, w_t, w_b, b_t, b_b, s_t, wall_c, src_c = [wide_c[i] for i in range(14)]
    ea, ex = na + 3, nx + 3

    def c(f, da, dx, la, lx):
        return win(f, oc, da, dx, la, lx)

    def advect_c(f, u, w, da, dx, la, lx):
        return c(u, da, dx, la, lx) * (c(f, da, dx + 1, la, lx) - c(f, da, dx - 1, la, lx)) * 0.5 + c(
            w, da, dx, la, lx
        ) * (c(f, da + 1, dx, la, lx) - c(f, da - 1, dx, la, lx)) * 0.5

    new_az = c(va_t, -2, -1, ea + 1, ex) - step_dt * (
        advect_c(va_t, u_t, w_t, -2, -1, ea + 1, ex)
        + c(b_t, -2, -1, ea + 1, ex) * (c(p_t, -1, -1, ea + 1, ex) - c(p_t, -2, -1, ea + 1, ex))
    )
    new_ax = c(vx_t, -1, -2, ea, ex + 1) - step_dt * (
        advect_c(vx_t, u_t, w_t, -1, -2, ea, ex + 1)
        + c(b_t, -1, -2, ea, ex + 1) * (c(p_t, -1, -1, ea, ex + 1) - c(p_t, -1, -2, ea, ex + 1))
    )
    rad_top = c(wall_c, -1, -1, ea, ex) * c(p_t, -1, -1, ea, ex)
    rad_below = c(vr_b, -1, -1, ea, ex) - step_dt * (
        advect_c(vr_b, u_b, w_b, -1, -1, ea, ex)
        + c(b_b, -1, -1, ea, ex) * (c(p_t, -1, -1, ea, ex) - c(p_b, -1, -1, ea, ex))
    )
    spread = (new_az[1:] - new_az[:-1]) + (new_ax[:, 1:] - new_ax[:, :-1]) + (rad_top - rad_below)
    press_ring = (
        c(p_t, -1, -1, ea, ex)
        - step_dt * (advect_c(p_t, u_t, w_t, -1, -1, ea, ex) + c(s_t, -1, -1, ea, ex) * spread)
        + step_dt * c(src_c, -1, -1, ea, ex)
    )

    total_az = na * lax.axis_size("az")
    first_az = lax.axis_index("az") * na
    first_ax = lax.axis_index("ax") * nx
    ring_az = jnp.remainder(mic_az - first_az + 1, total_az)
    ring_ax = mic_ax - first_ax + 1
    on_ring = (ring_az < ea) & (ring_ax >= 0) & (ring_ax < ex)
    owned = (ring_az >= 1) & (ring_az <= na) & (ring_ax >= 1) & (ring_ax <= nx)
    ring_cell = jnp.where(on_ring, ring_az * ex + ring_ax, -1)
    cell_hot = ring_cell[:, None] == lax.broadcasted_iota(jnp.int32, (1, ea * ex), 1)
    heard = jnp.sum(jnp.where(cell_hot, press_ring.reshape(1, ea * ex), 0.0), axis=1)
    misses = heard - measured
    square_sum = jnp.sum(jnp.where(owned, misses * misses, 0.0))
    placed = jnp.sum(jnp.where(cell_hot, misses[:, None], 0.0), axis=0).reshape(ea, ex)

    push_e = -step_dt * c(s_t, -1, -1, ea, ex) * placed
    r1a, r1x = na + 2, nx + 2
    head_az_e = push_e[:r1a, :r1x] - push_e[1 : 1 + r1a, :r1x]
    head_ax_e = push_e[:r1a, :r1x] - push_e[:r1a, 1 : 1 + r1x]
    head_rad_e = -push_e[:r1a, :r1x]
    u_t1, w_t1 = c(u_t, -1, -1, r1a, r1x), c(w_t, -1, -1, r1a, r1x)
    u_b1, w_b1 = c(u_b, -1, -1, r1a, r1x), c(w_b, -1, -1, r1a, r1x)
    b_t1 = c(b_t, -1, -1, r1a, r1x)
    own_e = (slice(1, 1 + na), slice(1, 1 + nx))
    back_press_t = (
        placed[1 : 1 + na, 1 : 1 + nx]
        - step_dt * advect_back(u_t1 * placed[:r1a, :r1x], w_t1 * placed[:r1a, :r1x], na, nx)
    )
    shove_az = step_dt * b_t1 * head_az_e
    shove_ax = step_dt * b_t1 * head_ax_e
    b_b0, wall_0, push_0 = c(b_b, 0, 0, na, nx), c(wall_c, 0, 0, na, nx), push_e[own_e]
    back_press_t = (
        back_press_t
        + (shove_az[own_e] - shove_az[0:na, 1 : 1 + nx])
        + (shove_ax[own_e] - shove_ax[1 : 1 + na, 0:nx])
        + step_dt * b_b0 * push_0
        + wall_0 * push_0
    )
    back_press_b = -step_dt * b_b0 * push_0
    back_az_t = head_az_e[own_e] - step_dt * advect_back(u_t1 * head_az_e, w_t1 * head_az_e, na, nx)
    back_ax_t = head_ax_e[own_e] - step_dt * advect_back(u_t1 * head_ax_e, w_t1 * head_ax_e, na, nx)
    back_rad_b = head_rad_e[own_e] - step_dt * advect_back(u_b1 * head_rad_e, w_b1 * head_rad_e, na, nx)
    zero = jnp.zeros_like(back_press_b)
    extra = jnp.stack(
        [
            jnp.stack([back_press_b, back_press_t], axis=-1),
            jnp.stack([zero, back_az_t], axis=-1),
            jnp.stack([zero, back_ax_t], axis=-1),
            jnp.stack([back_rad_b, zero], axis=-1),
        ]
    )

    of = (1, tile)
    g_a0, g_a1, g_a2, g_a3, g_u, g_w, g_b, g_push = [wide_f[i] for i in range(8)]

    def at(field, da, dx):
        return win(field, of, da, dx, na, nx)

    def head_az(da, dx):
        return at(g_a1, da, dx) + at(g_push, da, dx) - at(g_push, da + 1, dx)

    def head_ax(da, dx):
        return at(g_a2, da, dx) + at(g_push, da, dx) - at(g_push, da, dx + 1)

    casing = casing_mask((na, nx, nr))

    def head_rad(da, dx):
        push_here = at(g_push, da, dx)
        return at(g_a3, da, dx) + push_here - rad_next(push_here)

    def head_masked(da, dx):
        return jnp.where(casing, 0.0, head_rad(da, dx))

    def back_advect(head):
        return 0.5 * (at(g_u, 0, -1) * head(0, -1) - at(g_u, 0, 1) * head(0, 1)) + 0.5 * (
            at(g_w, -1, 0) * head(-1, 0) - at(g_w, 1, 0) * head(1, 0)
        )

    def seed(da, dx):
        return at(g_a0, da, dx)

    backs = [head(0, 0) - step_dt * back_advect(head) for head in (head_az, head_ax, head_masked)]
    shove_r = step_dt * at(g_b, 0, 0) * head_masked(0, 0)
    head_rad_own = head_rad(0, 0)
    back_press = (
        seed(0, 0)
        - step_dt * back_advect(seed)
        + (step_dt * at(g_b, 0, 0) * head_az(0, 0) - step_dt * at(g_b, -1, 0) * head_az(-1, 0))
        + (step_dt * at(g_b, 0, 0) * head_ax(0, 0) - step_dt * at(g_b, 0, -1) * head_ax(0, -1))
        + (shove_r - rad_prev(shove_r))
        + jnp.where(casing, wall[:, :, None] * head_rad_own, 0.0)
    )
    base = jnp.stack([back_press] + backs)

    press_top = acoustic[0, :, :, top]
    sens_base = press_top * (adjoint_in[3, :, :, top] + push[:, :, top])
    sens_placed = press_top * push_0
    seg_base = jnp.sum(jnp.where(segment_hot, sens_base[:, :, None], 0.0), axis=(0, 1))
    seg_placed = jnp.sum(jnp.where(segment_hot, sens_placed[:, :, None], 0.0), axis=(0, 1))

    totals = butterfly_sum(jnp.concatenate([square_sum[None], seg_base, seg_placed]), ("ax", "az"))
    mean_sq = totals[0] / mic_az.shape[0] + epsilon
    grad_scale = (na * lax.axis_size("az") * nx * lax.axis_size("ax") / nseg) ** (-0.5)
    liner_grad = (totals[1 : 1 + nseg] + totals[1 + nseg :] / mean_sq) * grad_scale
    misfit = 0.5 * jnp.log(mean_sq)
    adjoint_out = base + jnp.pad(extra / mean_sq, ((0, 0), (0, 0), (0, 0), (nr - 2, 0)))
    return (adjoint_out, liner_grad, misfit)


def solution(mesh):
    placed = (
        P(None, "az", "ax", None),
        P(None, "az", "ax", None),
        P(None, "az", "ax", None),
        P(),
        P("az", "ax"),
        P("az", "ax"),
        P(),
        P(),
        P(),
        P(),
    )
    return jax.shard_map(
        shards,
        mesh=mesh,
        in_specs=placed,
        out_specs=(P(None, "az", "ax", None), P(), P()),
        check_vma=False,
    )
```

```python
import jax
import jax.numpy as jnp
from jax import lax
from jax.sharding import PartitionSpec as P

step_dt = 0.25
epsilon = 1e-06


def with_halo(array, axis, dim, before, after, wrap):
    size, length = (lax.axis_size(axis), array.shape[dim])
    up = [(i, (i + 1) % size) for i in range(size if wrap else size - 1)]
    down = [(j, i) for i, j in up]
    parts = []
    if before:
        parts.append(lax.ppermute(lax.slice_in_dim(array, length - before, length, axis=dim), axis, up))
    parts.append(array)
    if after:
        parts.append(lax.ppermute(lax.slice_in_dim(array, 0, after, axis=dim), axis, down))
    return jnp.concatenate(parts, axis=dim)


def exchange(array, before, after, ax_before=None, ax_after=None):
    ax_before = before if ax_before is None else ax_before
    ax_after = after if ax_after is None else ax_after
    widened = with_halo(array, "ax", 2, ax_before, ax_after, False)
    return with_halo(widened, "az", 1, before, after, True)


def win(values, origin, da, dx, na, nx):
    a0, x0 = origin[0] + da, origin[1] + dx
    return values[a0 : a0 + na, x0 : x0 + nx]


def rad_next(values):
    return jnp.concatenate([values[..., 1:], jnp.zeros_like(values[..., :1])], axis=-1)


def rad_prev(values):
    return jnp.concatenate([jnp.zeros_like(values[..., :1]), values[..., :-1]], axis=-1)


def casing_mask(shape):
    return lax.broadcasted_iota(jnp.int32, shape, len(shape) - 1) == shape[-1] - 1


def advect_back(carried_ax, carried_az, na, nx):
    return 0.5 * (carried_ax[..., 1 : 1 + na, 0:nx] - carried_ax[..., 1 : 1 + na, 2 : 2 + nx]) + 0.5 * (
        carried_az[..., 0:na, 1 : 1 + nx] - carried_az[..., 2 : 2 + na, 1 : 1 + nx]
    )


def advect_back4(carried_ax, carried_az, na, nx):
    return 0.5 * (carried_ax[:, 1 : 1 + na, 0:nx, :] - carried_ax[:, 1 : 1 + na, 2 : 2 + nx, :]) + 0.5 * (
        carried_az[:, 0:na, 1 : 1 + nx, :] - carried_az[:, 2 : 2 + na, 1 : 1 + nx, :]
    )


def butterfly_sum(values, axes):
    for axis in axes:
        size = lax.axis_size(axis)
        if size & (size - 1):
            values = lax.psum(values, axis)
            continue
        step = 1
        while step < size:
            values = values + lax.ppermute(values, axis, [(i, i ^ step) for i in range(size)])
            step *= 2
    return values


def shards(
    acoustic,
    mean_flow,
    adjoint_in,
    admittance,
    segment_id,
    noise_code,
    noise_table,
    mic_az,
    mic_ax,
    measured,
):
    na, nx, nr = (acoustic.shape[1], acoustic.shape[2], acoustic.shape[3])
    nseg = admittance.shape[0]
    buoyancy = 1.0 / mean_flow[2]
    stiffness = mean_flow[2] * mean_flow[3] * mean_flow[3]
    axial_flow, swirl_flow = (mean_flow[0], mean_flow[1])

    segment_hot = segment_id[:, :, None] == lax.broadcasted_iota(jnp.int32, (1, 1, nseg), 2)
    wall = jnp.sum(jnp.where(segment_hot, admittance, 0.0), axis=2)
    noise_hot = noise_code[:, :, None] == lax.broadcasted_iota(jnp.int32, (1, 1, noise_table.shape[0]), 2)
    top_profile = (nr - 1 + 0.5) / nr
    source_top = jnp.sum(jnp.where(noise_hot, noise_table, 0.0), axis=2) * top_profile

    a0 = adjoint_in[0]
    push = -step_dt * stiffness * a0
    stack_f = jnp.stack([a0, adjoint_in[1], adjoint_in[2], adjoint_in[3], axial_flow, swirl_flow, buoyancy, push])
    top, below = nr - 1, nr - 2
    planes = [
        acoustic[0, :, :, top],
        acoustic[0, :, :, below],
        acoustic[1, :, :, top],
        acoustic[2, :, :, top],
        acoustic[3, :, :, below],
        axial_flow[:, :, top],
        axial_flow[:, :, below],
        swirl_flow[:, :, top],
        swirl_flow[:, :, below],
        buoyancy[:, :, top],
        buoyancy[:, :, below],
        stiffness[:, :, top],
        wall,
        source_top,
    ]
    stack_c = jnp.stack(planes)
    n_planes = len(planes)
    tile = 8
    reach = 3
    packed = jnp.pad(jnp.transpose(stack_c, (1, 2, 0)), ((0, 0), (0, 0), (0, nr - n_planes)))
    stack_all = jnp.concatenate([stack_f, packed[None]], axis=0)
    n_f = stack_f.shape[0]
    widened = with_halo(stack_all, "ax", 2, tile, tile, False)
    size_az, length_a = (lax.axis_size("az"), widened.shape[1])
    up = [(i, (i + 1) % size_az) for i in range(size_az)]
    down = [(j, i) for i, j in up]
    row_shape = (1,) + widened.shape[2:]
    sent_up = jnp.concatenate(
        [widened[:n_f, length_a - 1 :], widened[n_f, length_a - reach :].reshape((reach,) + row_shape)], axis=0
    )
    sent_down = jnp.concatenate(
        [
            widened[:n_f, :2].reshape((2 * n_f,) + row_shape),
            widened[n_f, :reach].reshape((reach,) + row_shape),
        ],
        axis=0,
    )
    from_below = lax.ppermute(sent_up, "az", up)
    from_above = lax.ppermute(sent_down, "az", down)
    wide_f = jnp.concatenate(
        [from_below[:n_f], widened[:n_f], from_above[: 2 * n_f].reshape((n_f, 2) + widened.shape[2:])], axis=1
    )
    wide_packed = jnp.concatenate(
        [from_below[n_f:, 0], widened[n_f], from_above[2 * n_f :, 0]], axis=0
    )
    wide_c = jnp.transpose(wide_packed[:, :, :n_planes], (2, 0, 1))

    oc = (reach, tile)
    p_t, p_b, va_t, vx_t, vr_b, u_t, u_b, w_t, w_b, b_t, b_b, s_t, wall_c, src_c = [wide_c[i] for i in range(14)]
    ea, ex = na + 3, nx + 3

    def c(f, da, dx, la, lx):
        return win(f, oc, da, dx, la, lx)

    def advect_c(f, u, w, da, dx, la, lx):
        return c(u, da, dx, la, lx) * (c(f, da, dx + 1, la, lx) - c(f, da, dx - 1, la, lx)) * 0.5 + c(
            w, da, dx, la, lx
        ) * (c(f, da + 1, dx, la, lx) - c(f, da - 1, dx, la, lx)) * 0.5

    new_az = c(va_t, -2, -1, ea + 1, ex) - step_dt * (
        advect_c(va_t, u_t, w_t, -2, -1, ea + 1, ex)
        + c(b_t, -2, -1, ea + 1, ex) * (c(p_t, -1, -1, ea + 1, ex) - c(p_t, -2, -1, ea + 1, ex))
    )
    new_ax = c(vx_t, -1, -2, ea, ex + 1) - step_dt * (
        advect_c(vx_t, u_t, w_t, -1, -2, ea, ex + 1)
        + c(b_t, -1, -2, ea, ex + 1) * (c(p_t, -1, -1, ea, ex + 1) - c(p_t, -1, -2, ea, ex + 1))
    )
    rad_top = c(wall_c, -1, -1, ea, ex) * c(p_t, -1, -1, ea, ex)
    rad_below = c(vr_b, -1, -1, ea, ex) - step_dt * (
        advect_c(vr_b, u_b, w_b, -1, -1, ea, ex)
        + c(b_b, -1, -1, ea, ex) * (c(p_t, -1, -1, ea, ex) - c(p_b, -1, -1, ea, ex))
    )
    spread = (new_az[1:] - new_az[:-1]) + (new_ax[:, 1:] - new_ax[:, :-1]) + (rad_top - rad_below)
    press_ring = (
        c(p_t, -1, -1, ea, ex)
        - step_dt * (advect_c(p_t, u_t, w_t, -1, -1, ea, ex) + c(s_t, -1, -1, ea, ex) * spread)
        + step_dt * c(src_c, -1, -1, ea, ex)
    )

    total_az = na * lax.axis_size("az")
    first_az = lax.axis_index("az") * na
    first_ax = lax.axis_index("ax") * nx
    ring_az = jnp.remainder(mic_az - first_az + 1, total_az)
    ring_ax = mic_ax - first_ax + 1
    on_ring = (ring_az < ea) & (ring_ax >= 0) & (ring_ax < ex)
    owned = (ring_az >= 1) & (ring_az <= na) & (ring_ax >= 1) & (ring_ax <= nx)
    ring_cell = jnp.where(on_ring, ring_az * ex + ring_ax, -1)
    cell_hot = ring_cell[:, None] == lax.broadcasted_iota(jnp.int32, (1, ea * ex), 1)
    heard = jnp.sum(jnp.where(cell_hot, press_ring.reshape(1, ea * ex), 0.0), axis=1)
    misses = heard - measured
    square_sum = jnp.sum(jnp.where(owned, misses * misses, 0.0))
    placed = jnp.sum(jnp.where(cell_hot, misses[:, None], 0.0), axis=0).reshape(ea, ex)

    push_e = -step_dt * c(s_t, -1, -1, ea, ex) * placed
    r1a, r1x = na + 2, nx + 2
    head_az_e = push_e[:r1a, :r1x] - push_e[1 : 1 + r1a, :r1x]
    head_ax_e = push_e[:r1a, :r1x] - push_e[:r1a, 1 : 1 + r1x]
    head_rad_e = -push_e[:r1a, :r1x]
    u_t1, w_t1 = c(u_t, -1, -1, r1a, r1x), c(w_t, -1, -1, r1a, r1x)
    u_b1, w_b1 = c(u_b, -1, -1, r1a, r1x), c(w_b, -1, -1, r1a, r1x)
    b_t1 = c(b_t, -1, -1, r1a, r1x)
    own_e = (slice(1, 1 + na), slice(1, 1 + nx))
    back_press_t = (
        placed[1 : 1 + na, 1 : 1 + nx]
        - step_dt * advect_back(u_t1 * placed[:r1a, :r1x], w_t1 * placed[:r1a, :r1x], na, nx)
    )
    shove_az = step_dt * b_t1 * head_az_e
    shove_ax = step_dt * b_t1 * head_ax_e
    b_b0, wall_0, push_0 = c(b_b, 0, 0, na, nx), c(wall_c, 0, 0, na, nx), push_e[own_e]
    back_press_t = (
        back_press_t
        + (shove_az[own_e] - shove_az[0:na, 1 : 1 + nx])
        + (shove_ax[own_e] - shove_ax[1 : 1 + na, 0:nx])
        + step_dt * b_b0 * push_0
        + wall_0 * push_0
    )
    back_press_b = -step_dt * b_b0 * push_0
    back_az_t = head_az_e[own_e] - step_dt * advect_back(u_t1 * head_az_e, w_t1 * head_az_e, na, nx)
    back_ax_t = head_ax_e[own_e] - step_dt * advect_back(u_t1 * head_ax_e, w_t1 * head_ax_e, na, nx)
    back_rad_b = head_rad_e[own_e] - step_dt * advect_back(u_b1 * head_rad_e, w_b1 * head_rad_e, na, nx)
    zero = jnp.zeros_like(back_press_b)
    extra = jnp.stack(
        [
            jnp.stack([back_press_b, back_press_t], axis=-1),
            jnp.stack([zero, back_az_t], axis=-1),
            jnp.stack([zero, back_ax_t], axis=-1),
            jnp.stack([back_rad_b, zero], axis=-1),
        ]
    )

    of = (1, tile)
    g_a0, g_a1, g_a2, g_a3, g_u, g_w, g_b, g_push = [wide_f[i] for i in range(8)]

    def at(field, da, dx):
        return win(field, of, da, dx, na, nx)

    def head_az(da, dx):
        return at(g_a1, da, dx) + at(g_push, da, dx) - at(g_push, da + 1, dx)

    def head_ax(da, dx):
        return at(g_a2, da, dx) + at(g_push, da, dx) - at(g_push, da, dx + 1)

    casing = casing_mask((na, nx, nr))

    def head_rad(da, dx):
        push_here = at(g_push, da, dx)
        return at(g_a3, da, dx) + push_here - rad_next(push_here)

    def head_masked(da, dx):
        return jnp.where(casing, 0.0, head_rad(da, dx))

    def back_advect(head):
        return 0.5 * (at(g_u, 0, -1) * head(0, -1) - at(g_u, 0, 1) * head(0, 1)) + 0.5 * (
            at(g_w, -1, 0) * head(-1, 0) - at(g_w, 1, 0) * head(1, 0)
        )

    def seed(da, dx):
        return at(g_a0, da, dx)

    backs = [head(0, 0) - step_dt * back_advect(head) for head in (head_az, head_ax, head_masked)]
    shove_r = step_dt * at(g_b, 0, 0) * head_masked(0, 0)
    head_rad_own = head_rad(0, 0)
    back_press = (
        seed(0, 0)
        - step_dt * back_advect(seed)
        + (step_dt * at(g_b, 0, 0) * head_az(0, 0) - step_dt * at(g_b, -1, 0) * head_az(-1, 0))
        + (step_dt * at(g_b, 0, 0) * head_ax(0, 0) - step_dt * at(g_b, 0, -1) * head_ax(0, -1))
        + (shove_r - rad_prev(shove_r))
        + jnp.where(casing, wall[:, :, None] * head_rad_own, 0.0)
    )
    base = jnp.stack([back_press] + backs)

    press_top = acoustic[0, :, :, top]
    sens_base = press_top * (adjoint_in[3, :, :, top] + push[:, :, top])
    sens_placed = press_top * push_0
    seg_base = jnp.sum(jnp.where(segment_hot, sens_base[:, :, None], 0.0), axis=(0, 1))
    seg_placed = jnp.sum(jnp.where(segment_hot, sens_placed[:, :, None], 0.0), axis=(0, 1))

    totals = butterfly_sum(jnp.concatenate([square_sum[None], seg_base, seg_placed]), ("ax", "az"))
    mean_sq = totals[0] / mic_az.shape[0] + epsilon
    grad_scale = (na * lax.axis_size("az") * nx * lax.axis_size("ax") / nseg) ** (-0.5)
    liner_grad = (totals[1 : 1 + nseg] + totals[1 + nseg :] / mean_sq) * grad_scale
    misfit = 0.5 * jnp.log(mean_sq)
    lane = lax.broadcasted_iota(jnp.int32, (1, 1, 1, nr), 3)
    extra_scaled = extra / mean_sq
    correction = jnp.where(
        lane == nr - 1,
        extra_scaled[..., 1:2],
        jnp.where(lane == nr - 2, extra_scaled[..., 0:1], 0.0),
    )
    adjoint_out = base + correction
    return (adjoint_out, liner_grad, misfit)


def solution(mesh):
    placed = (
        P(None, "az", "ax", None),
        P(None, "az", "ax", None),
        P(None, "az", "ax", None),
        P(),
        P("az", "ax"),
        P("az", "ax"),
        P(),
        P(),
        P(),
        P(),
    )
    return jax.shard_map(
        shards,
        mesh=mesh,
        in_specs=placed,
        out_specs=(P(None, "az", "ax", None), P(), P()),
        check_vma=False,
    )
```

```python
import jax
import jax.numpy as jnp
from jax import lax
from jax.sharding import PartitionSpec as P

step_dt = 0.25
epsilon = 1e-06


def with_halo(array, axis, dim, before, after, wrap):
    size, length = (lax.axis_size(axis), array.shape[dim])
    up = [(i, (i + 1) % size) for i in range(size if wrap else size - 1)]
    down = [(j, i) for i, j in up]
    parts = []
    if before:
        parts.append(lax.ppermute(lax.slice_in_dim(array, length - before, length, axis=dim), axis, up))
    parts.append(array)
    if after:
        parts.append(lax.ppermute(lax.slice_in_dim(array, 0, after, axis=dim), axis, down))
    return jnp.concatenate(parts, axis=dim)


def exchange(array, before, after, ax_before=None, ax_after=None):
    ax_before = before if ax_before is None else ax_before
    ax_after = after if ax_after is None else ax_after
    widened = with_halo(array, "ax", 2, ax_before, ax_after, False)
    return with_halo(widened, "az", 1, before, after, True)


def win(values, origin, da, dx, na, nx):
    a0, x0 = origin[0] + da, origin[1] + dx
    return values[a0 : a0 + na, x0 : x0 + nx]


def rad_next(values):
    return jnp.concatenate([values[..., 1:], jnp.zeros_like(values[..., :1])], axis=-1)


def rad_prev(values):
    return jnp.concatenate([jnp.zeros_like(values[..., :1]), values[..., :-1]], axis=-1)


def casing_mask(shape):
    return lax.broadcasted_iota(jnp.int32, shape, len(shape) - 1) == shape[-1] - 1


def advect_back(carried_ax, carried_az, na, nx):
    return 0.5 * (carried_ax[..., 1 : 1 + na, 0:nx] - carried_ax[..., 1 : 1 + na, 2 : 2 + nx]) + 0.5 * (
        carried_az[..., 0:na, 1 : 1 + nx] - carried_az[..., 2 : 2 + na, 1 : 1 + nx]
    )


def advect_back4(carried_ax, carried_az, na, nx):
    return 0.5 * (carried_ax[:, 1 : 1 + na, 0:nx, :] - carried_ax[:, 1 : 1 + na, 2 : 2 + nx, :]) + 0.5 * (
        carried_az[:, 0:na, 1 : 1 + nx, :] - carried_az[:, 2 : 2 + na, 1 : 1 + nx, :]
    )


def butterfly_sum(values, axes):
    for axis in axes:
        size = lax.axis_size(axis)
        if size & (size - 1):
            values = lax.psum(values, axis)
            continue
        step = 1
        while step < size:
            values = values + lax.ppermute(values, axis, [(i, i ^ step) for i in range(size)])
            step *= 2
    return values


def shards(
    acoustic,
    mean_flow,
    adjoint_in,
    admittance,
    segment_id,
    noise_code,
    noise_table,
    mic_az,
    mic_ax,
    measured,
):
    na, nx, nr = (acoustic.shape[1], acoustic.shape[2], acoustic.shape[3])
    nseg = admittance.shape[0]
    buoyancy = 1.0 / mean_flow[2]
    stiffness = mean_flow[2] * mean_flow[3] * mean_flow[3]
    axial_flow, swirl_flow = (mean_flow[0], mean_flow[1])

    segment_hot = segment_id[:, :, None] == lax.broadcasted_iota(jnp.int32, (1, 1, nseg), 2)
    wall = jnp.sum(jnp.where(segment_hot, admittance, 0.0), axis=2)
    noise_hot = noise_code[:, :, None] == lax.broadcasted_iota(jnp.int32, (1, 1, noise_table.shape[0]), 2)
    top_profile = (nr - 1 + 0.5) / nr
    source_top = jnp.sum(jnp.where(noise_hot, noise_table, 0.0), axis=2) * top_profile

    a0 = adjoint_in[0]
    push = -step_dt * stiffness * a0
    stack_f = jnp.stack([a0, adjoint_in[1], adjoint_in[2], adjoint_in[3], axial_flow, swirl_flow, buoyancy, push])
    top, below = nr - 1, nr - 2
    planes = [
        acoustic[0, :, :, top],
        acoustic[0, :, :, below],
        acoustic[1, :, :, top],
        acoustic[2, :, :, top],
        acoustic[3, :, :, below],
        axial_flow[:, :, top],
        axial_flow[:, :, below],
        swirl_flow[:, :, top],
        swirl_flow[:, :, below],
        buoyancy[:, :, top],
        buoyancy[:, :, below],
        stiffness[:, :, top],
        wall,
        source_top,
    ]
    stack_c = jnp.stack(planes)
    n_planes = len(planes)
    tile = 8
    reach = 3
    packed = jnp.pad(jnp.transpose(stack_c, (1, 2, 0)), ((0, 0), (0, 0), (0, nr - n_planes)))
    stack_all = jnp.concatenate([stack_f, packed[None]], axis=0)
    n_f = stack_f.shape[0]
    widened = with_halo(stack_all, "ax", 2, tile, tile, False)
    size_az, length_a = (lax.axis_size("az"), widened.shape[1])
    up = [(i, (i + 1) % size_az) for i in range(size_az)]
    down = [(j, i) for i, j in up]
    sent_up = jnp.stack(
        [widened[f, length_a - 1] for f in (0, 1, 2, 3, 5, 6, 7)]
        + [widened[n_f, length_a - reach + k] for k in range(reach)]
    )
    sent_down = jnp.stack(
        [widened[f, 0] for f in (0, 1, 2, 3, 5, 7)] + [widened[7, 1]] + [widened[n_f, k] for k in range(reach)]
    )
    from_below = lax.ppermute(sent_up, "az", up)
    from_above = lax.ppermute(sent_down, "az", down)
    blank = jnp.zeros_like(from_below[0])
    row_before = jnp.stack([from_below[i] for i in (0, 1, 2, 3)] + [blank] + [from_below[i] for i in (4, 5, 6)])
    row_after = jnp.stack([from_above[i] for i in (0, 1, 2, 3)] + [blank, from_above[4], blank, from_above[5]])
    row_after2 = jnp.stack([blank] * 7 + [from_above[6]])
    wide_f = jnp.concatenate(
        [row_before[:, None], widened[:n_f], row_after[:, None], row_after2[:, None]], axis=1
    )
    wide_packed = jnp.concatenate([from_below[7:], widened[n_f], from_above[7:]], axis=0)
    wide_c = jnp.transpose(wide_packed[:, :, :n_planes], (2, 0, 1))

    oc = (reach, tile)
    p_t, p_b, va_t, vx_t, vr_b, u_t, u_b, w_t, w_b, b_t, b_b, s_t, wall_c, src_c = [wide_c[i] for i in range(14)]
    ea, ex = na + 3, nx + 3

    def c(f, da, dx, la, lx):
        return win(f, oc, da, dx, la, lx)

    def advect_c(f, u, w, da, dx, la, lx):
        return c(u, da, dx, la, lx) * (c(f, da, dx + 1, la, lx) - c(f, da, dx - 1, la, lx)) * 0.5 + c(
            w, da, dx, la, lx
        ) * (c(f, da + 1, dx, la, lx) - c(f, da - 1, dx, la, lx)) * 0.5

    new_az = c(va_t, -2, -1, ea + 1, ex) - step_dt * (
        advect_c(va_t, u_t, w_t, -2, -1, ea + 1, ex)
        + c(b_t, -2, -1, ea + 1, ex) * (c(p_t, -1, -1, ea + 1, ex) - c(p_t, -2, -1, ea + 1, ex))
    )
    new_ax = c(vx_t, -1, -2, ea, ex + 1) - step_dt * (
        advect_c(vx_t, u_t, w_t, -1, -2, ea, ex + 1)
        + c(b_t, -1, -2, ea, ex + 1) * (c(p_t, -1, -1, ea, ex + 1) - c(p_t, -1, -2, ea, ex + 1))
    )
    rad_top = c(wall_c, -1, -1, ea, ex) * c(p_t, -1, -1, ea, ex)
    rad_below = c(vr_b, -1, -1, ea, ex) - step_dt * (
        advect_c(vr_b, u_b, w_b, -1, -1, ea, ex)
        + c(b_b, -1, -1, ea, ex) * (c(p_t, -1, -1, ea, ex) - c(p_b, -1, -1, ea, ex))
    )
    spread = (new_az[1:] - new_az[:-1]) + (new_ax[:, 1:] - new_ax[:, :-1]) + (rad_top - rad_below)
    press_ring = (
        c(p_t, -1, -1, ea, ex)
        - step_dt * (advect_c(p_t, u_t, w_t, -1, -1, ea, ex) + c(s_t, -1, -1, ea, ex) * spread)
        + step_dt * c(src_c, -1, -1, ea, ex)
    )

    total_az = na * lax.axis_size("az")
    first_az = lax.axis_index("az") * na
    first_ax = lax.axis_index("ax") * nx
    ring_az = jnp.remainder(mic_az - first_az + 1, total_az)
    ring_ax = mic_ax - first_ax + 1
    on_ring = (ring_az < ea) & (ring_ax >= 0) & (ring_ax < ex)
    owned = (ring_az >= 1) & (ring_az <= na) & (ring_ax >= 1) & (ring_ax <= nx)
    ring_cell = jnp.where(on_ring, ring_az * ex + ring_ax, -1)
    cell_hot = ring_cell[:, None] == lax.broadcasted_iota(jnp.int32, (1, ea * ex), 1)
    heard = jnp.sum(jnp.where(cell_hot, press_ring.reshape(1, ea * ex), 0.0), axis=1)
    misses = heard - measured
    square_sum = jnp.sum(jnp.where(owned, misses * misses, 0.0))
    placed = jnp.sum(jnp.where(cell_hot, misses[:, None], 0.0), axis=0).reshape(ea, ex)

    push_e = -step_dt * c(s_t, -1, -1, ea, ex) * placed
    r1a, r1x = na + 2, nx + 2
    head_az_e = push_e[:r1a, :r1x] - push_e[1 : 1 + r1a, :r1x]
    head_ax_e = push_e[:r1a, :r1x] - push_e[:r1a, 1 : 1 + r1x]
    head_rad_e = -push_e[:r1a, :r1x]
    u_t1, w_t1 = c(u_t, -1, -1, r1a, r1x), c(w_t, -1, -1, r1a, r1x)
    u_b1, w_b1 = c(u_b, -1, -1, r1a, r1x), c(w_b, -1, -1, r1a, r1x)
    b_t1 = c(b_t, -1, -1, r1a, r1x)
    own_e = (slice(1, 1 + na), slice(1, 1 + nx))
    back_press_t = (
        placed[1 : 1 + na, 1 : 1 + nx]
        - step_dt * advect_back(u_t1 * placed[:r1a, :r1x], w_t1 * placed[:r1a, :r1x], na, nx)
    )
    shove_az = step_dt * b_t1 * head_az_e
    shove_ax = step_dt * b_t1 * head_ax_e
    b_b0, wall_0, push_0 = c(b_b, 0, 0, na, nx), c(wall_c, 0, 0, na, nx), push_e[own_e]
    back_press_t = (
        back_press_t
        + (shove_az[own_e] - shove_az[0:na, 1 : 1 + nx])
        + (shove_ax[own_e] - shove_ax[1 : 1 + na, 0:nx])
        + step_dt * b_b0 * push_0
        + wall_0 * push_0
    )
    back_press_b = -step_dt * b_b0 * push_0
    back_az_t = head_az_e[own_e] - step_dt * advect_back(u_t1 * head_az_e, w_t1 * head_az_e, na, nx)
    back_ax_t = head_ax_e[own_e] - step_dt * advect_back(u_t1 * head_ax_e, w_t1 * head_ax_e, na, nx)
    back_rad_b = head_rad_e[own_e] - step_dt * advect_back(u_b1 * head_rad_e, w_b1 * head_rad_e, na, nx)
    zero = jnp.zeros_like(back_press_b)
    extra = jnp.stack(
        [
            jnp.stack([back_press_b, back_press_t], axis=-1),
            jnp.stack([zero, back_az_t], axis=-1),
            jnp.stack([zero, back_ax_t], axis=-1),
            jnp.stack([back_rad_b, zero], axis=-1),
        ]
    )

    of = (1, tile)
    g_a0, g_a1, g_a2, g_a3, g_u, g_w, g_b, g_push = [wide_f[i] for i in range(8)]

    def at(field, da, dx):
        return win(field, of, da, dx, na, nx)

    def head_az(da, dx):
        return at(g_a1, da, dx) + at(g_push, da, dx) - at(g_push, da + 1, dx)

    def head_ax(da, dx):
        return at(g_a2, da, dx) + at(g_push, da, dx) - at(g_push, da, dx + 1)

    casing = casing_mask((na, nx, nr))

    def head_rad(da, dx):
        push_here = at(g_push, da, dx)
        return at(g_a3, da, dx) + push_here - rad_next(push_here)

    def head_masked(da, dx):
        return jnp.where(casing, 0.0, head_rad(da, dx))

    def back_advect(head):
        return 0.5 * (at(g_u, 0, -1) * head(0, -1) - at(g_u, 0, 1) * head(0, 1)) + 0.5 * (
            at(g_w, -1, 0) * head(-1, 0) - at(g_w, 1, 0) * head(1, 0)
        )

    def seed(da, dx):
        return at(g_a0, da, dx)

    backs = [head(0, 0) - step_dt * back_advect(head) for head in (head_az, head_ax, head_masked)]
    shove_r = step_dt * at(g_b, 0, 0) * head_masked(0, 0)
    head_rad_own = head_rad(0, 0)
    back_press = (
        seed(0, 0)
        - step_dt * back_advect(seed)
        + (step_dt * at(g_b, 0, 0) * head_az(0, 0) - step_dt * at(g_b, -1, 0) * head_az(-1, 0))
        + (step_dt * at(g_b, 0, 0) * head_ax(0, 0) - step_dt * at(g_b, 0, -1) * head_ax(0, -1))
        + (shove_r - rad_prev(shove_r))
        + jnp.where(casing, wall[:, :, None] * head_rad_own, 0.0)
    )
    base = jnp.stack([back_press] + backs)

    press_top = acoustic[0, :, :, top]
    sens_base = press_top * (adjoint_in[3, :, :, top] + push[:, :, top])
    sens_placed = press_top * push_0
    seg_base = jnp.sum(jnp.where(segment_hot, sens_base[:, :, None], 0.0), axis=(0, 1))
    seg_placed = jnp.sum(jnp.where(segment_hot, sens_placed[:, :, None], 0.0), axis=(0, 1))

    totals = butterfly_sum(jnp.concatenate([square_sum[None], seg_base, seg_placed]), ("ax", "az"))
    mean_sq = totals[0] / mic_az.shape[0] + epsilon
    grad_scale = (na * lax.axis_size("az") * nx * lax.axis_size("ax") / nseg) ** (-0.5)
    liner_grad = (totals[1 : 1 + nseg] + totals[1 + nseg :] / mean_sq) * grad_scale
    misfit = 0.5 * jnp.log(mean_sq)
    lane = lax.broadcasted_iota(jnp.int32, (1, 1, 1, nr), 3)
    extra_scaled = extra / mean_sq
    correction = jnp.where(
        lane == nr - 1,
        extra_scaled[..., 1:2],
        jnp.where(lane == nr - 2, extra_scaled[..., 0:1], 0.0),
    )
    adjoint_out = base + correction
    return (adjoint_out, liner_grad, misfit)


def solution(mesh):
    placed = (
        P(None, "az", "ax", None),
        P(None, "az", "ax", None),
        P(None, "az", "ax", None),
        P(),
        P("az", "ax"),
        P("az", "ax"),
        P(),
        P(),
        P(),
        P(),
    )
    return jax.shard_map(
        shards,
        mesh=mesh,
        in_specs=placed,
        out_specs=(P(None, "az", "ax", None), P(), P()),
        check_vma=False,
    )
```

```python
import jax
import jax.numpy as jnp
from jax import lax
from jax.sharding import PartitionSpec as P

step_dt = 0.25
epsilon = 1e-06


def with_halo(array, axis, dim, before, after, wrap):
    size, length = (lax.axis_size(axis), array.shape[dim])
    up = [(i, (i + 1) % size) for i in range(size if wrap else size - 1)]
    down = [(j, i) for i, j in up]
    parts = []
    if before:
        parts.append(lax.ppermute(lax.slice_in_dim(array, length - before, length, axis=dim), axis, up))
    parts.append(array)
    if after:
        parts.append(lax.ppermute(lax.slice_in_dim(array, 0, after, axis=dim), axis, down))
    return jnp.concatenate(parts, axis=dim)


def exchange(array, before, after, ax_before=None, ax_after=None):
    ax_before = before if ax_before is None else ax_before
    ax_after = after if ax_after is None else ax_after
    widened = with_halo(array, "ax", 2, ax_before, ax_after, False)
    return with_halo(widened, "az", 1, before, after, True)


def win(values, origin, da, dx, na, nx):
    a0, x0 = origin[0] + da, origin[1] + dx
    return values[a0 : a0 + na, x0 : x0 + nx]


def rad_next(values):
    return jnp.concatenate([values[..., 1:], jnp.zeros_like(values[..., :1])], axis=-1)


def rad_prev(values):
    return jnp.concatenate([jnp.zeros_like(values[..., :1]), values[..., :-1]], axis=-1)


def casing_mask(shape):
    return lax.broadcasted_iota(jnp.int32, shape, len(shape) - 1) == shape[-1] - 1


def advect_back(carried_ax, carried_az, na, nx):
    return 0.5 * (carried_ax[..., 1 : 1 + na, 0:nx] - carried_ax[..., 1 : 1 + na, 2 : 2 + nx]) + 0.5 * (
        carried_az[..., 0:na, 1 : 1 + nx] - carried_az[..., 2 : 2 + na, 1 : 1 + nx]
    )


def advect_back4(carried_ax, carried_az, na, nx):
    return 0.5 * (carried_ax[:, 1 : 1 + na, 0:nx, :] - carried_ax[:, 1 : 1 + na, 2 : 2 + nx, :]) + 0.5 * (
        carried_az[:, 0:na, 1 : 1 + nx, :] - carried_az[:, 2 : 2 + na, 1 : 1 + nx, :]
    )


def butterfly_sum(values, axes):
    for axis in axes:
        size = lax.axis_size(axis)
        if size & (size - 1):
            values = lax.psum(values, axis)
            continue
        step = 1
        while step < size:
            values = values + lax.ppermute(values, axis, [(i, i ^ step) for i in range(size)])
            step *= 2
    return values


def shards(
    acoustic,
    mean_flow,
    adjoint_in,
    admittance,
    segment_id,
    noise_code,
    noise_table,
    mic_az,
    mic_ax,
    measured,
):
    na, nx, nr = (acoustic.shape[1], acoustic.shape[2], acoustic.shape[3])
    nseg = admittance.shape[0]
    buoyancy = 1.0 / mean_flow[2]
    stiffness = mean_flow[2] * mean_flow[3] * mean_flow[3]
    axial_flow, swirl_flow = (mean_flow[0], mean_flow[1])

    segment_hot = segment_id[:, :, None] == lax.broadcasted_iota(jnp.int32, (1, 1, nseg), 2)
    wall = jnp.sum(jnp.where(segment_hot, admittance, 0.0), axis=2)
    noise_hot = noise_code[:, :, None] == lax.broadcasted_iota(jnp.int32, (1, 1, noise_table.shape[0]), 2)
    top_profile = (nr - 1 + 0.5) / nr
    source_top = jnp.sum(jnp.where(noise_hot, noise_table, 0.0), axis=2) * top_profile

    a0 = adjoint_in[0]
    push = -step_dt * stiffness * a0
    stack_f = jnp.stack([a0, adjoint_in[1], adjoint_in[2], adjoint_in[3], axial_flow, swirl_flow, buoyancy, push])
    top, below = nr - 1, nr - 2
    planes = [
        acoustic[0, :, :, top],
        acoustic[0, :, :, below],
        acoustic[1, :, :, top],
        acoustic[2, :, :, top],
        acoustic[3, :, :, below],
        axial_flow[:, :, top],
        axial_flow[:, :, below],
        swirl_flow[:, :, top],
        swirl_flow[:, :, below],
        buoyancy[:, :, top],
        buoyancy[:, :, below],
        stiffness[:, :, top],
        wall,
        source_top,
    ]
    stack_c = jnp.stack(planes)
    n_planes = len(planes)
    tile = 8
    reach = 3
    packed = jnp.pad(jnp.transpose(stack_c, (1, 2, 0)), ((0, 0), (0, 0), (0, nr - n_planes)))
    stack_all = jnp.concatenate([stack_f, packed[None]], axis=0)
    n_f = stack_f.shape[0]
    widened = with_halo(stack_all, "ax", 2, tile, tile, False)
    size_az, length_a = (lax.axis_size("az"), widened.shape[1])
    up = [(i, (i + 1) % size_az) for i in range(size_az)]
    down = [(j, i) for i, j in up]
    sent_up = jnp.stack(
        [widened[f, length_a - 1] for f in (0, 1, 2, 3, 5, 6, 7)]
        + [widened[n_f, length_a - reach + k] for k in range(reach)]
    )
    sent_down = jnp.stack(
        [widened[f, 0] for f in (0, 1, 2, 3, 5, 7)] + [widened[7, 1]] + [widened[n_f, k] for k in range(reach)]
    )
    from_below = lax.ppermute(sent_up, "az", up)
    from_above = lax.ppermute(sent_down, "az", down)
    blank = jnp.zeros_like(from_below[0])
    row_before = jnp.stack([from_below[i] for i in (0, 1, 2, 3)] + [blank] + [from_below[i] for i in (4, 5, 6)])
    row_after = jnp.stack([from_above[i] for i in (0, 1, 2, 3)] + [blank, from_above[4], blank, from_above[5]])
    row_after2 = jnp.stack([blank] * 7 + [from_above[6]])
    wide_f = jnp.concatenate(
        [row_before[:, None], widened[:n_f], row_after[:, None], row_after2[:, None]], axis=1
    )
    wide_packed = jnp.concatenate([from_below[7:], widened[n_f], from_above[7:]], axis=0)
    wide_c = jnp.transpose(wide_packed[:, :, :n_planes], (2, 0, 1))

    oc = (reach, tile)
    p_t, p_b, va_t, vx_t, vr_b, u_t, u_b, w_t, w_b, b_t, b_b, s_t, wall_c, src_c = [wide_c[i] for i in range(14)]
    ea, ex = na + 3, nx + 3

    def c(f, da, dx, la, lx):
        return win(f, oc, da, dx, la, lx)

    def advect_c(f, u, w, da, dx, la, lx):
        return c(u, da, dx, la, lx) * (c(f, da, dx + 1, la, lx) - c(f, da, dx - 1, la, lx)) * 0.5 + c(
            w, da, dx, la, lx
        ) * (c(f, da + 1, dx, la, lx) - c(f, da - 1, dx, la, lx)) * 0.5

    new_az = c(va_t, -2, -1, ea + 1, ex) - step_dt * (
        advect_c(va_t, u_t, w_t, -2, -1, ea + 1, ex)
        + c(b_t, -2, -1, ea + 1, ex) * (c(p_t, -1, -1, ea + 1, ex) - c(p_t, -2, -1, ea + 1, ex))
    )
    new_ax = c(vx_t, -1, -2, ea, ex + 1) - step_dt * (
        advect_c(vx_t, u_t, w_t, -1, -2, ea, ex + 1)
        + c(b_t, -1, -2, ea, ex + 1) * (c(p_t, -1, -1, ea, ex + 1) - c(p_t, -1, -2, ea, ex + 1))
    )
    rad_top = c(wall_c, -1, -1, ea, ex) * c(p_t, -1, -1, ea, ex)
    rad_below = c(vr_b, -1, -1, ea, ex) - step_dt * (
        advect_c(vr_b, u_b, w_b, -1, -1, ea, ex)
        + c(b_b, -1, -1, ea, ex) * (c(p_t, -1, -1, ea, ex) - c(p_b, -1, -1, ea, ex))
    )
    spread = (new_az[1:] - new_az[:-1]) + (new_ax[:, 1:] - new_ax[:, :-1]) + (rad_top - rad_below)
    press_ring = (
        c(p_t, -1, -1, ea, ex)
        - step_dt * (advect_c(p_t, u_t, w_t, -1, -1, ea, ex) + c(s_t, -1, -1, ea, ex) * spread)
        + step_dt * c(src_c, -1, -1, ea, ex)
    )

    total_az = na * lax.axis_size("az")
    first_az = lax.axis_index("az") * na
    first_ax = lax.axis_index("ax") * nx
    ring_az = jnp.remainder(mic_az - first_az + 1, total_az)
    ring_ax = mic_ax - first_ax + 1
    on_ring = (ring_az < ea) & (ring_ax >= 0) & (ring_ax < ex)
    owned = (ring_az >= 1) & (ring_az <= na) & (ring_ax >= 1) & (ring_ax <= nx)
    ring_cell = jnp.where(on_ring, ring_az * ex + ring_ax, -1)
    cell_hot = ring_cell[:, None] == lax.broadcasted_iota(jnp.int32, (1, ea * ex), 1)
    heard = jnp.sum(jnp.where(cell_hot, press_ring.reshape(1, ea * ex), 0.0), axis=1)
    misses = heard - measured
    square_sum = jnp.sum(jnp.where(owned, misses * misses, 0.0))
    placed = jnp.sum(jnp.where(cell_hot, misses[:, None], 0.0), axis=0).reshape(ea, ex)

    push_e = -step_dt * c(s_t, -1, -1, ea, ex) * placed
    r1a, r1x = na + 2, nx + 2
    head_az_e = push_e[:r1a, :r1x] - push_e[1 : 1 + r1a, :r1x]
    head_ax_e = push_e[:r1a, :r1x] - push_e[:r1a, 1 : 1 + r1x]
    head_rad_e = -push_e[:r1a, :r1x]
    u_t1, w_t1 = c(u_t, -1, -1, r1a, r1x), c(w_t, -1, -1, r1a, r1x)
    u_b1, w_b1 = c(u_b, -1, -1, r1a, r1x), c(w_b, -1, -1, r1a, r1x)
    b_t1 = c(b_t, -1, -1, r1a, r1x)
    own_e = (slice(1, 1 + na), slice(1, 1 + nx))
    back_press_t = (
        placed[1 : 1 + na, 1 : 1 + nx]
        - step_dt * advect_back(u_t1 * placed[:r1a, :r1x], w_t1 * placed[:r1a, :r1x], na, nx)
    )
    shove_az = step_dt * b_t1 * head_az_e
    shove_ax = step_dt * b_t1 * head_ax_e
    b_b0, wall_0, push_0 = c(b_b, 0, 0, na, nx), c(wall_c, 0, 0, na, nx), push_e[own_e]
    back_press_t = (
        back_press_t
        + (shove_az[own_e] - shove_az[0:na, 1 : 1 + nx])
        + (shove_ax[own_e] - shove_ax[1 : 1 + na, 0:nx])
        + step_dt * b_b0 * push_0
        + wall_0 * push_0
    )
    back_press_b = -step_dt * b_b0 * push_0
    back_az_t = head_az_e[own_e] - step_dt * advect_back(u_t1 * head_az_e, w_t1 * head_az_e, na, nx)
    back_ax_t = head_ax_e[own_e] - step_dt * advect_back(u_t1 * head_ax_e, w_t1 * head_ax_e, na, nx)
    back_rad_b = head_rad_e[own_e] - step_dt * advect_back(u_b1 * head_rad_e, w_b1 * head_rad_e, na, nx)
    zero = jnp.zeros_like(back_press_b)
    extra = jnp.stack(
        [
            jnp.stack([back_press_b, back_press_t], axis=-1),
            jnp.stack([zero, back_az_t], axis=-1),
            jnp.stack([zero, back_ax_t], axis=-1),
            jnp.stack([back_rad_b, zero], axis=-1),
        ]
    )

    of = (1, tile)
    g_a0, g_a1, g_a2, g_a3, g_u, g_w, g_b, g_push = [wide_f[i] for i in range(8)]

    def at(field, da, dx):
        return win(field, of, da, dx, na, nx)

    def head_az(da, dx):
        return at(g_a1, da, dx) + at(g_push, da, dx) - at(g_push, da + 1, dx)

    def head_ax(da, dx):
        return at(g_a2, da, dx) + at(g_push, da, dx) - at(g_push, da, dx + 1)

    casing = casing_mask((na, nx, nr))

    def head_rad(da, dx):
        push_here = at(g_push, da, dx)
        return at(g_a3, da, dx) + push_here - rad_next(push_here)

    def head_masked(da, dx):
        return jnp.where(casing, 0.0, head_rad(da, dx))

    def back_advect(head):
        return 0.5 * (at(g_u, 0, -1) * head(0, -1) - at(g_u, 0, 1) * head(0, 1)) + 0.5 * (
            at(g_w, -1, 0) * head(-1, 0) - at(g_w, 1, 0) * head(1, 0)
        )

    def seed(da, dx):
        return at(g_a0, da, dx)

    backs = [head(0, 0) - step_dt * back_advect(head) for head in (head_az, head_ax, head_masked)]
    shove_r = step_dt * at(g_b, 0, 0) * head_masked(0, 0)
    head_rad_own = head_rad(0, 0)
    back_press = (
        seed(0, 0)
        - step_dt * back_advect(seed)
        + (step_dt * at(g_b, 0, 0) * head_az(0, 0) - step_dt * at(g_b, -1, 0) * head_az(-1, 0))
        + (step_dt * at(g_b, 0, 0) * head_ax(0, 0) - step_dt * at(g_b, 0, -1) * head_ax(0, -1))
        + (shove_r - rad_prev(shove_r))
        + jnp.where(casing, wall[:, :, None] * head_rad_own, 0.0)
    )
    base = jnp.stack([back_press] + backs)

    press_top = acoustic[0, :, :, top]
    sens_base = press_top * (adjoint_in[3, :, :, top] + push[:, :, top])
    sens_placed = press_top * push_0
    seg_base = jnp.sum(jnp.where(segment_hot, sens_base[:, :, None], 0.0), axis=(0, 1))
    seg_placed = jnp.sum(jnp.where(segment_hot, sens_placed[:, :, None], 0.0), axis=(0, 1))

    totals = butterfly_sum(jnp.concatenate([square_sum[None], seg_base, seg_placed]), ("az", "ax"))
    mean_sq = totals[0] / mic_az.shape[0] + epsilon
    grad_scale = (na * lax.axis_size("az") * nx * lax.axis_size("ax") / nseg) ** (-0.5)
    liner_grad = (totals[1 : 1 + nseg] + totals[1 + nseg :] / mean_sq) * grad_scale
    misfit = 0.5 * jnp.log(mean_sq)
    lane = lax.broadcasted_iota(jnp.int32, (1, 1, 1, nr), 3)
    extra_scaled = extra / mean_sq
    correction = jnp.where(
        lane == nr - 1,
        extra_scaled[..., 1:2],
        jnp.where(lane == nr - 2, extra_scaled[..., 0:1], 0.0),
    )
    adjoint_out = base + correction
    return (adjoint_out, liner_grad, misfit)


def solution(mesh):
    placed = (
        P(None, "az", "ax", None),
        P(None, "az", "ax", None),
        P(None, "az", "ax", None),
        P(),
        P("az", "ax"),
        P("az", "ax"),
        P(),
        P(),
        P(),
        P(),
    )
    return jax.shard_map(
        shards,
        mesh=mesh,
        in_specs=placed,
        out_specs=(P(None, "az", "ax", None), P(), P()),
        check_vma=False,
    )
```

```python
import jax
import jax.numpy as jnp
from jax import lax
from jax.sharding import PartitionSpec as P

step_dt = 0.25
epsilon = 1e-06
highest = lax.Precision.HIGHEST


def with_halo(array, axis, dim, before, after, wrap):
    size, length = (lax.axis_size(axis), array.shape[dim])
    up = [(i, (i + 1) % size) for i in range(size if wrap else size - 1)]
    down = [(j, i) for i, j in up]
    parts = []
    if before:
        parts.append(lax.ppermute(lax.slice_in_dim(array, length - before, length, axis=dim), axis, up))
    parts.append(array)
    if after:
        parts.append(lax.ppermute(lax.slice_in_dim(array, 0, after, axis=dim), axis, down))
    return jnp.concatenate(parts, axis=dim)


def exchange(array, before, after, ax_before=None, ax_after=None):
    ax_before = before if ax_before is None else ax_before
    ax_after = after if ax_after is None else ax_after
    widened = with_halo(array, "ax", 2, ax_before, ax_after, False)
    return with_halo(widened, "az", 1, before, after, True)


def win(values, origin, da, dx, na, nx):
    a0, x0 = origin[0] + da, origin[1] + dx
    return values[a0 : a0 + na, x0 : x0 + nx]


def rad_next(values):
    return jnp.concatenate([values[..., 1:], jnp.zeros_like(values[..., :1])], axis=-1)


def rad_prev(values):
    return jnp.concatenate([jnp.zeros_like(values[..., :1]), values[..., :-1]], axis=-1)


def casing_mask(shape):
    return lax.broadcasted_iota(jnp.int32, shape, len(shape) - 1) == shape[-1] - 1


def advect_back(carried_ax, carried_az, na, nx):
    return 0.5 * (carried_ax[..., 1 : 1 + na, 0:nx] - carried_ax[..., 1 : 1 + na, 2 : 2 + nx]) + 0.5 * (
        carried_az[..., 0:na, 1 : 1 + nx] - carried_az[..., 2 : 2 + na, 1 : 1 + nx]
    )


def advect_back4(carried_ax, carried_az, na, nx):
    return 0.5 * (carried_ax[:, 1 : 1 + na, 0:nx, :] - carried_ax[:, 1 : 1 + na, 2 : 2 + nx, :]) + 0.5 * (
        carried_az[:, 0:na, 1 : 1 + nx, :] - carried_az[:, 2 : 2 + na, 1 : 1 + nx, :]
    )


def butterfly_sum(values, axes):
    for axis in axes:
        size = lax.axis_size(axis)
        if size & (size - 1):
            values = lax.psum(values, axis)
            continue
        step = 1
        while step < size:
            values = values + lax.ppermute(values, axis, [(i, i ^ step) for i in range(size)])
            step *= 2
    return values


def shards(
    acoustic,
    mean_flow,
    adjoint_in,
    admittance,
    segment_id,
    noise_code,
    noise_table,
    mic_az,
    mic_ax,
    measured,
):
    na, nx, nr = (acoustic.shape[1], acoustic.shape[2], acoustic.shape[3])
    nseg = admittance.shape[0]
    buoyancy = 1.0 / mean_flow[2]
    stiffness = mean_flow[2] * mean_flow[3] * mean_flow[3]
    axial_flow, swirl_flow = (mean_flow[0], mean_flow[1])

    segment_hot = segment_id[:, :, None] == lax.broadcasted_iota(jnp.int32, (1, 1, nseg), 2)
    wall = jnp.sum(jnp.where(segment_hot, admittance, 0.0), axis=2)
    noise_hot = noise_code[:, :, None] == lax.broadcasted_iota(jnp.int32, (1, 1, noise_table.shape[0]), 2)
    top_profile = (nr - 1 + 0.5) / nr
    source_top = jnp.sum(jnp.where(noise_hot, noise_table, 0.0), axis=2) * top_profile

    a0 = adjoint_in[0]
    push = -step_dt * stiffness * a0
    stack_f = jnp.stack([a0, adjoint_in[1], adjoint_in[2], adjoint_in[3], axial_flow, swirl_flow, buoyancy, push])
    top, below = nr - 1, nr - 2
    press_top = acoustic[0, :, :, top]
    planes = [
        press_top,
        acoustic[0, :, :, below],
        acoustic[1, :, :, top],
        acoustic[2, :, :, top],
        acoustic[3, :, :, below],
        axial_flow[:, :, top],
        axial_flow[:, :, below],
        swirl_flow[:, :, top],
        swirl_flow[:, :, below],
        buoyancy[:, :, top],
        buoyancy[:, :, below],
        stiffness[:, :, top],
        wall,
        source_top,
        press_top * (adjoint_in[3, :, :, top] + push[:, :, top]),
        segment_id.astype(jnp.float32),
    ]
    n_planes = len(planes)
    group = jnp.stack(planes)
    size_ax, me_ax = (lax.axis_size("ax"), lax.axis_index("ax"))
    if size_ax & (size_ax - 1):
        group = lax.all_gather(group, "ax", axis=2, tiled=True)
    else:
        step = 1
        while step < size_ax:
            other = lax.ppermute(group, "ax", [(i, i ^ step) for i in range(size_ax)])
            group = jnp.where(
                (me_ax // step) % 2 == 0,
                jnp.concatenate([group, other], axis=2),
                jnp.concatenate([other, group], axis=2),
            )
            step *= 2
    width = group.shape[2]
    tile = 8
    reach = 3
    n_f = stack_f.shape[0]
    widened = with_halo(stack_f, "ax", 2, tile, tile, False)
    size_az, length_a = (lax.axis_size("az"), widened.shape[1])
    up = [(i, (i + 1) % size_az) for i in range(size_az)]
    down = [(j, i) for i, j in up]
    slot = widened.shape[2] * widened.shape[3]

    def as_slots(rows):
        flat = rows.reshape(-1)
        count = -(-flat.shape[0] // slot)
        return jnp.pad(flat, (0, count * slot - flat.shape[0])).reshape((count,) + widened.shape[2:])

    def from_slots(slots):
        return slots.reshape(-1)[: n_planes * reach * width].reshape(n_planes, reach, width)

    sent_up = jnp.concatenate(
        [jnp.stack([widened[f, length_a - 1] for f in (0, 1, 2, 3, 5, 6, 7)]), as_slots(group[:, length_a - reach :])]
    )
    sent_down = jnp.concatenate(
        [jnp.stack([widened[f, 0] for f in (0, 1, 2, 3, 5, 7)] + [widened[7, 1]]), as_slots(group[:, :reach])]
    )
    from_below = lax.ppermute(sent_up, "az", up)
    from_above = lax.ppermute(sent_down, "az", down)
    blank = jnp.zeros_like(from_below[0])
    row_before = jnp.stack([from_below[i] for i in (0, 1, 2, 3)] + [blank] + [from_below[i] for i in (4, 5, 6)])
    row_after = jnp.stack([from_above[i] for i in (0, 1, 2, 3)] + [blank, from_above[4], blank, from_above[5]])
    row_after2 = jnp.stack([blank] * 7 + [from_above[6]])
    wide_f = jnp.concatenate(
        [row_before[:, None], widened[:n_f], row_after[:, None], row_after2[:, None]], axis=1
    )
    group_wide = jnp.concatenate([from_slots(from_below[7:]), group, from_slots(from_above[7:])], axis=1)
    group_wide = jnp.pad(group_wide, ((0, 0), (0, 0), (reach, reach)))

    oc = (reach, reach)
    p_t, p_b, va_t, vx_t, vr_b, u_t, u_b, w_t, w_b, b_t, b_b, s_t, wall_c, src_c = [group_wide[i] for i in range(14)]
    ea, eg, ex = (na + 3, width + 3, nx + 3)

    def c(f, da, dx, la, lx):
        return win(f, oc, da, dx, la, lx)

    def advect_c(f, u, w, da, dx, la, lx):
        return c(u, da, dx, la, lx) * (c(f, da, dx + 1, la, lx) - c(f, da, dx - 1, la, lx)) * 0.5 + c(
            w, da, dx, la, lx
        ) * (c(f, da + 1, dx, la, lx) - c(f, da - 1, dx, la, lx)) * 0.5

    new_az = c(va_t, -2, -1, ea + 1, eg) - step_dt * (
        advect_c(va_t, u_t, w_t, -2, -1, ea + 1, eg)
        + c(b_t, -2, -1, ea + 1, eg) * (c(p_t, -1, -1, ea + 1, eg) - c(p_t, -2, -1, ea + 1, eg))
    )
    new_ax = c(vx_t, -1, -2, ea, eg + 1) - step_dt * (
        advect_c(vx_t, u_t, w_t, -1, -2, ea, eg + 1)
        + c(b_t, -1, -2, ea, eg + 1) * (c(p_t, -1, -1, ea, eg + 1) - c(p_t, -1, -2, ea, eg + 1))
    )
    rad_top = c(wall_c, -1, -1, ea, eg) * c(p_t, -1, -1, ea, eg)
    rad_below = c(vr_b, -1, -1, ea, eg) - step_dt * (
        advect_c(vr_b, u_b, w_b, -1, -1, ea, eg)
        + c(b_b, -1, -1, ea, eg) * (c(p_t, -1, -1, ea, eg) - c(p_b, -1, -1, ea, eg))
    )
    spread = (new_az[1:] - new_az[:-1]) + (new_ax[:, 1:] - new_ax[:, :-1]) + (rad_top - rad_below)
    press_grid = (
        c(p_t, -1, -1, ea, eg)
        - step_dt * (advect_c(p_t, u_t, w_t, -1, -1, ea, eg) + c(s_t, -1, -1, ea, eg) * spread)
        + step_dt * c(src_c, -1, -1, ea, eg)
    )

    total_az = na * lax.axis_size("az")
    first_az = lax.axis_index("az") * na
    grid_az = jnp.remainder(mic_az - first_az + 1, total_az)
    row_hot = (grid_az[:, None] == lax.broadcasted_iota(jnp.int32, (1, ea), 1)).astype(jnp.float32)
    col_hot = (mic_ax + 1)[:, None] == lax.broadcasted_iota(jnp.int32, (1, eg), 1)
    heard = jnp.sum(jnp.where(col_hot, jnp.dot(row_hot, press_grid, precision=highest), 0.0), axis=1)
    misses = heard - measured
    in_group = (grid_az >= 1) & (grid_az <= na)
    square_sum = jnp.sum(jnp.where(in_group, misses * misses, 0.0))
    placed_grid = jnp.dot(row_hot.T, jnp.where(col_hot, misses[:, None], 0.0), precision=highest)

    rows_own = slice(reach, reach + na)
    cols_own = slice(reach, reach + width)
    segment_group = group_wide[15, rows_own, cols_own].astype(jnp.int32)
    segment_hot_group = segment_group[:, :, None] == lax.broadcasted_iota(jnp.int32, (1, 1, nseg), 2)
    sens_placed = (
        group_wide[0, rows_own, cols_own]
        * (-step_dt * group_wide[11, rows_own, cols_own])
        * placed_grid[1 : 1 + na, 1 : 1 + width]
    )
    seg_base = jnp.sum(jnp.where(segment_hot_group, group_wide[14, rows_own, cols_own][:, :, None], 0.0), axis=(0, 1))
    seg_placed = jnp.sum(jnp.where(segment_hot_group, sens_placed[:, :, None], 0.0), axis=(0, 1))

    local = lax.dynamic_slice_in_dim(group_wide, me_ax * nx, nx + 2 * reach, axis=2)
    placed = lax.dynamic_slice_in_dim(placed_grid, me_ax * nx, ex, axis=1)
    p_t, p_b, va_t, vx_t, vr_b, u_t, u_b, w_t, w_b, b_t, b_b, s_t, wall_c, src_c = [local[i] for i in range(14)]

    push_e = -step_dt * c(s_t, -1, -1, ea, ex) * placed
    r1a, r1x = na + 2, nx + 2
    head_az_e = push_e[:r1a, :r1x] - push_e[1 : 1 + r1a, :r1x]
    head_ax_e = push_e[:r1a, :r1x] - push_e[:r1a, 1 : 1 + r1x]
    head_rad_e = -push_e[:r1a, :r1x]
    u_t1, w_t1 = c(u_t, -1, -1, r1a, r1x), c(w_t, -1, -1, r1a, r1x)
    u_b1, w_b1 = c(u_b, -1, -1, r1a, r1x), c(w_b, -1, -1, r1a, r1x)
    b_t1 = c(b_t, -1, -1, r1a, r1x)
    own_e = (slice(1, 1 + na), slice(1, 1 + nx))
    back_press_t = (
        placed[1 : 1 + na, 1 : 1 + nx]
        - step_dt * advect_back(u_t1 * placed[:r1a, :r1x], w_t1 * placed[:r1a, :r1x], na, nx)
    )
    shove_az = step_dt * b_t1 * head_az_e
    shove_ax = step_dt * b_t1 * head_ax_e
    b_b0, wall_0, push_0 = c(b_b, 0, 0, na, nx), c(wall_c, 0, 0, na, nx), push_e[own_e]
    back_press_t = (
        back_press_t
        + (shove_az[own_e] - shove_az[0:na, 1 : 1 + nx])
        + (shove_ax[own_e] - shove_ax[1 : 1 + na, 0:nx])
        + step_dt * b_b0 * push_0
        + wall_0 * push_0
    )
    back_press_b = -step_dt * b_b0 * push_0
    back_az_t = head_az_e[own_e] - step_dt * advect_back(u_t1 * head_az_e, w_t1 * head_az_e, na, nx)
    back_ax_t = head_ax_e[own_e] - step_dt * advect_back(u_t1 * head_ax_e, w_t1 * head_ax_e, na, nx)
    back_rad_b = head_rad_e[own_e] - step_dt * advect_back(u_b1 * head_rad_e, w_b1 * head_rad_e, na, nx)
    zero = jnp.zeros_like(back_press_b)
    extra = jnp.stack(
        [
            jnp.stack([back_press_b, back_press_t], axis=-1),
            jnp.stack([zero, back_az_t], axis=-1),
            jnp.stack([zero, back_ax_t], axis=-1),
            jnp.stack([back_rad_b, zero], axis=-1),
        ]
    )

    of = (1, tile)
    g_a0, g_a1, g_a2, g_a3, g_u, g_w, g_b, g_push = [wide_f[i] for i in range(8)]

    def at(field, da, dx):
        return win(field, of, da, dx, na, nx)

    def head_az(da, dx):
        return at(g_a1, da, dx) + at(g_push, da, dx) - at(g_push, da + 1, dx)

    def head_ax(da, dx):
        return at(g_a2, da, dx) + at(g_push, da, dx) - at(g_push, da, dx + 1)

    casing = casing_mask((na, nx, nr))

    def head_rad(da, dx):
        push_here = at(g_push, da, dx)
        return at(g_a3, da, dx) + push_here - rad_next(push_here)

    def head_masked(da, dx):
        return jnp.where(casing, 0.0, head_rad(da, dx))

    def back_advect(head):
        return 0.5 * (at(g_u, 0, -1) * head(0, -1) - at(g_u, 0, 1) * head(0, 1)) + 0.5 * (
            at(g_w, -1, 0) * head(-1, 0) - at(g_w, 1, 0) * head(1, 0)
        )

    def seed(da, dx):
        return at(g_a0, da, dx)

    backs = [head(0, 0) - step_dt * back_advect(head) for head in (head_az, head_ax, head_masked)]
    shove_r = step_dt * at(g_b, 0, 0) * head_masked(0, 0)
    head_rad_own = head_rad(0, 0)
    back_press = (
        seed(0, 0)
        - step_dt * back_advect(seed)
        + (step_dt * at(g_b, 0, 0) * head_az(0, 0) - step_dt * at(g_b, -1, 0) * head_az(-1, 0))
        + (step_dt * at(g_b, 0, 0) * head_ax(0, 0) - step_dt * at(g_b, 0, -1) * head_ax(0, -1))
        + (shove_r - rad_prev(shove_r))
        + jnp.where(casing, wall[:, :, None] * head_rad_own, 0.0)
    )
    base = jnp.stack([back_press] + backs)

    totals = butterfly_sum(jnp.concatenate([square_sum[None], seg_base, seg_placed]), ("az",))
    mean_sq = totals[0] / mic_az.shape[0] + epsilon
    grad_scale = (na * lax.axis_size("az") * nx * lax.axis_size("ax") / nseg) ** (-0.5)
    liner_grad = (totals[1 : 1 + nseg] + totals[1 + nseg :] / mean_sq) * grad_scale
    misfit = 0.5 * jnp.log(mean_sq)
    lane = lax.broadcasted_iota(jnp.int32, (1, 1, 1, nr), 3)
    extra_scaled = extra / mean_sq
    correction = jnp.where(
        lane == nr - 1,
        extra_scaled[..., 1:2],
        jnp.where(lane == nr - 2, extra_scaled[..., 0:1], 0.0),
    )
    adjoint_out = base + correction
    return (adjoint_out, liner_grad, misfit)


def solution(mesh):
    placed = (
        P(None, "az", "ax", None),
        P(None, "az", "ax", None),
        P(None, "az", "ax", None),
        P(),
        P("az", "ax"),
        P("az", "ax"),
        P(),
        P(),
        P(),
        P(),
    )
    return jax.shard_map(
        shards,
        mesh=mesh,
        in_specs=placed,
        out_specs=(P(None, "az", "ax", None), P(), P()),
        check_vma=False,
    )
```

```python
import jax
import jax.numpy as jnp
from jax import lax
from jax.sharding import PartitionSpec as P

step_dt = 0.25
epsilon = 1e-06


def with_halo(array, axis, dim, before, after, wrap):
    size, length = (lax.axis_size(axis), array.shape[dim])
    up = [(i, (i + 1) % size) for i in range(size if wrap else size - 1)]
    down = [(j, i) for i, j in up]
    parts = []
    if before:
        parts.append(lax.ppermute(lax.slice_in_dim(array, length - before, length, axis=dim), axis, up))
    parts.append(array)
    if after:
        parts.append(lax.ppermute(lax.slice_in_dim(array, 0, after, axis=dim), axis, down))
    return jnp.concatenate(parts, axis=dim)


def exchange(array, before, after, ax_before=None, ax_after=None):
    ax_before = before if ax_before is None else ax_before
    ax_after = after if ax_after is None else ax_after
    widened = with_halo(array, "ax", 2, ax_before, ax_after, False)
    return with_halo(widened, "az", 1, before, after, True)


def win(values, origin, da, dx, na, nx):
    a0, x0 = origin[0] + da, origin[1] + dx
    return values[a0 : a0 + na, x0 : x0 + nx]


def rad_next(values):
    return jnp.concatenate([values[..., 1:], jnp.zeros_like(values[..., :1])], axis=-1)


def rad_prev(values):
    return jnp.concatenate([jnp.zeros_like(values[..., :1]), values[..., :-1]], axis=-1)


def casing_mask(shape):
    return lax.broadcasted_iota(jnp.int32, shape, len(shape) - 1) == shape[-1] - 1


def advect_back(carried_ax, carried_az, na, nx):
    return 0.5 * (carried_ax[..., 1 : 1 + na, 0:nx] - carried_ax[..., 1 : 1 + na, 2 : 2 + nx]) + 0.5 * (
        carried_az[..., 0:na, 1 : 1 + nx] - carried_az[..., 2 : 2 + na, 1 : 1 + nx]
    )


def advect_back4(carried_ax, carried_az, na, nx):
    return 0.5 * (carried_ax[:, 1 : 1 + na, 0:nx, :] - carried_ax[:, 1 : 1 + na, 2 : 2 + nx, :]) + 0.5 * (
        carried_az[:, 0:na, 1 : 1 + nx, :] - carried_az[:, 2 : 2 + na, 1 : 1 + nx, :]
    )


def butterfly_sum(values, axes):
    for axis in axes:
        size = lax.axis_size(axis)
        if size & (size - 1):
            values = lax.psum(values, axis)
            continue
        step = 1
        while step < size:
            values = values + lax.ppermute(values, axis, [(i, i ^ step) for i in range(size)])
            step *= 2
    return values


def shards(
    acoustic,
    mean_flow,
    adjoint_in,
    admittance,
    segment_id,
    noise_code,
    noise_table,
    mic_az,
    mic_ax,
    measured,
):
    na, nx, nr = (acoustic.shape[1], acoustic.shape[2], acoustic.shape[3])
    nseg = admittance.shape[0]
    buoyancy = 1.0 / mean_flow[2]
    stiffness = mean_flow[2] * mean_flow[3] * mean_flow[3]
    axial_flow, swirl_flow = (mean_flow[0], mean_flow[1])

    segment_hot = segment_id[:, :, None] == lax.broadcasted_iota(jnp.int32, (1, 1, nseg), 2)
    wall = jnp.sum(jnp.where(segment_hot, admittance, 0.0), axis=2)
    noise_hot = noise_code[:, :, None] == lax.broadcasted_iota(jnp.int32, (1, 1, noise_table.shape[0]), 2)
    top_profile = (nr - 1 + 0.5) / nr
    source_top = jnp.sum(jnp.where(noise_hot, noise_table, 0.0), axis=2) * top_profile

    a0 = adjoint_in[0]
    push = -step_dt * stiffness * a0
    stack_f = jnp.stack([a0, adjoint_in[1], adjoint_in[2], adjoint_in[3], axial_flow, swirl_flow, buoyancy, push])
    top, below = nr - 1, nr - 2
    planes = [
        acoustic[0, :, :, top],
        acoustic[0, :, :, below],
        acoustic[1, :, :, top],
        acoustic[2, :, :, top],
        acoustic[3, :, :, below],
        axial_flow[:, :, top],
        axial_flow[:, :, below],
        swirl_flow[:, :, top],
        swirl_flow[:, :, below],
        buoyancy[:, :, top],
        buoyancy[:, :, below],
        stiffness[:, :, top],
        wall,
        source_top,
    ]
    stack_c = jnp.stack(planes)
    n_planes = len(planes)
    tile = 8
    reach = 3
    n_f = stack_f.shape[0]
    row_slot = tile * nr

    def to_slot(block):
        per_row = jnp.transpose(block, (1, 0, 2)).reshape(block.shape[1], -1)
        return jnp.pad(per_row, ((0, 0), (0, row_slot - per_row.shape[1]))).reshape(block.shape[1], tile, nr)

    def from_slot(slot_rows):
        flat = slot_rows.reshape(slot_rows.shape[0], -1)[:, : n_planes * nx]
        return jnp.transpose(flat.reshape(slot_rows.shape[0], n_planes, nx), (1, 0, 2))

    casing_slot = to_slot(stack_c)[None]
    size_ax = lax.axis_size("ax")
    right = [(i, i + 1) for i in range(size_ax - 1)]
    left = [(j, i) for i, j in right]
    from_left = lax.ppermute(jnp.concatenate([stack_f[:, :, nx - tile :], casing_slot]), "ax", right)
    from_right = lax.ppermute(jnp.concatenate([stack_f[:, :, :tile], casing_slot]), "ax", left)
    widened = jnp.concatenate([from_left[:n_f], stack_f, from_right[:n_f]], axis=2)
    wide_x_c = jnp.concatenate(
        [from_slot(from_left[n_f])[:, :, nx - reach :], stack_c, from_slot(from_right[n_f])[:, :, :reach]], axis=2
    )
    size_az, length_a = (lax.axis_size("az"), widened.shape[1])
    up = [(i, (i + 1) % size_az) for i in range(size_az)]
    down = [(j, i) for i, j in up]
    slot = widened.shape[2] * widened.shape[3]

    def as_slots(rows):
        flat = rows.reshape(-1)
        count = -(-flat.shape[0] // slot)
        return jnp.pad(flat, (0, count * slot - flat.shape[0])).reshape((count,) + widened.shape[2:])

    def from_slots(slots):
        return slots.reshape(-1)[: n_planes * reach * (nx + 2 * reach)].reshape(n_planes, reach, nx + 2 * reach)

    sent_up = jnp.concatenate(
        [jnp.stack([widened[f, length_a - 1] for f in (0, 1, 2, 3, 5, 6, 7)]), as_slots(wide_x_c[:, length_a - reach :])]
    )
    sent_down = jnp.concatenate(
        [jnp.stack([widened[f, 0] for f in (0, 1, 2, 3, 5, 7)] + [widened[7, 1]]), as_slots(wide_x_c[:, :reach])]
    )
    from_below = lax.ppermute(sent_up, "az", up)
    from_above = lax.ppermute(sent_down, "az", down)
    blank = jnp.zeros_like(from_below[0])
    row_before = jnp.stack([from_below[i] for i in (0, 1, 2, 3)] + [blank] + [from_below[i] for i in (4, 5, 6)])
    row_after = jnp.stack([from_above[i] for i in (0, 1, 2, 3)] + [blank, from_above[4], blank, from_above[5]])
    row_after2 = jnp.stack([blank] * 7 + [from_above[6]])
    wide_f = jnp.concatenate(
        [row_before[:, None], widened[:n_f], row_after[:, None], row_after2[:, None]], axis=1
    )
    wide_c = jnp.concatenate([from_slots(from_below[7:]), wide_x_c, from_slots(from_above[7:])], axis=1)

    oc = (reach, reach)
    p_t, p_b, va_t, vx_t, vr_b, u_t, u_b, w_t, w_b, b_t, b_b, s_t, wall_c, src_c = [wide_c[i] for i in range(14)]
    ea, ex = na + 3, nx + 3

    def c(f, da, dx, la, lx):
        return win(f, oc, da, dx, la, lx)

    def advect_c(f, u, w, da, dx, la, lx):
        return c(u, da, dx, la, lx) * (c(f, da, dx + 1, la, lx) - c(f, da, dx - 1, la, lx)) * 0.5 + c(
            w, da, dx, la, lx
        ) * (c(f, da + 1, dx, la, lx) - c(f, da - 1, dx, la, lx)) * 0.5

    new_az = c(va_t, -2, -1, ea + 1, ex) - step_dt * (
        advect_c(va_t, u_t, w_t, -2, -1, ea + 1, ex)
        + c(b_t, -2, -1, ea + 1, ex) * (c(p_t, -1, -1, ea + 1, ex) - c(p_t, -2, -1, ea + 1, ex))
    )
    new_ax = c(vx_t, -1, -2, ea, ex + 1) - step_dt * (
        advect_c(vx_t, u_t, w_t, -1, -2, ea, ex + 1)
        + c(b_t, -1, -2, ea, ex + 1) * (c(p_t, -1, -1, ea, ex + 1) - c(p_t, -1, -2, ea, ex + 1))
    )
    rad_top = c(wall_c, -1, -1, ea, ex) * c(p_t, -1, -1, ea, ex)
    rad_below = c(vr_b, -1, -1, ea, ex) - step_dt * (
        advect_c(vr_b, u_b, w_b, -1, -1, ea, ex)
        + c(b_b, -1, -1, ea, ex) * (c(p_t, -1, -1, ea, ex) - c(p_b, -1, -1, ea, ex))
    )
    spread = (new_az[1:] - new_az[:-1]) + (new_ax[:, 1:] - new_ax[:, :-1]) + (rad_top - rad_below)
    press_ring = (
        c(p_t, -1, -1, ea, ex)
        - step_dt * (advect_c(p_t, u_t, w_t, -1, -1, ea, ex) + c(s_t, -1, -1, ea, ex) * spread)
        + step_dt * c(src_c, -1, -1, ea, ex)
    )

    total_az = na * lax.axis_size("az")
    first_az = lax.axis_index("az") * na
    first_ax = lax.axis_index("ax") * nx
    ring_az = jnp.remainder(mic_az - first_az + 1, total_az)
    ring_ax = mic_ax - first_ax + 1
    on_ring = (ring_az < ea) & (ring_ax >= 0) & (ring_ax < ex)
    owned = (ring_az >= 1) & (ring_az <= na) & (ring_ax >= 1) & (ring_ax <= nx)
    ring_cell = jnp.where(on_ring, ring_az * ex + ring_ax, -1)
    cell_hot = ring_cell[:, None] == lax.broadcasted_iota(jnp.int32, (1, ea * ex), 1)
    heard = jnp.sum(jnp.where(cell_hot, press_ring.reshape(1, ea * ex), 0.0), axis=1)
    misses = heard - measured
    square_sum = jnp.sum(jnp.where(owned, misses * misses, 0.0))
    placed = jnp.sum(jnp.where(cell_hot, misses[:, None], 0.0), axis=0).reshape(ea, ex)

    push_e = -step_dt * c(s_t, -1, -1, ea, ex) * placed
    r1a, r1x = na + 2, nx + 2
    head_az_e = push_e[:r1a, :r1x] - push_e[1 : 1 + r1a, :r1x]
    head_ax_e = push_e[:r1a, :r1x] - push_e[:r1a, 1 : 1 + r1x]
    head_rad_e = -push_e[:r1a, :r1x]
    u_t1, w_t1 = c(u_t, -1, -1, r1a, r1x), c(w_t, -1, -1, r1a, r1x)
    u_b1, w_b1 = c(u_b, -1, -1, r1a, r1x), c(w_b, -1, -1, r1a, r1x)
    b_t1 = c(b_t, -1, -1, r1a, r1x)
    own_e = (slice(1, 1 + na), slice(1, 1 + nx))
    back_press_t = (
        placed[1 : 1 + na, 1 : 1 + nx]
        - step_dt * advect_back(u_t1 * placed[:r1a, :r1x], w_t1 * placed[:r1a, :r1x], na, nx)
    )
    shove_az = step_dt * b_t1 * head_az_e
    shove_ax = step_dt * b_t1 * head_ax_e
    b_b0, wall_0, push_0 = c(b_b, 0, 0, na, nx), c(wall_c, 0, 0, na, nx), push_e[own_e]
    back_press_t = (
        back_press_t
        + (shove_az[own_e] - shove_az[0:na, 1 : 1 + nx])
        + (shove_ax[own_e] - shove_ax[1 : 1 + na, 0:nx])
        + step_dt * b_b0 * push_0
        + wall_0 * push_0
    )
    back_press_b = -step_dt * b_b0 * push_0
    back_az_t = head_az_e[own_e] - step_dt * advect_back(u_t1 * head_az_e, w_t1 * head_az_e, na, nx)
    back_ax_t = head_ax_e[own_e] - step_dt * advect_back(u_t1 * head_ax_e, w_t1 * head_ax_e, na, nx)
    back_rad_b = head_rad_e[own_e] - step_dt * advect_back(u_b1 * head_rad_e, w_b1 * head_rad_e, na, nx)
    zero = jnp.zeros_like(back_press_b)
    extra = jnp.stack(
        [
            jnp.stack([back_press_b, back_press_t], axis=-1),
            jnp.stack([zero, back_az_t], axis=-1),
            jnp.stack([zero, back_ax_t], axis=-1),
            jnp.stack([back_rad_b, zero], axis=-1),
        ]
    )

    of = (1, tile)
    g_a0, g_a1, g_a2, g_a3, g_u, g_w, g_b, g_push = [wide_f[i] for i in range(8)]

    def at(field, da, dx):
        return win(field, of, da, dx, na, nx)

    def head_az(da, dx):
        return at(g_a1, da, dx) + at(g_push, da, dx) - at(g_push, da + 1, dx)

    def head_ax(da, dx):
        return at(g_a2, da, dx) + at(g_push, da, dx) - at(g_push, da, dx + 1)

    casing = casing_mask((na, nx, nr))

    def head_rad(da, dx):
        push_here = at(g_push, da, dx)
        return at(g_a3, da, dx) + push_here - rad_next(push_here)

    def head_masked(da, dx):
        return jnp.where(casing, 0.0, head_rad(da, dx))

    def back_advect(head):
        return 0.5 * (at(g_u, 0, -1) * head(0, -1) - at(g_u, 0, 1) * head(0, 1)) + 0.5 * (
            at(g_w, -1, 0) * head(-1, 0) - at(g_w, 1, 0) * head(1, 0)
        )

    def seed(da, dx):
        return at(g_a0, da, dx)

    backs = [head(0, 0) - step_dt * back_advect(head) for head in (head_az, head_ax, head_masked)]
    shove_r = step_dt * at(g_b, 0, 0) * head_masked(0, 0)
    head_rad_own = head_rad(0, 0)
    back_press = (
        seed(0, 0)
        - step_dt * back_advect(seed)
        + (step_dt * at(g_b, 0, 0) * head_az(0, 0) - step_dt * at(g_b, -1, 0) * head_az(-1, 0))
        + (step_dt * at(g_b, 0, 0) * head_ax(0, 0) - step_dt * at(g_b, 0, -1) * head_ax(0, -1))
        + (shove_r - rad_prev(shove_r))
        + jnp.where(casing, wall[:, :, None] * head_rad_own, 0.0)
    )
    base = jnp.stack([back_press] + backs)

    press_top = acoustic[0, :, :, top]
    sens_base = press_top * (adjoint_in[3, :, :, top] + push[:, :, top])
    sens_placed = press_top * push_0
    seg_base = jnp.sum(jnp.where(segment_hot, sens_base[:, :, None], 0.0), axis=(0, 1))
    seg_placed = jnp.sum(jnp.where(segment_hot, sens_placed[:, :, None], 0.0), axis=(0, 1))

    totals = butterfly_sum(jnp.concatenate([square_sum[None], seg_base, seg_placed]), ("az", "ax"))
    mean_sq = totals[0] / mic_az.shape[0] + epsilon
    grad_scale = (na * lax.axis_size("az") * nx * lax.axis_size("ax") / nseg) ** (-0.5)
    liner_grad = (totals[1 : 1 + nseg] + totals[1 + nseg :] / mean_sq) * grad_scale
    misfit = 0.5 * jnp.log(mean_sq)
    lane = lax.broadcasted_iota(jnp.int32, (1, 1, 1, nr), 3)
    extra_scaled = extra / mean_sq
    correction = jnp.where(
        lane == nr - 1,
        extra_scaled[..., 1:2],
        jnp.where(lane == nr - 2, extra_scaled[..., 0:1], 0.0),
    )
    adjoint_out = base + correction
    return (adjoint_out, liner_grad, misfit)


def solution(mesh):
    placed = (
        P(None, "az", "ax", None),
        P(None, "az", "ax", None),
        P(None, "az", "ax", None),
        P(),
        P("az", "ax"),
        P("az", "ax"),
        P(),
        P(),
        P(),
        P(),
    )
    return jax.shard_map(
        shards,
        mesh=mesh,
        in_specs=placed,
        out_specs=(P(None, "az", "ax", None), P(), P()),
        check_vma=False,
    )
```

```python
import jax
import jax.numpy as jnp
from jax import lax
from jax.sharding import PartitionSpec as P

step_dt = 0.25
epsilon = 1e-06
highest = lax.Precision.HIGHEST


def with_halo(array, axis, dim, before, after, wrap):
    size, length = (lax.axis_size(axis), array.shape[dim])
    up = [(i, (i + 1) % size) for i in range(size if wrap else size - 1)]
    down = [(j, i) for i, j in up]
    parts = []
    if before:
        parts.append(lax.ppermute(lax.slice_in_dim(array, length - before, length, axis=dim), axis, up))
    parts.append(array)
    if after:
        parts.append(lax.ppermute(lax.slice_in_dim(array, 0, after, axis=dim), axis, down))
    return jnp.concatenate(parts, axis=dim)


def exchange(array, before, after, ax_before=None, ax_after=None):
    ax_before = before if ax_before is None else ax_before
    ax_after = after if ax_after is None else ax_after
    widened = with_halo(array, "ax", 2, ax_before, ax_after, False)
    return with_halo(widened, "az", 1, before, after, True)


def win(values, origin, da, dx, na, nx):
    a0, x0 = origin[0] + da, origin[1] + dx
    return values[a0 : a0 + na, x0 : x0 + nx]


def rad_next(values):
    return jnp.concatenate([values[..., 1:], jnp.zeros_like(values[..., :1])], axis=-1)


def rad_prev(values):
    return jnp.concatenate([jnp.zeros_like(values[..., :1]), values[..., :-1]], axis=-1)


def casing_mask(shape):
    return lax.broadcasted_iota(jnp.int32, shape, len(shape) - 1) == shape[-1] - 1


def advect_back(carried_ax, carried_az, na, nx):
    return 0.5 * (carried_ax[..., 1 : 1 + na, 0:nx] - carried_ax[..., 1 : 1 + na, 2 : 2 + nx]) + 0.5 * (
        carried_az[..., 0:na, 1 : 1 + nx] - carried_az[..., 2 : 2 + na, 1 : 1 + nx]
    )


def advect_back4(carried_ax, carried_az, na, nx):
    return 0.5 * (carried_ax[:, 1 : 1 + na, 0:nx, :] - carried_ax[:, 1 : 1 + na, 2 : 2 + nx, :]) + 0.5 * (
        carried_az[:, 0:na, 1 : 1 + nx, :] - carried_az[:, 2 : 2 + na, 1 : 1 + nx, :]
    )


def butterfly_sum(values, axes):
    for axis in axes:
        size = lax.axis_size(axis)
        if size & (size - 1):
            values = lax.psum(values, axis)
            continue
        step = 1
        while step < size:
            values = values + lax.ppermute(values, axis, [(i, i ^ step) for i in range(size)])
            step *= 2
    return values


def shards(
    acoustic,
    mean_flow,
    adjoint_in,
    admittance,
    segment_id,
    noise_code,
    noise_table,
    mic_az,
    mic_ax,
    measured,
):
    na, nx, nr = (acoustic.shape[1], acoustic.shape[2], acoustic.shape[3])
    nseg = admittance.shape[0]
    buoyancy = 1.0 / mean_flow[2]
    stiffness = mean_flow[2] * mean_flow[3] * mean_flow[3]
    axial_flow, swirl_flow = (mean_flow[0], mean_flow[1])

    segment_hot = segment_id[:, :, None] == lax.broadcasted_iota(jnp.int32, (1, 1, nseg), 2)
    wall = jnp.sum(jnp.where(segment_hot, admittance, 0.0), axis=2)
    noise_hot = noise_code[:, :, None] == lax.broadcasted_iota(jnp.int32, (1, 1, noise_table.shape[0]), 2)
    top_profile = (nr - 1 + 0.5) / nr
    source_top = jnp.sum(jnp.where(noise_hot, noise_table, 0.0), axis=2) * top_profile

    a0 = adjoint_in[0]
    push = -step_dt * stiffness * a0
    stack_f = jnp.stack([a0, adjoint_in[1], adjoint_in[2], adjoint_in[3], axial_flow, swirl_flow, buoyancy, push])
    top, below = nr - 1, nr - 2
    taken = [(0, top), (0, below), (1, top), (2, top), (3, below)]
    taken_coef = [(0, top), (0, below), (1, top), (1, below), (2, top), (2, below), (3, top)]
    n_planes = len(taken) + len(taken_coef) + 2
    lane_in = lax.broadcasted_iota(jnp.int32, (nr, nr), 0)
    lane_out = lax.broadcasted_iota(jnp.int32, (nr, nr), 1)

    def chooser(picks, first):
        return jnp.stack(
            [
                sum(
                    ((lane_in == r) & (lane_out == first + k)).astype(jnp.float32)
                    for k, (f, r) in enumerate(picks)
                    if f == field
                )
                + jnp.zeros((nr, nr), jnp.float32)
                for field in range(4)
            ]
        )

    coefficients = jnp.stack([axial_flow, swirl_flow, buoyancy, stiffness])
    packed = jnp.einsum("faxr,frk->axk", acoustic, chooser(taken, 0), precision=highest) + jnp.einsum(
        "faxr,frk->axk", coefficients, chooser(taken_coef, len(taken)), precision=highest
    )
    hot_both = jnp.concatenate([segment_hot, noise_hot], axis=2).astype(jnp.float32)
    n_tab = noise_table.shape[0]
    wall_lane, source_lane = (n_planes - 2, n_planes - 1)
    row = lax.broadcasted_iota(jnp.int32, (nseg + n_tab, nr), 0)
    col = lax.broadcasted_iota(jnp.int32, (nseg + n_tab, nr), 1)
    table_both = jnp.concatenate([admittance, noise_table * top_profile])
    spread_table = jnp.where(
        ((row < nseg) & (col == wall_lane)) | ((row >= nseg) & (col == source_lane)), table_both[:, None], 0.0
    )
    packed = packed + jnp.einsum("axs,sk->axk", hot_both, spread_table, precision=highest)
    tile = 8
    reach = 3
    stack_all = jnp.concatenate([stack_f, packed[None]], axis=0)
    n_f = stack_f.shape[0]
    widened = with_halo(stack_all, "ax", 2, tile, tile, False)
    size_az, length_a = (lax.axis_size("az"), widened.shape[1])
    up = [(i, (i + 1) % size_az) for i in range(size_az)]
    down = [(j, i) for i, j in up]
    sent_up = jnp.stack(
        [widened[f, length_a - 1] for f in (0, 1, 2, 3, 5, 6, 7)]
        + [widened[n_f, length_a - reach + k] for k in range(reach)]
    )
    sent_down = jnp.stack(
        [widened[f, 0] for f in (0, 1, 2, 3, 5, 7)] + [widened[7, 1]] + [widened[n_f, k] for k in range(reach)]
    )
    from_below = lax.ppermute(sent_up, "az", up)
    from_above = lax.ppermute(sent_down, "az", down)
    blank = jnp.zeros_like(from_below[0])
    row_before = jnp.stack([from_below[i] for i in (0, 1, 2, 3)] + [blank] + [from_below[i] for i in (4, 5, 6)])
    row_after = jnp.stack([from_above[i] for i in (0, 1, 2, 3)] + [blank, from_above[4], blank, from_above[5]])
    row_after2 = jnp.stack([blank] * 7 + [from_above[6]])
    wide_f = jnp.concatenate(
        [row_before[:, None], widened[:n_f], row_after[:, None], row_after2[:, None]], axis=1
    )
    wide_packed = jnp.concatenate([from_below[7:], widened[n_f], from_above[7:]], axis=0)
    wide_c = jnp.transpose(wide_packed[:, :, :n_planes], (2, 0, 1))

    oc = (reach, tile)
    p_t, p_b, va_t, vx_t, vr_b, u_t, u_b, w_t, w_b, b_t, b_b, s_t, wall_c, src_c = [wide_c[i] for i in range(14)]
    ea, ex = na + 3, nx + 3

    def c(f, da, dx, la, lx):
        return win(f, oc, da, dx, la, lx)

    def advect_c(f, u, w, da, dx, la, lx):
        return c(u, da, dx, la, lx) * (c(f, da, dx + 1, la, lx) - c(f, da, dx - 1, la, lx)) * 0.5 + c(
            w, da, dx, la, lx
        ) * (c(f, da + 1, dx, la, lx) - c(f, da - 1, dx, la, lx)) * 0.5

    new_az = c(va_t, -2, -1, ea + 1, ex) - step_dt * (
        advect_c(va_t, u_t, w_t, -2, -1, ea + 1, ex)
        + c(b_t, -2, -1, ea + 1, ex) * (c(p_t, -1, -1, ea + 1, ex) - c(p_t, -2, -1, ea + 1, ex))
    )
    new_ax = c(vx_t, -1, -2, ea, ex + 1) - step_dt * (
        advect_c(vx_t, u_t, w_t, -1, -2, ea, ex + 1)
        + c(b_t, -1, -2, ea, ex + 1) * (c(p_t, -1, -1, ea, ex + 1) - c(p_t, -1, -2, ea, ex + 1))
    )
    rad_top = c(wall_c, -1, -1, ea, ex) * c(p_t, -1, -1, ea, ex)
    rad_below = c(vr_b, -1, -1, ea, ex) - step_dt * (
        advect_c(vr_b, u_b, w_b, -1, -1, ea, ex)
        + c(b_b, -1, -1, ea, ex) * (c(p_t, -1, -1, ea, ex) - c(p_b, -1, -1, ea, ex))
    )
    spread = (new_az[1:] - new_az[:-1]) + (new_ax[:, 1:] - new_ax[:, :-1]) + (rad_top - rad_below)
    press_ring = (
        c(p_t, -1, -1, ea, ex)
        - step_dt * (advect_c(p_t, u_t, w_t, -1, -1, ea, ex) + c(s_t, -1, -1, ea, ex) * spread)
        + step_dt * c(src_c, -1, -1, ea, ex)
    )

    total_az = na * lax.axis_size("az")
    first_az = lax.axis_index("az") * na
    first_ax = lax.axis_index("ax") * nx
    ring_az = jnp.remainder(mic_az - first_az + 1, total_az)
    ring_ax = mic_ax - first_ax + 1
    on_ring = (ring_az < ea) & (ring_ax >= 0) & (ring_ax < ex)
    owned = (ring_az >= 1) & (ring_az <= na) & (ring_ax >= 1) & (ring_ax <= nx)
    ring_cell = jnp.where(on_ring, ring_az * ex + ring_ax, -1)
    cell_hot = ring_cell[:, None] == lax.broadcasted_iota(jnp.int32, (1, ea * ex), 1)
    heard = jnp.sum(jnp.where(cell_hot, press_ring.reshape(1, ea * ex), 0.0), axis=1)
    misses = heard - measured
    square_sum = jnp.sum(jnp.where(owned, misses * misses, 0.0))
    placed = jnp.sum(jnp.where(cell_hot, misses[:, None], 0.0), axis=0).reshape(ea, ex)

    push_e = -step_dt * c(s_t, -1, -1, ea, ex) * placed
    r1a, r1x = na + 2, nx + 2
    head_az_e = push_e[:r1a, :r1x] - push_e[1 : 1 + r1a, :r1x]
    head_ax_e = push_e[:r1a, :r1x] - push_e[:r1a, 1 : 1 + r1x]
    head_rad_e = -push_e[:r1a, :r1x]
    u_t1, w_t1 = c(u_t, -1, -1, r1a, r1x), c(w_t, -1, -1, r1a, r1x)
    u_b1, w_b1 = c(u_b, -1, -1, r1a, r1x), c(w_b, -1, -1, r1a, r1x)
    b_t1 = c(b_t, -1, -1, r1a, r1x)
    own_e = (slice(1, 1 + na), slice(1, 1 + nx))
    back_press_t = (
        placed[1 : 1 + na, 1 : 1 + nx]
        - step_dt * advect_back(u_t1 * placed[:r1a, :r1x], w_t1 * placed[:r1a, :r1x], na, nx)
    )
    shove_az = step_dt * b_t1 * head_az_e
    shove_ax = step_dt * b_t1 * head_ax_e
    b_b0, wall_0, push_0 = c(b_b, 0, 0, na, nx), c(wall_c, 0, 0, na, nx), push_e[own_e]
    back_press_t = (
        back_press_t
        + (shove_az[own_e] - shove_az[0:na, 1 : 1 + nx])
        + (shove_ax[own_e] - shove_ax[1 : 1 + na, 0:nx])
        + step_dt * b_b0 * push_0
        + wall_0 * push_0
    )
    back_press_b = -step_dt * b_b0 * push_0
    back_az_t = head_az_e[own_e] - step_dt * advect_back(u_t1 * head_az_e, w_t1 * head_az_e, na, nx)
    back_ax_t = head_ax_e[own_e] - step_dt * advect_back(u_t1 * head_ax_e, w_t1 * head_ax_e, na, nx)
    back_rad_b = head_rad_e[own_e] - step_dt * advect_back(u_b1 * head_rad_e, w_b1 * head_rad_e, na, nx)
    zero = jnp.zeros_like(back_press_b)
    extra = jnp.stack(
        [
            jnp.stack([back_press_b, back_press_t], axis=-1),
            jnp.stack([zero, back_az_t], axis=-1),
            jnp.stack([zero, back_ax_t], axis=-1),
            jnp.stack([back_rad_b, zero], axis=-1),
        ]
    )

    of = (1, tile)
    g_a0, g_a1, g_a2, g_a3, g_u, g_w, g_b, g_push = [wide_f[i] for i in range(8)]

    def at(field, da, dx):
        return win(field, of, da, dx, na, nx)

    def head_az(da, dx):
        return at(g_a1, da, dx) + at(g_push, da, dx) - at(g_push, da + 1, dx)

    def head_ax(da, dx):
        return at(g_a2, da, dx) + at(g_push, da, dx) - at(g_push, da, dx + 1)

    casing = casing_mask((na, nx, nr))

    def head_rad(da, dx):
        push_here = at(g_push, da, dx)
        return at(g_a3, da, dx) + push_here - rad_next(push_here)

    def head_masked(da, dx):
        return jnp.where(casing, 0.0, head_rad(da, dx))

    def back_advect(head):
        return 0.5 * (at(g_u, 0, -1) * head(0, -1) - at(g_u, 0, 1) * head(0, 1)) + 0.5 * (
            at(g_w, -1, 0) * head(-1, 0) - at(g_w, 1, 0) * head(1, 0)
        )

    def seed(da, dx):
        return at(g_a0, da, dx)

    backs = [head(0, 0) - step_dt * back_advect(head) for head in (head_az, head_ax, head_masked)]
    shove_r = step_dt * at(g_b, 0, 0) * head_masked(0, 0)
    head_rad_own = head_rad(0, 0)
    back_press = (
        seed(0, 0)
        - step_dt * back_advect(seed)
        + (step_dt * at(g_b, 0, 0) * head_az(0, 0) - step_dt * at(g_b, -1, 0) * head_az(-1, 0))
        + (step_dt * at(g_b, 0, 0) * head_ax(0, 0) - step_dt * at(g_b, 0, -1) * head_ax(0, -1))
        + (shove_r - rad_prev(shove_r))
        + jnp.where(casing, wall[:, :, None] * head_rad_own, 0.0)
    )
    base = jnp.stack([back_press] + backs)

    press_top = acoustic[0, :, :, top]
    sens_base = press_top * (adjoint_in[3, :, :, top] + push[:, :, top])
    sens_placed = press_top * push_0
    seg_base = jnp.sum(jnp.where(segment_hot, sens_base[:, :, None], 0.0), axis=(0, 1))
    seg_placed = jnp.sum(jnp.where(segment_hot, sens_placed[:, :, None], 0.0), axis=(0, 1))

    totals = butterfly_sum(jnp.concatenate([square_sum[None], seg_base, seg_placed]), ("az", "ax"))
    mean_sq = totals[0] / mic_az.shape[0] + epsilon
    grad_scale = (na * lax.axis_size("az") * nx * lax.axis_size("ax") / nseg) ** (-0.5)
    liner_grad = (totals[1 : 1 + nseg] + totals[1 + nseg :] / mean_sq) * grad_scale
    misfit = 0.5 * jnp.log(mean_sq)
    lane = lax.broadcasted_iota(jnp.int32, (1, 1, 1, nr), 3)
    extra_scaled = extra / mean_sq
    correction = jnp.where(
        lane == nr - 1,
        extra_scaled[..., 1:2],
        jnp.where(lane == nr - 2, extra_scaled[..., 0:1], 0.0),
    )
    adjoint_out = base + correction
    return (adjoint_out, liner_grad, misfit)


def solution(mesh):
    placed = (
        P(None, "az", "ax", None),
        P(None, "az", "ax", None),
        P(None, "az", "ax", None),
        P(),
        P("az", "ax"),
        P("az", "ax"),
        P(),
        P(),
        P(),
        P(),
    )
    return jax.shard_map(
        shards,
        mesh=mesh,
        in_specs=placed,
        out_specs=(P(None, "az", "ax", None), P(), P()),
        check_vma=False,
    )
```

```python
import jax
import jax.numpy as jnp
from jax import lax
from jax.sharding import PartitionSpec as P

step_dt = 0.25
epsilon = 1e-06


def with_halo(array, axis, dim, before, after, wrap):
    size, length = (lax.axis_size(axis), array.shape[dim])
    up = [(i, (i + 1) % size) for i in range(size if wrap else size - 1)]
    down = [(j, i) for i, j in up]
    parts = []
    if before:
        parts.append(lax.ppermute(lax.slice_in_dim(array, length - before, length, axis=dim), axis, up))
    parts.append(array)
    if after:
        parts.append(lax.ppermute(lax.slice_in_dim(array, 0, after, axis=dim), axis, down))
    return jnp.concatenate(parts, axis=dim)


def exchange(array, before, after, ax_before=None, ax_after=None):
    ax_before = before if ax_before is None else ax_before
    ax_after = after if ax_after is None else ax_after
    widened = with_halo(array, "ax", 2, ax_before, ax_after, False)
    return with_halo(widened, "az", 1, before, after, True)


def win(values, origin, da, dx, na, nx):
    a0, x0 = origin[0] + da, origin[1] + dx
    return values[a0 : a0 + na, x0 : x0 + nx]


def rad_next(values):
    return jnp.concatenate([values[..., 1:], jnp.zeros_like(values[..., :1])], axis=-1)


def rad_prev(values):
    return jnp.concatenate([jnp.zeros_like(values[..., :1]), values[..., :-1]], axis=-1)


def casing_mask(shape):
    return lax.broadcasted_iota(jnp.int32, shape, len(shape) - 1) == shape[-1] - 1


def advect_back(carried_ax, carried_az, na, nx):
    return 0.5 * (carried_ax[..., 1 : 1 + na, 0:nx] - carried_ax[..., 1 : 1 + na, 2 : 2 + nx]) + 0.5 * (
        carried_az[..., 0:na, 1 : 1 + nx] - carried_az[..., 2 : 2 + na, 1 : 1 + nx]
    )


def advect_back4(carried_ax, carried_az, na, nx):
    return 0.5 * (carried_ax[:, 1 : 1 + na, 0:nx, :] - carried_ax[:, 1 : 1 + na, 2 : 2 + nx, :]) + 0.5 * (
        carried_az[:, 0:na, 1 : 1 + nx, :] - carried_az[:, 2 : 2 + na, 1 : 1 + nx, :]
    )


def butterfly_sum(values, axes):
    for axis in axes:
        size = lax.axis_size(axis)
        if size & (size - 1):
            values = lax.psum(values, axis)
            continue
        step = 1
        while step < size:
            values = values + lax.ppermute(values, axis, [(i, i ^ step) for i in range(size)])
            step *= 2
    return values


def shards(
    acoustic,
    mean_flow,
    adjoint_in,
    admittance,
    segment_id,
    noise_code,
    noise_table,
    mic_az,
    mic_ax,
    measured,
):
    na, nx, nr = (acoustic.shape[1], acoustic.shape[2], acoustic.shape[3])
    nseg = admittance.shape[0]
    buoyancy = 1.0 / mean_flow[2]
    stiffness = mean_flow[2] * mean_flow[3] * mean_flow[3]
    axial_flow, swirl_flow = (mean_flow[0], mean_flow[1])

    segment_hot = segment_id[:, :, None] == lax.broadcasted_iota(jnp.int32, (1, 1, nseg), 2)
    wall = jnp.sum(jnp.where(segment_hot, admittance, 0.0), axis=2)
    noise_hot = noise_code[:, :, None] == lax.broadcasted_iota(jnp.int32, (1, 1, noise_table.shape[0]), 2)
    top_profile = (nr - 1 + 0.5) / nr
    source_top = jnp.sum(jnp.where(noise_hot, noise_table, 0.0), axis=2) * top_profile

    a0 = adjoint_in[0]
    push = -step_dt * stiffness * a0
    stack_f = jnp.stack([a0, adjoint_in[1], adjoint_in[2], adjoint_in[3], axial_flow, swirl_flow, buoyancy, push])
    top, below = nr - 1, nr - 2
    planes = [
        acoustic[0, :, :, top],
        acoustic[0, :, :, below],
        acoustic[1, :, :, top],
        acoustic[2, :, :, top],
        acoustic[3, :, :, below],
        axial_flow[:, :, top],
        axial_flow[:, :, below],
        swirl_flow[:, :, top],
        swirl_flow[:, :, below],
        buoyancy[:, :, top],
        buoyancy[:, :, below],
        stiffness[:, :, top],
        wall,
        source_top,
    ]
    stack_c = jnp.stack(planes)
    n_planes = len(planes)
    tile = 8
    reach = 3
    packed = jnp.pad(jnp.transpose(stack_c, (1, 2, 0)), ((0, 0), (0, 0), (0, nr - n_planes)))
    stack_all = jnp.concatenate([stack_f, packed[None]], axis=0)
    n_f = stack_f.shape[0]
    sent_x = jnp.concatenate([stack_all[:5], stack_all[6:]], axis=0)
    size_ax = lax.axis_size("ax")
    right = [(i, i + 1) for i in range(size_ax - 1)]
    left = [(j, i) for i, j in right]
    length_x = stack_all.shape[2]
    x_before = lax.ppermute(sent_x[:, :, length_x - tile :], "ax", right)
    x_after = lax.ppermute(sent_x[:, :, :tile], "ax", left)
    no_w = jnp.zeros_like(x_before[:1])
    x_before = jnp.concatenate([x_before[:5], no_w, x_before[5:]], axis=0)
    x_after = jnp.concatenate([x_after[:5], no_w, x_after[5:]], axis=0)
    widened = jnp.concatenate([x_before, stack_all, x_after], axis=2)
    size_az, length_a = (lax.axis_size("az"), widened.shape[1])
    up = [(i, (i + 1) % size_az) for i in range(size_az)]
    down = [(j, i) for i, j in up]
    def casing_rows(rows):
        joined = jnp.concatenate([widened[n_f, r, :, :n_planes] for r in rows], axis=-1)
        return jnp.pad(joined, ((0, 0), (0, nr - joined.shape[-1])))

    sent_up = jnp.stack(
        [widened[f, length_a - 1] for f in (0, 1, 2, 3, 5, 6, 7)]
        + [casing_rows(range(length_a - reach, length_a))]
    )
    sent_down = jnp.stack(
        [widened[f, 0] for f in (0, 1, 2, 3, 5, 7)] + [widened[7, 1]] + [casing_rows(range(reach))]
    )
    from_below = lax.ppermute(sent_up, "az", up)
    from_above = lax.ppermute(sent_down, "az", down)
    blank = jnp.zeros_like(from_below[0])
    row_before = jnp.stack([from_below[i] for i in (0, 1, 2, 3)] + [blank] + [from_below[i] for i in (4, 5, 6)])
    row_after = jnp.stack([from_above[i] for i in (0, 1, 2, 3)] + [blank, from_above[4], blank, from_above[5]])
    row_after2 = jnp.stack([blank] * 7 + [from_above[6]])
    wide_f = jnp.concatenate(
        [row_before[:, None], widened[:n_f], row_after[:, None], row_after2[:, None]], axis=1
    )
    def casing_unpack(row):
        return jnp.stack([row[:, k * n_planes : (k + 1) * n_planes] for k in range(reach)])

    wide_packed = jnp.concatenate(
        [casing_unpack(from_below[7]), widened[n_f, :, :, :n_planes], casing_unpack(from_above[7])], axis=0
    )
    wide_c = jnp.transpose(wide_packed[:, :, :n_planes], (2, 0, 1))

    oc = (reach, tile)
    p_t, p_b, va_t, vx_t, vr_b, u_t, u_b, w_t, w_b, b_t, b_b, s_t, wall_c, src_c = [wide_c[i] for i in range(14)]
    ea, ex = na + 3, nx + 3

    def c(f, da, dx, la, lx):
        return win(f, oc, da, dx, la, lx)

    def advect_c(f, u, w, da, dx, la, lx):
        return c(u, da, dx, la, lx) * (c(f, da, dx + 1, la, lx) - c(f, da, dx - 1, la, lx)) * 0.5 + c(
            w, da, dx, la, lx
        ) * (c(f, da + 1, dx, la, lx) - c(f, da - 1, dx, la, lx)) * 0.5

    new_az = c(va_t, -2, -1, ea + 1, ex) - step_dt * (
        advect_c(va_t, u_t, w_t, -2, -1, ea + 1, ex)
        + c(b_t, -2, -1, ea + 1, ex) * (c(p_t, -1, -1, ea + 1, ex) - c(p_t, -2, -1, ea + 1, ex))
    )
    new_ax = c(vx_t, -1, -2, ea, ex + 1) - step_dt * (
        advect_c(vx_t, u_t, w_t, -1, -2, ea, ex + 1)
        + c(b_t, -1, -2, ea, ex + 1) * (c(p_t, -1, -1, ea, ex + 1) - c(p_t, -1, -2, ea, ex + 1))
    )
    rad_top = c(wall_c, -1, -1, ea, ex) * c(p_t, -1, -1, ea, ex)
    rad_below = c(vr_b, -1, -1, ea, ex) - step_dt * (
        advect_c(vr_b, u_b, w_b, -1, -1, ea, ex)
        + c(b_b, -1, -1, ea, ex) * (c(p_t, -1, -1, ea, ex) - c(p_b, -1, -1, ea, ex))
    )
    spread = (new_az[1:] - new_az[:-1]) + (new_ax[:, 1:] - new_ax[:, :-1]) + (rad_top - rad_below)
    press_ring = (
        c(p_t, -1, -1, ea, ex)
        - step_dt * (advect_c(p_t, u_t, w_t, -1, -1, ea, ex) + c(s_t, -1, -1, ea, ex) * spread)
        + step_dt * c(src_c, -1, -1, ea, ex)
    )

    total_az = na * lax.axis_size("az")
    first_az = lax.axis_index("az") * na
    first_ax = lax.axis_index("ax") * nx
    ring_az = jnp.remainder(mic_az - first_az + 1, total_az)
    ring_ax = mic_ax - first_ax + 1
    on_ring = (ring_az < ea) & (ring_ax >= 0) & (ring_ax < ex)
    owned = (ring_az >= 1) & (ring_az <= na) & (ring_ax >= 1) & (ring_ax <= nx)
    ring_cell = jnp.where(on_ring, ring_az * ex + ring_ax, -1)
    cell_hot = ring_cell[:, None] == lax.broadcasted_iota(jnp.int32, (1, ea * ex), 1)
    heard = jnp.sum(jnp.where(cell_hot, press_ring.reshape(1, ea * ex), 0.0), axis=1)
    misses = heard - measured
    square_sum = jnp.sum(jnp.where(owned, misses * misses, 0.0))
    placed = jnp.sum(jnp.where(cell_hot, misses[:, None], 0.0), axis=0).reshape(ea, ex)

    push_e = -step_dt * c(s_t, -1, -1, ea, ex) * placed
    r1a, r1x = na + 2, nx + 2
    head_az_e = push_e[:r1a, :r1x] - push_e[1 : 1 + r1a, :r1x]
    head_ax_e = push_e[:r1a, :r1x] - push_e[:r1a, 1 : 1 + r1x]
    head_rad_e = -push_e[:r1a, :r1x]
    u_t1, w_t1 = c(u_t, -1, -1, r1a, r1x), c(w_t, -1, -1, r1a, r1x)
    u_b1, w_b1 = c(u_b, -1, -1, r1a, r1x), c(w_b, -1, -1, r1a, r1x)
    b_t1 = c(b_t, -1, -1, r1a, r1x)
    own_e = (slice(1, 1 + na), slice(1, 1 + nx))
    back_press_t = (
        placed[1 : 1 + na, 1 : 1 + nx]
        - step_dt * advect_back(u_t1 * placed[:r1a, :r1x], w_t1 * placed[:r1a, :r1x], na, nx)
    )
    shove_az = step_dt * b_t1 * head_az_e
    shove_ax = step_dt * b_t1 * head_ax_e
    b_b0, wall_0, push_0 = c(b_b, 0, 0, na, nx), c(wall_c, 0, 0, na, nx), push_e[own_e]
    back_press_t = (
        back_press_t
        + (shove_az[own_e] - shove_az[0:na, 1 : 1 + nx])
        + (shove_ax[own_e] - shove_ax[1 : 1 + na, 0:nx])
        + step_dt * b_b0 * push_0
        + wall_0 * push_0
    )
    back_press_b = -step_dt * b_b0 * push_0
    back_az_t = head_az_e[own_e] - step_dt * advect_back(u_t1 * head_az_e, w_t1 * head_az_e, na, nx)
    back_ax_t = head_ax_e[own_e] - step_dt * advect_back(u_t1 * head_ax_e, w_t1 * head_ax_e, na, nx)
    back_rad_b = head_rad_e[own_e] - step_dt * advect_back(u_b1 * head_rad_e, w_b1 * head_rad_e, na, nx)
    zero = jnp.zeros_like(back_press_b)
    extra = jnp.stack(
        [
            jnp.stack([back_press_b, back_press_t], axis=-1),
            jnp.stack([zero, back_az_t], axis=-1),
            jnp.stack([zero, back_ax_t], axis=-1),
            jnp.stack([back_rad_b, zero], axis=-1),
        ]
    )

    of = (1, tile)
    g_a0, g_a1, g_a2, g_a3, g_u, g_w, g_b, g_push = [wide_f[i] for i in range(8)]

    def at(field, da, dx):
        return win(field, of, da, dx, na, nx)

    def head_az(da, dx):
        return at(g_a1, da, dx) + at(g_push, da, dx) - at(g_push, da + 1, dx)

    def head_ax(da, dx):
        return at(g_a2, da, dx) + at(g_push, da, dx) - at(g_push, da, dx + 1)

    casing = casing_mask((na, nx, nr))

    def head_rad(da, dx):
        push_here = at(g_push, da, dx)
        return at(g_a3, da, dx) + push_here - rad_next(push_here)

    def head_masked(da, dx):
        return jnp.where(casing, 0.0, head_rad(da, dx))

    def back_advect(head):
        return 0.5 * (at(g_u, 0, -1) * head(0, -1) - at(g_u, 0, 1) * head(0, 1)) + 0.5 * (
            at(g_w, -1, 0) * head(-1, 0) - at(g_w, 1, 0) * head(1, 0)
        )

    def seed(da, dx):
        return at(g_a0, da, dx)

    backs = [head(0, 0) - step_dt * back_advect(head) for head in (head_az, head_ax, head_masked)]
    shove_r = step_dt * at(g_b, 0, 0) * head_masked(0, 0)
    head_rad_own = head_rad(0, 0)
    back_press = (
        seed(0, 0)
        - step_dt * back_advect(seed)
        + (step_dt * at(g_b, 0, 0) * head_az(0, 0) - step_dt * at(g_b, -1, 0) * head_az(-1, 0))
        + (step_dt * at(g_b, 0, 0) * head_ax(0, 0) - step_dt * at(g_b, 0, -1) * head_ax(0, -1))
        + (shove_r - rad_prev(shove_r))
        + jnp.where(casing, wall[:, :, None] * head_rad_own, 0.0)
    )
    base = jnp.stack([back_press] + backs)

    press_top = acoustic[0, :, :, top]
    sens_base = press_top * (adjoint_in[3, :, :, top] + push[:, :, top])
    sens_placed = press_top * push_0
    seg_base = jnp.sum(jnp.where(segment_hot, sens_base[:, :, None], 0.0), axis=(0, 1))
    seg_placed = jnp.sum(jnp.where(segment_hot, sens_placed[:, :, None], 0.0), axis=(0, 1))

    totals = butterfly_sum(jnp.concatenate([square_sum[None], seg_base, seg_placed]), ("az", "ax"))
    mean_sq = totals[0] / mic_az.shape[0] + epsilon
    grad_scale = (na * lax.axis_size("az") * nx * lax.axis_size("ax") / nseg) ** (-0.5)
    liner_grad = (totals[1 : 1 + nseg] + totals[1 + nseg :] / mean_sq) * grad_scale
    misfit = 0.5 * jnp.log(mean_sq)
    lane = lax.broadcasted_iota(jnp.int32, (1, 1, 1, nr), 3)
    extra_scaled = extra / mean_sq
    correction = jnp.where(
        lane == nr - 1,
        extra_scaled[..., 1:2],
        jnp.where(lane == nr - 2, extra_scaled[..., 0:1], 0.0),
    )
    adjoint_out = base + correction
    return (adjoint_out, liner_grad, misfit)


def solution(mesh):
    placed = (
        P(None, "az", "ax", None),
        P(None, "az", "ax", None),
        P(None, "az", "ax", None),
        P(),
        P("az", "ax"),
        P("az", "ax"),
        P(),
        P(),
        P(),
        P(),
    )
    return jax.shard_map(
        shards,
        mesh=mesh,
        in_specs=placed,
        out_specs=(P(None, "az", "ax", None), P(), P()),
        check_vma=False,
    )
```

```python
import jax
import jax.numpy as jnp
from jax import lax
from jax.sharding import PartitionSpec as P

step_dt = 0.25
epsilon = 1e-06
highest = lax.Precision.HIGHEST


def with_halo(array, axis, dim, before, after, wrap):
    size, length = (lax.axis_size(axis), array.shape[dim])
    up = [(i, (i + 1) % size) for i in range(size if wrap else size - 1)]
    down = [(j, i) for i, j in up]
    parts = []
    if before:
        parts.append(lax.ppermute(lax.slice_in_dim(array, length - before, length, axis=dim), axis, up))
    parts.append(array)
    if after:
        parts.append(lax.ppermute(lax.slice_in_dim(array, 0, after, axis=dim), axis, down))
    return jnp.concatenate(parts, axis=dim)


def exchange(array, before, after, ax_before=None, ax_after=None):
    ax_before = before if ax_before is None else ax_before
    ax_after = after if ax_after is None else ax_after
    widened = with_halo(array, "ax", 2, ax_before, ax_after, False)
    return with_halo(widened, "az", 1, before, after, True)


def win(values, origin, da, dx, na, nx):
    a0, x0 = origin[0] + da, origin[1] + dx
    return values[a0 : a0 + na, x0 : x0 + nx]


def rad_next(values):
    return jnp.concatenate([values[..., 1:], jnp.zeros_like(values[..., :1])], axis=-1)


def rad_prev(values):
    return jnp.concatenate([jnp.zeros_like(values[..., :1]), values[..., :-1]], axis=-1)


def casing_mask(shape):
    return lax.broadcasted_iota(jnp.int32, shape, len(shape) - 1) == shape[-1] - 1


def advect_back(carried_ax, carried_az, na, nx):
    return 0.5 * (carried_ax[..., 1 : 1 + na, 0:nx] - carried_ax[..., 1 : 1 + na, 2 : 2 + nx]) + 0.5 * (
        carried_az[..., 0:na, 1 : 1 + nx] - carried_az[..., 2 : 2 + na, 1 : 1 + nx]
    )


def advect_back4(carried_ax, carried_az, na, nx):
    return 0.5 * (carried_ax[:, 1 : 1 + na, 0:nx, :] - carried_ax[:, 1 : 1 + na, 2 : 2 + nx, :]) + 0.5 * (
        carried_az[:, 0:na, 1 : 1 + nx, :] - carried_az[:, 2 : 2 + na, 1 : 1 + nx, :]
    )


def butterfly_sum(values, axes):
    for axis in axes:
        size = lax.axis_size(axis)
        if size & (size - 1):
            values = lax.psum(values, axis)
            continue
        step = 1
        while step < size:
            values = values + lax.ppermute(values, axis, [(i, i ^ step) for i in range(size)])
            step *= 2
    return values


def shards(
    acoustic,
    mean_flow,
    adjoint_in,
    admittance,
    segment_id,
    noise_code,
    noise_table,
    mic_az,
    mic_ax,
    measured,
):
    na, nx, nr = (acoustic.shape[1], acoustic.shape[2], acoustic.shape[3])
    nseg = admittance.shape[0]
    buoyancy = 1.0 / mean_flow[2]
    stiffness = mean_flow[2] * mean_flow[3] * mean_flow[3]
    axial_flow, swirl_flow = (mean_flow[0], mean_flow[1])

    segment_hot = segment_id[:, :, None] == lax.broadcasted_iota(jnp.int32, (1, 1, nseg), 2)
    wall = jnp.sum(jnp.where(segment_hot, admittance, 0.0), axis=2)
    noise_hot = noise_code[:, :, None] == lax.broadcasted_iota(jnp.int32, (1, 1, noise_table.shape[0]), 2)
    top_profile = (nr - 1 + 0.5) / nr
    source_top = jnp.sum(jnp.where(noise_hot, noise_table, 0.0), axis=2) * top_profile

    a0 = adjoint_in[0]
    push = -step_dt * stiffness * a0
    stack_f = jnp.stack([a0, adjoint_in[1], adjoint_in[2], adjoint_in[3], axial_flow, swirl_flow, buoyancy, push])
    top, below = nr - 1, nr - 2
    press_top = acoustic[0, :, :, top]
    planes = [
        press_top,
        acoustic[0, :, :, below],
        acoustic[1, :, :, top],
        acoustic[2, :, :, top],
        acoustic[3, :, :, below],
        axial_flow[:, :, top],
        axial_flow[:, :, below],
        swirl_flow[:, :, top],
        swirl_flow[:, :, below],
        buoyancy[:, :, top],
        buoyancy[:, :, below],
        stiffness[:, :, top],
        wall,
        source_top,
        press_top * (adjoint_in[3, :, :, top] + push[:, :, top]),
        segment_id.astype(jnp.float32),
    ]
    n_planes = len(planes)
    group = jnp.stack(planes)
    size_ax, me_ax = (lax.axis_size("ax"), lax.axis_index("ax"))
    if size_ax & (size_ax - 1):
        group = lax.all_gather(group, "ax", axis=2, tiled=True)
    else:
        step = 1
        while step < size_ax:
            other = lax.ppermute(group, "ax", [(i, i ^ step) for i in range(size_ax)])
            group = jnp.where(
                (me_ax // step) % 2 == 0,
                jnp.concatenate([group, other], axis=2),
                jnp.concatenate([other, group], axis=2),
            )
            step *= 2
    width = group.shape[2]
    tile = 8
    reach = 3
    n_f = stack_f.shape[0]
    widened = with_halo(stack_f, "ax", 2, tile, tile, False)
    size_az, length_a = (lax.axis_size("az"), widened.shape[1])
    up = [(i, (i + 1) % size_az) for i in range(size_az)]
    down = [(j, i) for i, j in up]
    slot = widened.shape[2] * widened.shape[3]

    def as_slots(rows):
        flat = rows.reshape(-1)
        count = -(-flat.shape[0] // slot)
        return jnp.pad(flat, (0, count * slot - flat.shape[0])).reshape((count,) + widened.shape[2:])

    def from_slots(slots):
        return slots.reshape(-1)[: n_planes * reach * width].reshape(n_planes, reach, width)

    sent_up = jnp.concatenate(
        [jnp.stack([widened[f, length_a - 1] for f in (0, 1, 2, 3, 5, 6, 7)]), as_slots(group[:, length_a - reach :])]
    )
    sent_down = jnp.concatenate(
        [jnp.stack([widened[f, 0] for f in (0, 1, 2, 3, 5, 7)] + [widened[7, 1]]), as_slots(group[:, :reach])]
    )
    sent_up = jnp.concatenate([sent_up, jnp.zeros_like(sent_up[:2])])
    sent_down = jnp.concatenate([sent_down, jnp.zeros_like(sent_down[:2])])
    from_below = lax.ppermute(sent_up, "az", up)[:8]
    from_above = lax.ppermute(sent_down, "az", down)[:8]
    blank = jnp.zeros_like(from_below[0])
    row_before = jnp.stack([from_below[i] for i in (0, 1, 2, 3)] + [blank] + [from_below[i] for i in (4, 5, 6)])
    row_after = jnp.stack([from_above[i] for i in (0, 1, 2, 3)] + [blank, from_above[4], blank, from_above[5]])
    row_after2 = jnp.stack([blank] * 7 + [from_above[6]])
    wide_f = jnp.concatenate(
        [row_before[:, None], widened[:n_f], row_after[:, None], row_after2[:, None]], axis=1
    )
    group_wide = jnp.concatenate([from_slots(from_below[7:]), group, from_slots(from_above[7:])], axis=1)
    group_wide = jnp.pad(group_wide, ((0, 0), (0, 0), (reach, reach)))

    oc = (reach, reach)
    p_t, p_b, va_t, vx_t, vr_b, u_t, u_b, w_t, w_b, b_t, b_b, s_t, wall_c, src_c = [group_wide[i] for i in range(14)]
    ea, eg, ex = (na + 3, width + 3, nx + 3)

    def c(f, da, dx, la, lx):
        return win(f, oc, da, dx, la, lx)

    def advect_c(f, u, w, da, dx, la, lx):
        return c(u, da, dx, la, lx) * (c(f, da, dx + 1, la, lx) - c(f, da, dx - 1, la, lx)) * 0.5 + c(
            w, da, dx, la, lx
        ) * (c(f, da + 1, dx, la, lx) - c(f, da - 1, dx, la, lx)) * 0.5

    new_az = c(va_t, -2, -1, ea + 1, eg) - step_dt * (
        advect_c(va_t, u_t, w_t, -2, -1, ea + 1, eg)
        + c(b_t, -2, -1, ea + 1, eg) * (c(p_t, -1, -1, ea + 1, eg) - c(p_t, -2, -1, ea + 1, eg))
    )
    new_ax = c(vx_t, -1, -2, ea, eg + 1) - step_dt * (
        advect_c(vx_t, u_t, w_t, -1, -2, ea, eg + 1)
        + c(b_t, -1, -2, ea, eg + 1) * (c(p_t, -1, -1, ea, eg + 1) - c(p_t, -1, -2, ea, eg + 1))
    )
    rad_top = c(wall_c, -1, -1, ea, eg) * c(p_t, -1, -1, ea, eg)
    rad_below = c(vr_b, -1, -1, ea, eg) - step_dt * (
        advect_c(vr_b, u_b, w_b, -1, -1, ea, eg)
        + c(b_b, -1, -1, ea, eg) * (c(p_t, -1, -1, ea, eg) - c(p_b, -1, -1, ea, eg))
    )
    spread = (new_az[1:] - new_az[:-1]) + (new_ax[:, 1:] - new_ax[:, :-1]) + (rad_top - rad_below)
    press_grid = (
        c(p_t, -1, -1, ea, eg)
        - step_dt * (advect_c(p_t, u_t, w_t, -1, -1, ea, eg) + c(s_t, -1, -1, ea, eg) * spread)
        + step_dt * c(src_c, -1, -1, ea, eg)
    )

    total_az = na * lax.axis_size("az")
    first_az = lax.axis_index("az") * na
    grid_az = jnp.remainder(mic_az - first_az + 1, total_az)
    row_hot = (grid_az[:, None] == lax.broadcasted_iota(jnp.int32, (1, ea), 1)).astype(jnp.float32)
    col_hot = (mic_ax + 1)[:, None] == lax.broadcasted_iota(jnp.int32, (1, eg), 1)
    heard = jnp.sum(jnp.where(col_hot, jnp.dot(row_hot, press_grid, precision=highest), 0.0), axis=1)
    misses = heard - measured
    in_group = (grid_az >= 1) & (grid_az <= na)
    square_sum = jnp.sum(jnp.where(in_group, misses * misses, 0.0))
    placed_grid = jnp.dot(row_hot.T, jnp.where(col_hot, misses[:, None], 0.0), precision=highest)

    rows_own = slice(reach, reach + na)
    cols_own = slice(reach, reach + width)
    segment_group = group_wide[15, rows_own, cols_own].astype(jnp.int32)
    segment_hot_group = segment_group[:, :, None] == lax.broadcasted_iota(jnp.int32, (1, 1, nseg), 2)
    sens_placed = (
        group_wide[0, rows_own, cols_own]
        * (-step_dt * group_wide[11, rows_own, cols_own])
        * placed_grid[1 : 1 + na, 1 : 1 + width]
    )
    seg_base = jnp.sum(jnp.where(segment_hot_group, group_wide[14, rows_own, cols_own][:, :, None], 0.0), axis=(0, 1))
    seg_placed = jnp.sum(jnp.where(segment_hot_group, sens_placed[:, :, None], 0.0), axis=(0, 1))

    local = lax.dynamic_slice_in_dim(group_wide, me_ax * nx, nx + 2 * reach, axis=2)
    placed = lax.dynamic_slice_in_dim(placed_grid, me_ax * nx, ex, axis=1)
    p_t, p_b, va_t, vx_t, vr_b, u_t, u_b, w_t, w_b, b_t, b_b, s_t, wall_c, src_c = [local[i] for i in range(14)]

    push_e = -step_dt * c(s_t, -1, -1, ea, ex) * placed
    r1a, r1x = na + 2, nx + 2
    head_az_e = push_e[:r1a, :r1x] - push_e[1 : 1 + r1a, :r1x]
    head_ax_e = push_e[:r1a, :r1x] - push_e[:r1a, 1 : 1 + r1x]
    head_rad_e = -push_e[:r1a, :r1x]
    u_t1, w_t1 = c(u_t, -1, -1, r1a, r1x), c(w_t, -1, -1, r1a, r1x)
    u_b1, w_b1 = c(u_b, -1, -1, r1a, r1x), c(w_b, -1, -1, r1a, r1x)
    b_t1 = c(b_t, -1, -1, r1a, r1x)
    own_e = (slice(1, 1 + na), slice(1, 1 + nx))
    back_press_t = (
        placed[1 : 1 + na, 1 : 1 + nx]
        - step_dt * advect_back(u_t1 * placed[:r1a, :r1x], w_t1 * placed[:r1a, :r1x], na, nx)
    )
    shove_az = step_dt * b_t1 * head_az_e
    shove_ax = step_dt * b_t1 * head_ax_e
    b_b0, wall_0, push_0 = c(b_b, 0, 0, na, nx), c(wall_c, 0, 0, na, nx), push_e[own_e]
    back_press_t = (
        back_press_t
        + (shove_az[own_e] - shove_az[0:na, 1 : 1 + nx])
        + (shove_ax[own_e] - shove_ax[1 : 1 + na, 0:nx])
        + step_dt * b_b0 * push_0
        + wall_0 * push_0
    )
    back_press_b = -step_dt * b_b0 * push_0
    back_az_t = head_az_e[own_e] - step_dt * advect_back(u_t1 * head_az_e, w_t1 * head_az_e, na, nx)
    back_ax_t = head_ax_e[own_e] - step_dt * advect_back(u_t1 * head_ax_e, w_t1 * head_ax_e, na, nx)
    back_rad_b = head_rad_e[own_e] - step_dt * advect_back(u_b1 * head_rad_e, w_b1 * head_rad_e, na, nx)
    zero = jnp.zeros_like(back_press_b)
    extra = jnp.stack(
        [
            jnp.stack([back_press_b, back_press_t], axis=-1),
            jnp.stack([zero, back_az_t], axis=-1),
            jnp.stack([zero, back_ax_t], axis=-1),
            jnp.stack([back_rad_b, zero], axis=-1),
        ]
    )

    of = (1, tile)
    g_a0, g_a1, g_a2, g_a3, g_u, g_w, g_b, g_push = [wide_f[i] for i in range(8)]

    def at(field, da, dx):
        return win(field, of, da, dx, na, nx)

    def head_az(da, dx):
        return at(g_a1, da, dx) + at(g_push, da, dx) - at(g_push, da + 1, dx)

    def head_ax(da, dx):
        return at(g_a2, da, dx) + at(g_push, da, dx) - at(g_push, da, dx + 1)

    casing = casing_mask((na, nx, nr))

    def head_rad(da, dx):
        push_here = at(g_push, da, dx)
        return at(g_a3, da, dx) + push_here - rad_next(push_here)

    def head_masked(da, dx):
        return jnp.where(casing, 0.0, head_rad(da, dx))

    def back_advect(head):
        return 0.5 * (at(g_u, 0, -1) * head(0, -1) - at(g_u, 0, 1) * head(0, 1)) + 0.5 * (
            at(g_w, -1, 0) * head(-1, 0) - at(g_w, 1, 0) * head(1, 0)
        )

    def seed(da, dx):
        return at(g_a0, da, dx)

    backs = [head(0, 0) - step_dt * back_advect(head) for head in (head_az, head_ax, head_masked)]
    shove_r = step_dt * at(g_b, 0, 0) * head_masked(0, 0)
    head_rad_own = head_rad(0, 0)
    back_press = (
        seed(0, 0)
        - step_dt * back_advect(seed)
        + (step_dt * at(g_b, 0, 0) * head_az(0, 0) - step_dt * at(g_b, -1, 0) * head_az(-1, 0))
        + (step_dt * at(g_b, 0, 0) * head_ax(0, 0) - step_dt * at(g_b, 0, -1) * head_ax(0, -1))
        + (shove_r - rad_prev(shove_r))
        + jnp.where(casing, wall[:, :, None] * head_rad_own, 0.0)
    )
    base = jnp.stack([back_press] + backs)

    totals = butterfly_sum(jnp.concatenate([square_sum[None], seg_base, seg_placed]), ("az",))
    mean_sq = totals[0] / mic_az.shape[0] + epsilon
    grad_scale = (na * lax.axis_size("az") * nx * lax.axis_size("ax") / nseg) ** (-0.5)
    liner_grad = (totals[1 : 1 + nseg] + totals[1 + nseg :] / mean_sq) * grad_scale
    misfit = 0.5 * jnp.log(mean_sq)
    lane = lax.broadcasted_iota(jnp.int32, (1, 1, 1, nr), 3)
    extra_scaled = extra / mean_sq
    correction = jnp.where(
        lane == nr - 1,
        extra_scaled[..., 1:2],
        jnp.where(lane == nr - 2, extra_scaled[..., 0:1], 0.0),
    )
    adjoint_out = base + correction
    return (adjoint_out, liner_grad, misfit)


def solution(mesh):
    placed = (
        P(None, "az", "ax", None),
        P(None, "az", "ax", None),
        P(None, "az", "ax", None),
        P(),
        P("az", "ax"),
        P("az", "ax"),
        P(),
        P(),
        P(),
        P(),
    )
    return jax.shard_map(
        shards,
        mesh=mesh,
        in_specs=placed,
        out_specs=(P(None, "az", "ax", None), P(), P()),
        check_vma=False,
    )
```

```python
import jax
import jax.numpy as jnp
from jax import lax
from jax.sharding import PartitionSpec as P

step_dt = 0.25
epsilon = 1e-06


def with_halo(array, axis, dim, before, after, wrap):
    size, length = (lax.axis_size(axis), array.shape[dim])
    up = [(i, (i + 1) % size) for i in range(size if wrap else size - 1)]
    down = [(j, i) for i, j in up]
    parts = []
    if before:
        parts.append(lax.ppermute(lax.slice_in_dim(array, length - before, length, axis=dim), axis, up))
    parts.append(array)
    if after:
        parts.append(lax.ppermute(lax.slice_in_dim(array, 0, after, axis=dim), axis, down))
    return jnp.concatenate(parts, axis=dim)


def exchange(array, before, after, ax_before=None, ax_after=None):
    ax_before = before if ax_before is None else ax_before
    ax_after = after if ax_after is None else ax_after
    widened = with_halo(array, "ax", 2, ax_before, ax_after, False)
    return with_halo(widened, "az", 1, before, after, True)


def win(values, origin, da, dx, na, nx):
    a0, x0 = origin[0] + da, origin[1] + dx
    return values[a0 : a0 + na, x0 : x0 + nx]


def rad_next(values):
    return jnp.concatenate([values[..., 1:], jnp.zeros_like(values[..., :1])], axis=-1)


def rad_prev(values):
    return jnp.concatenate([jnp.zeros_like(values[..., :1]), values[..., :-1]], axis=-1)


def casing_mask(shape):
    return lax.broadcasted_iota(jnp.int32, shape, len(shape) - 1) == shape[-1] - 1


def advect_back(carried_ax, carried_az, na, nx):
    return 0.5 * (carried_ax[..., 1 : 1 + na, 0:nx] - carried_ax[..., 1 : 1 + na, 2 : 2 + nx]) + 0.5 * (
        carried_az[..., 0:na, 1 : 1 + nx] - carried_az[..., 2 : 2 + na, 1 : 1 + nx]
    )


def advect_back4(carried_ax, carried_az, na, nx):
    return 0.5 * (carried_ax[:, 1 : 1 + na, 0:nx, :] - carried_ax[:, 1 : 1 + na, 2 : 2 + nx, :]) + 0.5 * (
        carried_az[:, 0:na, 1 : 1 + nx, :] - carried_az[:, 2 : 2 + na, 1 : 1 + nx, :]
    )


def butterfly_sum(values, axes):
    for axis in axes:
        size = lax.axis_size(axis)
        if size & (size - 1):
            values = lax.psum(values, axis)
            continue
        if axis == "ax" and size <= 4:
            terms = [values] + [lax.ppermute(values, axis, [(i, i ^ k) for i in range(size)]) for k in range(1, size)]
            while len(terms) > 1:
                terms = [terms[j] + terms[j + 1] for j in range(0, len(terms), 2)]
            values = terms[0]
            continue
        step = 1
        while step < size:
            values = values + lax.ppermute(values, axis, [(i, i ^ step) for i in range(size)])
            step *= 2
    return values


def shards(
    acoustic,
    mean_flow,
    adjoint_in,
    admittance,
    segment_id,
    noise_code,
    noise_table,
    mic_az,
    mic_ax,
    measured,
):
    na, nx, nr = (acoustic.shape[1], acoustic.shape[2], acoustic.shape[3])
    nseg = admittance.shape[0]
    buoyancy = 1.0 / mean_flow[2]
    stiffness = mean_flow[2] * mean_flow[3] * mean_flow[3]
    axial_flow, swirl_flow = (mean_flow[0], mean_flow[1])

    segment_hot = segment_id[:, :, None] == lax.broadcasted_iota(jnp.int32, (1, 1, nseg), 2)
    wall = jnp.sum(jnp.where(segment_hot, admittance, 0.0), axis=2)
    noise_hot = noise_code[:, :, None] == lax.broadcasted_iota(jnp.int32, (1, 1, noise_table.shape[0]), 2)
    top_profile = (nr - 1 + 0.5) / nr
    source_top = jnp.sum(jnp.where(noise_hot, noise_table, 0.0), axis=2) * top_profile

    a0 = adjoint_in[0]
    push = -step_dt * stiffness * a0
    stack_f = jnp.stack([a0, adjoint_in[1], adjoint_in[2], adjoint_in[3], axial_flow, swirl_flow, buoyancy, push])
    top, below = nr - 1, nr - 2
    planes = [
        acoustic[0, :, :, top],
        acoustic[0, :, :, below],
        acoustic[1, :, :, top],
        acoustic[2, :, :, top],
        acoustic[3, :, :, below],
        axial_flow[:, :, top],
        axial_flow[:, :, below],
        swirl_flow[:, :, top],
        swirl_flow[:, :, below],
        buoyancy[:, :, top],
        buoyancy[:, :, below],
        stiffness[:, :, top],
        wall,
        source_top,
    ]
    stack_c = jnp.stack(planes)
    n_planes = len(planes)
    tile = 8
    reach = 3
    packed = jnp.pad(jnp.transpose(stack_c, (1, 2, 0)), ((0, 0), (0, 0), (0, nr - n_planes)))
    stack_all = jnp.concatenate([stack_f, packed[None]], axis=0)
    n_f = stack_f.shape[0]
    widened = with_halo(stack_all, "ax", 2, tile, tile, False)
    size_az, length_a = (lax.axis_size("az"), widened.shape[1])
    up = [(i, (i + 1) % size_az) for i in range(size_az)]
    down = [(j, i) for i, j in up]
    sent_up = jnp.stack(
        [widened[f, length_a - 1] for f in (0, 1, 2, 3, 5, 6, 7)]
        + [widened[n_f, length_a - reach + k] for k in range(reach)]
    )
    sent_down = jnp.stack(
        [widened[f, 0] for f in (0, 1, 2, 3, 5, 7)] + [widened[7, 1]] + [widened[n_f, k] for k in range(reach)]
    )
    from_below = lax.ppermute(sent_up, "az", up)
    from_above = lax.ppermute(sent_down, "az", down)
    blank = jnp.zeros_like(from_below[0])
    row_before = jnp.stack([from_below[i] for i in (0, 1, 2, 3)] + [blank] + [from_below[i] for i in (4, 5, 6)])
    row_after = jnp.stack([from_above[i] for i in (0, 1, 2, 3)] + [blank, from_above[4], blank, from_above[5]])
    row_after2 = jnp.stack([blank] * 7 + [from_above[6]])
    wide_f = jnp.concatenate(
        [row_before[:, None], widened[:n_f], row_after[:, None], row_after2[:, None]], axis=1
    )
    wide_packed = jnp.concatenate([from_below[7:], widened[n_f], from_above[7:]], axis=0)
    wide_c = jnp.transpose(wide_packed[:, :, :n_planes], (2, 0, 1))

    oc = (reach, tile)
    p_t, p_b, va_t, vx_t, vr_b, u_t, u_b, w_t, w_b, b_t, b_b, s_t, wall_c, src_c = [wide_c[i] for i in range(14)]
    ea, ex = na + 3, nx + 3

    def c(f, da, dx, la, lx):
        return win(f, oc, da, dx, la, lx)

    def advect_c(f, u, w, da, dx, la, lx):
        return c(u, da, dx, la, lx) * (c(f, da, dx + 1, la, lx) - c(f, da, dx - 1, la, lx)) * 0.5 + c(
            w, da, dx, la, lx
        ) * (c(f, da + 1, dx, la, lx) - c(f, da - 1, dx, la, lx)) * 0.5

    new_az = c(va_t, -2, -1, ea + 1, ex) - step_dt * (
        advect_c(va_t, u_t, w_t, -2, -1, ea + 1, ex)
        + c(b_t, -2, -1, ea + 1, ex) * (c(p_t, -1, -1, ea + 1, ex) - c(p_t, -2, -1, ea + 1, ex))
    )
    new_ax = c(vx_t, -1, -2, ea, ex + 1) - step_dt * (
        advect_c(vx_t, u_t, w_t, -1, -2, ea, ex + 1)
        + c(b_t, -1, -2, ea, ex + 1) * (c(p_t, -1, -1, ea, ex + 1) - c(p_t, -1, -2, ea, ex + 1))
    )
    rad_top = c(wall_c, -1, -1, ea, ex) * c(p_t, -1, -1, ea, ex)
    rad_below = c(vr_b, -1, -1, ea, ex) - step_dt * (
        advect_c(vr_b, u_b, w_b, -1, -1, ea, ex)
        + c(b_b, -1, -1, ea, ex) * (c(p_t, -1, -1, ea, ex) - c(p_b, -1, -1, ea, ex))
    )
    spread = (new_az[1:] - new_az[:-1]) + (new_ax[:, 1:] - new_ax[:, :-1]) + (rad_top - rad_below)
    press_ring = (
        c(p_t, -1, -1, ea, ex)
        - step_dt * (advect_c(p_t, u_t, w_t, -1, -1, ea, ex) + c(s_t, -1, -1, ea, ex) * spread)
        + step_dt * c(src_c, -1, -1, ea, ex)
    )

    total_az = na * lax.axis_size("az")
    first_az = lax.axis_index("az") * na
    first_ax = lax.axis_index("ax") * nx
    ring_az = jnp.remainder(mic_az - first_az + 1, total_az)
    ring_ax = mic_ax - first_ax + 1
    on_ring = (ring_az < ea) & (ring_ax >= 0) & (ring_ax < ex)
    owned = (ring_az >= 1) & (ring_az <= na) & (ring_ax >= 1) & (ring_ax <= nx)
    ring_cell = jnp.where(on_ring, ring_az * ex + ring_ax, -1)
    cell_hot = ring_cell[:, None] == lax.broadcasted_iota(jnp.int32, (1, ea * ex), 1)
    heard = jnp.sum(jnp.where(cell_hot, press_ring.reshape(1, ea * ex), 0.0), axis=1)
    misses = heard - measured
    square_sum = jnp.sum(jnp.where(owned, misses * misses, 0.0))
    placed = jnp.sum(jnp.where(cell_hot, misses[:, None], 0.0), axis=0).reshape(ea, ex)

    push_e = -step_dt * c(s_t, -1, -1, ea, ex) * placed
    r1a, r1x = na + 2, nx + 2
    head_az_e = push_e[:r1a, :r1x] - push_e[1 : 1 + r1a, :r1x]
    head_ax_e = push_e[:r1a, :r1x] - push_e[:r1a, 1 : 1 + r1x]
    head_rad_e = -push_e[:r1a, :r1x]
    u_t1, w_t1 = c(u_t, -1, -1, r1a, r1x), c(w_t, -1, -1, r1a, r1x)
    u_b1, w_b1 = c(u_b, -1, -1, r1a, r1x), c(w_b, -1, -1, r1a, r1x)
    b_t1 = c(b_t, -1, -1, r1a, r1x)
    own_e = (slice(1, 1 + na), slice(1, 1 + nx))
    back_press_t = (
        placed[1 : 1 + na, 1 : 1 + nx]
        - step_dt * advect_back(u_t1 * placed[:r1a, :r1x], w_t1 * placed[:r1a, :r1x], na, nx)
    )
    shove_az = step_dt * b_t1 * head_az_e
    shove_ax = step_dt * b_t1 * head_ax_e
    b_b0, wall_0, push_0 = c(b_b, 0, 0, na, nx), c(wall_c, 0, 0, na, nx), push_e[own_e]
    back_press_t = (
        back_press_t
        + (shove_az[own_e] - shove_az[0:na, 1 : 1 + nx])
        + (shove_ax[own_e] - shove_ax[1 : 1 + na, 0:nx])
        + step_dt * b_b0 * push_0
        + wall_0 * push_0
    )
    back_press_b = -step_dt * b_b0 * push_0
    back_az_t = head_az_e[own_e] - step_dt * advect_back(u_t1 * head_az_e, w_t1 * head_az_e, na, nx)
    back_ax_t = head_ax_e[own_e] - step_dt * advect_back(u_t1 * head_ax_e, w_t1 * head_ax_e, na, nx)
    back_rad_b = head_rad_e[own_e] - step_dt * advect_back(u_b1 * head_rad_e, w_b1 * head_rad_e, na, nx)
    zero = jnp.zeros_like(back_press_b)
    extra = jnp.stack(
        [
            jnp.stack([back_press_b, back_press_t], axis=-1),
            jnp.stack([zero, back_az_t], axis=-1),
            jnp.stack([zero, back_ax_t], axis=-1),
            jnp.stack([back_rad_b, zero], axis=-1),
        ]
    )

    of = (1, tile)
    g_a0, g_a1, g_a2, g_a3, g_u, g_w, g_b, g_push = [wide_f[i] for i in range(8)]

    def at(field, da, dx):
        return win(field, of, da, dx, na, nx)

    def head_az(da, dx):
        return at(g_a1, da, dx) + at(g_push, da, dx) - at(g_push, da + 1, dx)

    def head_ax(da, dx):
        return at(g_a2, da, dx) + at(g_push, da, dx) - at(g_push, da, dx + 1)

    casing = casing_mask((na, nx, nr))

    def head_rad(da, dx):
        push_here = at(g_push, da, dx)
        return at(g_a3, da, dx) + push_here - rad_next(push_here)

    def head_masked(da, dx):
        return jnp.where(casing, 0.0, head_rad(da, dx))

    def back_advect(head):
        return 0.5 * (at(g_u, 0, -1) * head(0, -1) - at(g_u, 0, 1) * head(0, 1)) + 0.5 * (
            at(g_w, -1, 0) * head(-1, 0) - at(g_w, 1, 0) * head(1, 0)
        )

    def seed(da, dx):
        return at(g_a0, da, dx)

    backs = [head(0, 0) - step_dt * back_advect(head) for head in (head_az, head_ax, head_masked)]
    shove_r = step_dt * at(g_b, 0, 0) * head_masked(0, 0)
    head_rad_own = head_rad(0, 0)
    back_press = (
        seed(0, 0)
        - step_dt * back_advect(seed)
        + (step_dt * at(g_b, 0, 0) * head_az(0, 0) - step_dt * at(g_b, -1, 0) * head_az(-1, 0))
        + (step_dt * at(g_b, 0, 0) * head_ax(0, 0) - step_dt * at(g_b, 0, -1) * head_ax(0, -1))
        + (shove_r - rad_prev(shove_r))
        + jnp.where(casing, wall[:, :, None] * head_rad_own, 0.0)
    )
    base = jnp.stack([back_press] + backs)

    press_top = acoustic[0, :, :, top]
    sens_base = press_top * (adjoint_in[3, :, :, top] + push[:, :, top])
    sens_placed = press_top * push_0
    seg_base = jnp.sum(jnp.where(segment_hot, sens_base[:, :, None], 0.0), axis=(0, 1))
    seg_placed = jnp.sum(jnp.where(segment_hot, sens_placed[:, :, None], 0.0), axis=(0, 1))

    totals = butterfly_sum(jnp.concatenate([square_sum[None], seg_base, seg_placed]), ("az", "ax"))
    mean_sq = totals[0] / mic_az.shape[0] + epsilon
    grad_scale = (na * lax.axis_size("az") * nx * lax.axis_size("ax") / nseg) ** (-0.5)
    liner_grad = (totals[1 : 1 + nseg] + totals[1 + nseg :] / mean_sq) * grad_scale
    misfit = 0.5 * jnp.log(mean_sq)
    lane = lax.broadcasted_iota(jnp.int32, (1, 1, 1, nr), 3)
    extra_scaled = extra / mean_sq
    correction = jnp.where(
        lane == nr - 1,
        extra_scaled[..., 1:2],
        jnp.where(lane == nr - 2, extra_scaled[..., 0:1], 0.0),
    )
    adjoint_out = base + correction
    return (adjoint_out, liner_grad, misfit)


def solution(mesh):
    placed = (
        P(None, "az", "ax", None),
        P(None, "az", "ax", None),
        P(None, "az", "ax", None),
        P(),
        P("az", "ax"),
        P("az", "ax"),
        P(),
        P(),
        P(),
        P(),
    )
    return jax.shard_map(
        shards,
        mesh=mesh,
        in_specs=placed,
        out_specs=(P(None, "az", "ax", None), P(), P()),
        check_vma=False,
    )
```

```python
import jax
import jax.numpy as jnp
from jax import lax
from jax.sharding import PartitionSpec as P

step_dt = 0.25
epsilon = 1e-06


def with_halo(array, axis, dim, before, after, wrap):
    size, length = (lax.axis_size(axis), array.shape[dim])
    up = [(i, (i + 1) % size) for i in range(size if wrap else size - 1)]
    down = [(j, i) for i, j in up]
    parts = []
    if before:
        parts.append(lax.ppermute(lax.slice_in_dim(array, length - before, length, axis=dim), axis, up))
    parts.append(array)
    if after:
        parts.append(lax.ppermute(lax.slice_in_dim(array, 0, after, axis=dim), axis, down))
    return jnp.concatenate(parts, axis=dim)


def exchange(array, before, after, ax_before=None, ax_after=None):
    ax_before = before if ax_before is None else ax_before
    ax_after = after if ax_after is None else ax_after
    widened = with_halo(array, "ax", 2, ax_before, ax_after, False)
    return with_halo(widened, "az", 1, before, after, True)


def win(values, origin, da, dx, na, nx):
    a0, x0 = origin[0] + da, origin[1] + dx
    return values[a0 : a0 + na, x0 : x0 + nx]


def rad_next(values):
    return jnp.concatenate([values[..., 1:], jnp.zeros_like(values[..., :1])], axis=-1)


def rad_prev(values):
    return jnp.concatenate([jnp.zeros_like(values[..., :1]), values[..., :-1]], axis=-1)


def casing_mask(shape):
    return lax.broadcasted_iota(jnp.int32, shape, len(shape) - 1) == shape[-1] - 1


def advect_back(carried_ax, carried_az, na, nx):
    return 0.5 * (carried_ax[..., 1 : 1 + na, 0:nx] - carried_ax[..., 1 : 1 + na, 2 : 2 + nx]) + 0.5 * (
        carried_az[..., 0:na, 1 : 1 + nx] - carried_az[..., 2 : 2 + na, 1 : 1 + nx]
    )


def advect_back4(carried_ax, carried_az, na, nx):
    return 0.5 * (carried_ax[:, 1 : 1 + na, 0:nx, :] - carried_ax[:, 1 : 1 + na, 2 : 2 + nx, :]) + 0.5 * (
        carried_az[:, 0:na, 1 : 1 + nx, :] - carried_az[:, 2 : 2 + na, 1 : 1 + nx, :]
    )


def butterfly_sum(values, axes):
    for axis in axes:
        size = lax.axis_size(axis)
        if size & (size - 1):
            values = lax.psum(values, axis)
            continue
        step = 1
        while step < size:
            values = values + lax.ppermute(values, axis, [(i, i ^ step) for i in range(size)])
            step *= 2
    return values


def shards(
    acoustic,
    mean_flow,
    adjoint_in,
    admittance,
    segment_id,
    noise_code,
    noise_table,
    mic_az,
    mic_ax,
    measured,
):
    na, nx, nr = (acoustic.shape[1], acoustic.shape[2], acoustic.shape[3])
    nseg = admittance.shape[0]
    buoyancy = 1.0 / mean_flow[2]
    stiffness = mean_flow[2] * mean_flow[3] * mean_flow[3]
    axial_flow, swirl_flow = (mean_flow[0], mean_flow[1])

    segment_hot = segment_id[:, :, None] == lax.broadcasted_iota(jnp.int32, (1, 1, nseg), 2)
    wall = jnp.sum(jnp.where(segment_hot, admittance, 0.0), axis=2)
    noise_hot = noise_code[:, :, None] == lax.broadcasted_iota(jnp.int32, (1, 1, noise_table.shape[0]), 2)
    top_profile = (nr - 1 + 0.5) / nr
    source_top = jnp.sum(jnp.where(noise_hot, noise_table, 0.0), axis=2) * top_profile

    a0 = adjoint_in[0]
    push = -step_dt * stiffness * a0
    stack_f = jnp.stack([a0, adjoint_in[1], adjoint_in[2], adjoint_in[3], axial_flow, swirl_flow, buoyancy, push])
    top, below = nr - 1, nr - 2
    planes = [
        acoustic[0, :, :, top],
        acoustic[0, :, :, below],
        acoustic[1, :, :, top],
        acoustic[2, :, :, top],
        acoustic[3, :, :, below],
        axial_flow[:, :, top],
        axial_flow[:, :, below],
        swirl_flow[:, :, top],
        swirl_flow[:, :, below],
        buoyancy[:, :, top],
        buoyancy[:, :, below],
        stiffness[:, :, top],
        wall,
        source_top,
    ]
    stack_c = jnp.stack(planes)
    n_planes = len(planes)
    tile = 8
    reach = 3
    packed = jnp.pad(jnp.transpose(stack_c, (1, 2, 0)), ((0, 0), (0, 0), (0, nr - n_planes)))
    stack_all = jnp.concatenate([stack_f, packed[None]], axis=0)
    n_f = stack_f.shape[0]
    widened = with_halo(stack_all, "ax", 2, tile, tile, False)
    size_az, length_a = (lax.axis_size("az"), widened.shape[1])
    up = [(i, (i + 1) % size_az) for i in range(size_az)]
    down = [(j, i) for i, j in up]
    sent_up = jnp.stack(
        [widened[f, length_a - 1] for f in (0, 1, 2, 3, 5, 6, 7)]
        + [widened[n_f, length_a - reach + k] for k in range(reach)]
    )
    sent_down = jnp.stack(
        [widened[f, 0] for f in (0, 1, 2, 3, 5, 7)] + [widened[7, 1]] + [widened[n_f, k] for k in range(reach)]
    )
    from_below = lax.ppermute(sent_up, "az", up)
    from_above = lax.ppermute(sent_down, "az", down)
    blank = jnp.zeros_like(from_below[0])
    row_before = jnp.stack([from_below[i] for i in (0, 1, 2, 3)] + [blank] + [from_below[i] for i in (4, 5, 6)])
    row_after = jnp.stack([from_above[i] for i in (0, 1, 2, 3)] + [blank, from_above[4], blank, from_above[5]])
    row_after2 = jnp.stack([blank] * 7 + [from_above[6]])
    wide_f = jnp.concatenate(
        [row_before[:, None], widened[:n_f], row_after[:, None], row_after2[:, None]], axis=1
    )
    wide_packed = jnp.concatenate([from_below[7:], widened[n_f], from_above[7:]], axis=0)
    wide_c = jnp.transpose(wide_packed[:, :, :n_planes], (2, 0, 1))

    oc = (reach, tile)
    p_t, p_b, va_t, vx_t, vr_b, u_t, u_b, w_t, w_b, b_t, b_b, s_t, wall_c, src_c = [wide_c[i] for i in range(14)]
    ea, ex = na + 3, nx + 3

    def c(f, da, dx, la, lx):
        return win(f, oc, da, dx, la, lx)

    def advect_c(f, u, w, da, dx, la, lx):
        return c(u, da, dx, la, lx) * (c(f, da, dx + 1, la, lx) - c(f, da, dx - 1, la, lx)) * 0.5 + c(
            w, da, dx, la, lx
        ) * (c(f, da + 1, dx, la, lx) - c(f, da - 1, dx, la, lx)) * 0.5

    new_az = c(va_t, -2, -1, ea + 1, ex) - step_dt * (
        advect_c(va_t, u_t, w_t, -2, -1, ea + 1, ex)
        + c(b_t, -2, -1, ea + 1, ex) * (c(p_t, -1, -1, ea + 1, ex) - c(p_t, -2, -1, ea + 1, ex))
    )
    new_ax = c(vx_t, -1, -2, ea, ex + 1) - step_dt * (
        advect_c(vx_t, u_t, w_t, -1, -2, ea, ex + 1)
        + c(b_t, -1, -2, ea, ex + 1) * (c(p_t, -1, -1, ea, ex + 1) - c(p_t, -1, -2, ea, ex + 1))
    )
    rad_top = c(wall_c, -1, -1, ea, ex) * c(p_t, -1, -1, ea, ex)
    rad_below = c(vr_b, -1, -1, ea, ex) - step_dt * (
        advect_c(vr_b, u_b, w_b, -1, -1, ea, ex)
        + c(b_b, -1, -1, ea, ex) * (c(p_t, -1, -1, ea, ex) - c(p_b, -1, -1, ea, ex))
    )
    spread = (new_az[1:] - new_az[:-1]) + (new_ax[:, 1:] - new_ax[:, :-1]) + (rad_top - rad_below)
    press_ring = (
        c(p_t, -1, -1, ea, ex)
        - step_dt * (advect_c(p_t, u_t, w_t, -1, -1, ea, ex) + c(s_t, -1, -1, ea, ex) * spread)
        + step_dt * c(src_c, -1, -1, ea, ex)
    )

    total_az = na * lax.axis_size("az")
    first_az = lax.axis_index("az") * na
    first_ax = lax.axis_index("ax") * nx
    ring_az = jnp.remainder(mic_az - first_az + 1, total_az)
    ring_ax = mic_ax - first_ax + 1
    on_ring = (ring_az < ea) & (ring_ax >= 0) & (ring_ax < ex)
    owned = (ring_az >= 1) & (ring_az <= na) & (ring_ax >= 1) & (ring_ax <= nx)
    ring_cell = jnp.where(on_ring, ring_az * ex + ring_ax, -1)
    cell_hot = ring_cell[:, None] == lax.broadcasted_iota(jnp.int32, (1, ea * ex), 1)
    heard = jnp.sum(jnp.where(cell_hot, press_ring.reshape(1, ea * ex), 0.0), axis=1)
    misses = heard - measured
    square_sum = jnp.sum(jnp.where(owned, misses * misses, 0.0))
    placed = jnp.sum(jnp.where(cell_hot, misses[:, None], 0.0), axis=0).reshape(ea, ex)

    push_e = -step_dt * c(s_t, -1, -1, ea, ex) * placed
    r1a, r1x = na + 2, nx + 2
    head_az_e = push_e[:r1a, :r1x] - push_e[1 : 1 + r1a, :r1x]
    head_ax_e = push_e[:r1a, :r1x] - push_e[:r1a, 1 : 1 + r1x]
    head_rad_e = -push_e[:r1a, :r1x]
    u_t1, w_t1 = c(u_t, -1, -1, r1a, r1x), c(w_t, -1, -1, r1a, r1x)
    u_b1, w_b1 = c(u_b, -1, -1, r1a, r1x), c(w_b, -1, -1, r1a, r1x)
    b_t1 = c(b_t, -1, -1, r1a, r1x)
    own_e = (slice(1, 1 + na), slice(1, 1 + nx))
    back_press_t = (
        placed[1 : 1 + na, 1 : 1 + nx]
        - step_dt * advect_back(u_t1 * placed[:r1a, :r1x], w_t1 * placed[:r1a, :r1x], na, nx)
    )
    shove_az = step_dt * b_t1 * head_az_e
    shove_ax = step_dt * b_t1 * head_ax_e
    b_b0, wall_0, push_0 = c(b_b, 0, 0, na, nx), c(wall_c, 0, 0, na, nx), push_e[own_e]
    back_press_t = (
        back_press_t
        + (shove_az[own_e] - shove_az[0:na, 1 : 1 + nx])
        + (shove_ax[own_e] - shove_ax[1 : 1 + na, 0:nx])
        + step_dt * b_b0 * push_0
        + wall_0 * push_0
    )
    back_press_b = -step_dt * b_b0 * push_0
    back_az_t = head_az_e[own_e] - step_dt * advect_back(u_t1 * head_az_e, w_t1 * head_az_e, na, nx)
    back_ax_t = head_ax_e[own_e] - step_dt * advect_back(u_t1 * head_ax_e, w_t1 * head_ax_e, na, nx)
    back_rad_b = head_rad_e[own_e] - step_dt * advect_back(u_b1 * head_rad_e, w_b1 * head_rad_e, na, nx)
    zero = jnp.zeros_like(back_press_b)
    extra = jnp.stack(
        [
            jnp.stack([back_press_b, back_press_t], axis=-1),
            jnp.stack([zero, back_az_t], axis=-1),
            jnp.stack([zero, back_ax_t], axis=-1),
            jnp.stack([back_rad_b, zero], axis=-1),
        ]
    )

    of = (1, tile)
    g_a0, g_a1, g_a2, g_a3, g_u, g_w, g_b, g_push = [wide_f[i] for i in range(8)]

    def at(field, da, dx):
        return win(field, of, da, dx, na, nx)

    def head_az(da, dx):
        return at(g_a1, da, dx) + at(g_push, da, dx) - at(g_push, da + 1, dx)

    def head_ax(da, dx):
        return at(g_a2, da, dx) + at(g_push, da, dx) - at(g_push, da, dx + 1)

    casing = casing_mask((na, nx, nr))

    def head_rad(da, dx):
        push_here = at(g_push, da, dx)
        return at(g_a3, da, dx) + push_here - rad_next(push_here)

    def head_masked(da, dx):
        return jnp.where(casing, 0.0, head_rad(da, dx))

    def back_advect(head):
        return 0.5 * (at(g_u, 0, -1) * head(0, -1) - at(g_u, 0, 1) * head(0, 1)) + 0.5 * (
            at(g_w, -1, 0) * head(-1, 0) - at(g_w, 1, 0) * head(1, 0)
        )

    def seed(da, dx):
        return at(g_a0, da, dx)

    backs = [head(0, 0) - step_dt * back_advect(head) for head in (head_az, head_ax, head_masked)]
    shove_r = step_dt * at(g_b, 0, 0) * head_masked(0, 0)
    head_rad_own = head_rad(0, 0)
    back_press = (
        seed(0, 0)
        - step_dt * back_advect(seed)
        + (step_dt * at(g_b, 0, 0) * head_az(0, 0) - step_dt * at(g_b, -1, 0) * head_az(-1, 0))
        + (step_dt * at(g_b, 0, 0) * head_ax(0, 0) - step_dt * at(g_b, 0, -1) * head_ax(0, -1))
        + (shove_r - rad_prev(shove_r))
        + jnp.where(casing, wall[:, :, None] * head_rad_own, 0.0)
    )
    base = jnp.stack([back_press] + backs)

    late_rad, late_push, late_press, _ = lax.optimization_barrier((adjoint_in[3], push, acoustic[0], widened))
    press_top = late_press[:, :, top]
    sens_base = press_top * (late_rad[:, :, top] + late_push[:, :, top])
    sens_placed = press_top * push_0
    seg_base = jnp.sum(jnp.where(segment_hot, sens_base[:, :, None], 0.0), axis=(0, 1))
    seg_placed = jnp.sum(jnp.where(segment_hot, sens_placed[:, :, None], 0.0), axis=(0, 1))

    totals = butterfly_sum(jnp.concatenate([square_sum[None], seg_base, seg_placed]), ("az", "ax"))
    mean_sq = totals[0] / mic_az.shape[0] + epsilon
    grad_scale = (na * lax.axis_size("az") * nx * lax.axis_size("ax") / nseg) ** (-0.5)
    liner_grad = (totals[1 : 1 + nseg] + totals[1 + nseg :] / mean_sq) * grad_scale
    misfit = 0.5 * jnp.log(mean_sq)
    lane = lax.broadcasted_iota(jnp.int32, (1, 1, 1, nr), 3)
    extra_scaled = extra / mean_sq
    correction = jnp.where(
        lane == nr - 1,
        extra_scaled[..., 1:2],
        jnp.where(lane == nr - 2, extra_scaled[..., 0:1], 0.0),
    )
    adjoint_out = base + correction
    return (adjoint_out, liner_grad, misfit)


def solution(mesh):
    placed = (
        P(None, "az", "ax", None),
        P(None, "az", "ax", None),
        P(None, "az", "ax", None),
        P(),
        P("az", "ax"),
        P("az", "ax"),
        P(),
        P(),
        P(),
        P(),
    )
    return jax.shard_map(
        shards,
        mesh=mesh,
        in_specs=placed,
        out_specs=(P(None, "az", "ax", None), P(), P()),
        check_vma=False,
    )
```

```python
import jax
import jax.numpy as jnp
from jax import lax
from jax.sharding import PartitionSpec as P

step_dt = 0.25
epsilon = 1e-06


def with_halo(array, axis, dim, before, after, wrap):
    size, length = (lax.axis_size(axis), array.shape[dim])
    up = [(i, (i + 1) % size) for i in range(size if wrap else size - 1)]
    down = [(j, i) for i, j in up]
    parts = []
    if before:
        parts.append(lax.ppermute(lax.slice_in_dim(array, length - before, length, axis=dim), axis, up))
    parts.append(array)
    if after:
        parts.append(lax.ppermute(lax.slice_in_dim(array, 0, after, axis=dim), axis, down))
    return jnp.concatenate(parts, axis=dim)


def exchange(array, before, after, ax_before=None, ax_after=None):
    ax_before = before if ax_before is None else ax_before
    ax_after = after if ax_after is None else ax_after
    widened = with_halo(array, "ax", 2, ax_before, ax_after, False)
    return with_halo(widened, "az", 1, before, after, True)


def win(values, origin, da, dx, na, nx):
    a0, x0 = origin[0] + da, origin[1] + dx
    return values[a0 : a0 + na, x0 : x0 + nx]


def rad_next(values):
    return jnp.concatenate([values[..., 1:], jnp.zeros_like(values[..., :1])], axis=-1)


def rad_prev(values):
    return jnp.concatenate([jnp.zeros_like(values[..., :1]), values[..., :-1]], axis=-1)


def casing_mask(shape):
    return lax.broadcasted_iota(jnp.int32, shape, len(shape) - 1) == shape[-1] - 1


def advect_back(carried_ax, carried_az, na, nx):
    return 0.5 * (carried_ax[..., 1 : 1 + na, 0:nx] - carried_ax[..., 1 : 1 + na, 2 : 2 + nx]) + 0.5 * (
        carried_az[..., 0:na, 1 : 1 + nx] - carried_az[..., 2 : 2 + na, 1 : 1 + nx]
    )


def advect_back4(carried_ax, carried_az, na, nx):
    return 0.5 * (carried_ax[:, 1 : 1 + na, 0:nx, :] - carried_ax[:, 1 : 1 + na, 2 : 2 + nx, :]) + 0.5 * (
        carried_az[:, 0:na, 1 : 1 + nx, :] - carried_az[:, 2 : 2 + na, 1 : 1 + nx, :]
    )


def butterfly_sum(values, axes):
    for axis in axes:
        size = lax.axis_size(axis)
        if size & (size - 1):
            values = lax.psum(values, axis)
            continue
        step = 1
        while step < size:
            values = values + lax.ppermute(values, axis, [(i, i ^ step) for i in range(size)])
            step *= 2
    return values


def shards(
    acoustic,
    mean_flow,
    adjoint_in,
    admittance,
    segment_id,
    noise_code,
    noise_table,
    mic_az,
    mic_ax,
    measured,
):
    na, nx, nr = (acoustic.shape[1], acoustic.shape[2], acoustic.shape[3])
    nseg = admittance.shape[0]
    buoyancy = 1.0 / mean_flow[2]
    stiffness = mean_flow[2] * mean_flow[3] * mean_flow[3]
    axial_flow, swirl_flow = (mean_flow[0], mean_flow[1])

    segment_hot = segment_id[:, :, None] == lax.broadcasted_iota(jnp.int32, (1, 1, nseg), 2)
    wall = jnp.sum(jnp.where(segment_hot, admittance, 0.0), axis=2)
    noise_hot = noise_code[:, :, None] == lax.broadcasted_iota(jnp.int32, (1, 1, noise_table.shape[0]), 2)
    top_profile = (nr - 1 + 0.5) / nr
    source_top = jnp.sum(jnp.where(noise_hot, noise_table, 0.0), axis=2) * top_profile

    a0 = adjoint_in[0]
    push = -step_dt * stiffness * a0
    stack_f = jnp.stack([a0, adjoint_in[1], adjoint_in[2], adjoint_in[3], axial_flow, swirl_flow, buoyancy, push])
    top, below = nr - 1, nr - 2
    planes = [
        acoustic[0, :, :, top],
        acoustic[0, :, :, below],
        acoustic[1, :, :, top],
        acoustic[2, :, :, top],
        acoustic[3, :, :, below],
        axial_flow[:, :, top],
        axial_flow[:, :, below],
        swirl_flow[:, :, top],
        swirl_flow[:, :, below],
        buoyancy[:, :, top],
        buoyancy[:, :, below],
        stiffness[:, :, top],
        wall,
        source_top,
    ]
    stack_c = jnp.stack(planes)
    n_planes = len(planes)
    tile = 8
    reach = 3
    packed = jnp.pad(jnp.transpose(stack_c, (1, 2, 0)), ((0, 0), (0, 0), (0, nr - n_planes)))
    stack_all = jnp.concatenate([stack_f, packed[None]], axis=0)
    n_f = stack_f.shape[0]
    widened = with_halo(stack_all, "ax", 2, tile, tile, False)
    size_az, length_a = (lax.axis_size("az"), widened.shape[1])
    up = [(i, (i + 1) % size_az) for i in range(size_az)]
    down = [(j, i) for i, j in up]
    sent_up = jnp.stack(
        [widened[f, length_a - 1] for f in (0, 1, 2, 3, 5, 6, 7)]
        + [widened[n_f, length_a - reach + k] for k in range(reach)]
    )
    sent_down = jnp.stack(
        [widened[f, 0] for f in (0, 1, 2, 3, 5, 7)] + [widened[7, 1]] + [widened[n_f, k] for k in range(reach)]
    )
    from_below = lax.ppermute(sent_up, "az", up)
    from_above = lax.ppermute(sent_down, "az", down)
    blank = jnp.zeros_like(from_below[0])
    row_before = jnp.stack([from_below[i] for i in (0, 1, 2, 3)] + [blank] + [from_below[i] for i in (4, 5, 6)])
    row_after = jnp.stack([from_above[i] for i in (0, 1, 2, 3)] + [blank, from_above[4], blank, from_above[5]])
    row_after2 = jnp.stack([blank] * 7 + [from_above[6]])
    wide_f = jnp.concatenate(
        [row_before[:, None], widened[:n_f], row_after[:, None], row_after2[:, None]], axis=1
    )
    wide_packed = jnp.concatenate([from_below[7:], widened[n_f], from_above[7:]], axis=0)
    wide_c = jnp.transpose(wide_packed[:, :, :n_planes], (2, 0, 1))

    oc = (reach, tile)
    p_t, p_b, va_t, vx_t, vr_b, u_t, u_b, w_t, w_b, b_t, b_b, s_t, wall_c, src_c = [wide_c[i] for i in range(14)]
    ea, ex = na + 3, nx + 3

    def c(f, da, dx, la, lx):
        return win(f, oc, da, dx, la, lx)

    def advect_c(f, u, w, da, dx, la, lx):
        return c(u, da, dx, la, lx) * (c(f, da, dx + 1, la, lx) - c(f, da, dx - 1, la, lx)) * 0.5 + c(
            w, da, dx, la, lx
        ) * (c(f, da + 1, dx, la, lx) - c(f, da - 1, dx, la, lx)) * 0.5

    new_az = c(va_t, -2, -1, ea + 1, ex) - step_dt * (
        advect_c(va_t, u_t, w_t, -2, -1, ea + 1, ex)
        + c(b_t, -2, -1, ea + 1, ex) * (c(p_t, -1, -1, ea + 1, ex) - c(p_t, -2, -1, ea + 1, ex))
    )
    new_ax = c(vx_t, -1, -2, ea, ex + 1) - step_dt * (
        advect_c(vx_t, u_t, w_t, -1, -2, ea, ex + 1)
        + c(b_t, -1, -2, ea, ex + 1) * (c(p_t, -1, -1, ea, ex + 1) - c(p_t, -1, -2, ea, ex + 1))
    )
    rad_top = c(wall_c, -1, -1, ea, ex) * c(p_t, -1, -1, ea, ex)
    rad_below = c(vr_b, -1, -1, ea, ex) - step_dt * (
        advect_c(vr_b, u_b, w_b, -1, -1, ea, ex)
        + c(b_b, -1, -1, ea, ex) * (c(p_t, -1, -1, ea, ex) - c(p_b, -1, -1, ea, ex))
    )
    spread = (new_az[1:] - new_az[:-1]) + (new_ax[:, 1:] - new_ax[:, :-1]) + (rad_top - rad_below)
    press_ring = (
        c(p_t, -1, -1, ea, ex)
        - step_dt * (advect_c(p_t, u_t, w_t, -1, -1, ea, ex) + c(s_t, -1, -1, ea, ex) * spread)
        + step_dt * c(src_c, -1, -1, ea, ex)
    )

    total_az = na * lax.axis_size("az")
    first_az = lax.axis_index("az") * na
    first_ax = lax.axis_index("ax") * nx
    ring_az = jnp.remainder(mic_az - first_az + 1, total_az)
    ring_ax = mic_ax - first_ax + 1
    on_ring = (ring_az < ea) & (ring_ax >= 0) & (ring_ax < ex)
    owned = (ring_az >= 1) & (ring_az <= na) & (ring_ax >= 1) & (ring_ax <= nx)
    ring_cell = jnp.where(on_ring, ring_az * ex + ring_ax, -1)
    cell_hot = ring_cell[:, None] == lax.broadcasted_iota(jnp.int32, (1, ea * ex), 1)
    heard = jnp.sum(jnp.where(cell_hot, press_ring.reshape(1, ea * ex), 0.0), axis=1)
    misses = heard - measured
    square_sum = jnp.sum(jnp.where(owned, misses * misses, 0.0))
    placed = jnp.sum(jnp.where(cell_hot, misses[:, None], 0.0), axis=0).reshape(ea, ex)

    push_e = -step_dt * c(s_t, -1, -1, ea, ex) * placed
    r1a, r1x = na + 2, nx + 2
    head_az_e = push_e[:r1a, :r1x] - push_e[1 : 1 + r1a, :r1x]
    head_ax_e = push_e[:r1a, :r1x] - push_e[:r1a, 1 : 1 + r1x]
    head_rad_e = -push_e[:r1a, :r1x]
    u_t1, w_t1 = c(u_t, -1, -1, r1a, r1x), c(w_t, -1, -1, r1a, r1x)
    u_b1, w_b1 = c(u_b, -1, -1, r1a, r1x), c(w_b, -1, -1, r1a, r1x)
    b_t1 = c(b_t, -1, -1, r1a, r1x)
    own_e = (slice(1, 1 + na), slice(1, 1 + nx))
    back_press_t = (
        placed[1 : 1 + na, 1 : 1 + nx]
        - step_dt * advect_back(u_t1 * placed[:r1a, :r1x], w_t1 * placed[:r1a, :r1x], na, nx)
    )
    shove_az = step_dt * b_t1 * head_az_e
    shove_ax = step_dt * b_t1 * head_ax_e
    b_b0, wall_0, push_0 = c(b_b, 0, 0, na, nx), c(wall_c, 0, 0, na, nx), push_e[own_e]
    back_press_t = (
        back_press_t
        + (shove_az[own_e] - shove_az[0:na, 1 : 1 + nx])
        + (shove_ax[own_e] - shove_ax[1 : 1 + na, 0:nx])
        + step_dt * b_b0 * push_0
        + wall_0 * push_0
    )
    back_press_b = -step_dt * b_b0 * push_0
    back_az_t = head_az_e[own_e] - step_dt * advect_back(u_t1 * head_az_e, w_t1 * head_az_e, na, nx)
    back_ax_t = head_ax_e[own_e] - step_dt * advect_back(u_t1 * head_ax_e, w_t1 * head_ax_e, na, nx)
    back_rad_b = head_rad_e[own_e] - step_dt * advect_back(u_b1 * head_rad_e, w_b1 * head_rad_e, na, nx)
    zero = jnp.zeros_like(back_press_b)
    extra = jnp.stack(
        [
            jnp.stack([back_press_b, back_press_t], axis=-1),
            jnp.stack([zero, back_az_t], axis=-1),
            jnp.stack([zero, back_ax_t], axis=-1),
            jnp.stack([back_rad_b, zero], axis=-1),
        ]
    )

    of = (1, tile)
    g_a0, g_a1, g_a2, g_a3, g_u, g_w, g_b, g_push = [wide_f[i] for i in range(8)]

    def at(field, da, dx):
        return win(field, of, da, dx, na, nx)

    def head_az(da, dx):
        return at(g_a1, da, dx) + at(g_push, da, dx) - at(g_push, da + 1, dx)

    def head_ax(da, dx):
        return at(g_a2, da, dx) + at(g_push, da, dx) - at(g_push, da, dx + 1)

    casing = casing_mask((na, nx, nr))

    def head_rad(da, dx):
        push_here = at(g_push, da, dx)
        return at(g_a3, da, dx) + push_here - rad_next(push_here)

    def head_masked(da, dx):
        return jnp.where(casing, 0.0, head_rad(da, dx))

    def back_advect(head):
        return 0.5 * (at(g_u, 0, -1) * head(0, -1) - at(g_u, 0, 1) * head(0, 1)) + 0.5 * (
            at(g_w, -1, 0) * head(-1, 0) - at(g_w, 1, 0) * head(1, 0)
        )

    def seed(da, dx):
        return at(g_a0, da, dx)

    backs = [head(0, 0) - step_dt * back_advect(head) for head in (head_az, head_ax, head_masked)]
    shove_r = step_dt * at(g_b, 0, 0) * head_masked(0, 0)
    head_rad_own = head_rad(0, 0)
    back_press = (
        seed(0, 0)
        - step_dt * back_advect(seed)
        + (step_dt * at(g_b, 0, 0) * head_az(0, 0) - step_dt * at(g_b, -1, 0) * head_az(-1, 0))
        + (step_dt * at(g_b, 0, 0) * head_ax(0, 0) - step_dt * at(g_b, 0, -1) * head_ax(0, -1))
        + (shove_r - rad_prev(shove_r))
        + jnp.where(casing, wall[:, :, None] * head_rad_own, 0.0)
    )
    base = jnp.stack([back_press] + backs)

    late_rad, late_push, late_press, _ = lax.optimization_barrier((adjoint_in[3], push, acoustic[0], widened))
    press_top = late_press[:, :, top]
    sens_base = press_top * (late_rad[:, :, top] + late_push[:, :, top])
    sens_placed = press_top * push_0
    seg_base = jnp.sum(jnp.where(segment_hot, sens_base[:, :, None], 0.0), axis=(0, 1))
    seg_placed = jnp.sum(jnp.where(segment_hot, sens_placed[:, :, None], 0.0), axis=(0, 1))

    totals = butterfly_sum(jnp.concatenate([square_sum[None], seg_base, seg_placed]), ("az", "ax"))
    mean_sq = totals[0] / mic_az.shape[0] + epsilon
    grad_scale = (na * lax.axis_size("az") * nx * lax.axis_size("ax") / nseg) ** (-0.5)
    liner_grad = (totals[1 : 1 + nseg] + totals[1 + nseg :] / mean_sq) * grad_scale
    misfit = 0.5 * jnp.log(mean_sq)
    adjoint_out = lax.dynamic_update_slice(base, base[..., nr - 2 :] + extra / mean_sq, (0, 0, 0, nr - 2))
    return (adjoint_out, liner_grad, misfit)


def solution(mesh):
    placed = (
        P(None, "az", "ax", None),
        P(None, "az", "ax", None),
        P(None, "az", "ax", None),
        P(),
        P("az", "ax"),
        P("az", "ax"),
        P(),
        P(),
        P(),
        P(),
    )
    return jax.shard_map(
        shards,
        mesh=mesh,
        in_specs=placed,
        out_specs=(P(None, "az", "ax", None), P(), P()),
        check_vma=False,
    )
```

```python
import jax
import jax.numpy as jnp
from jax import lax
from jax.sharding import PartitionSpec as P

step_dt = 0.25
epsilon = 1e-06


def with_halo(array, axis, dim, before, after, wrap):
    size, length = (lax.axis_size(axis), array.shape[dim])
    up = [(i, (i + 1) % size) for i in range(size if wrap else size - 1)]
    down = [(j, i) for i, j in up]
    parts = []
    if before:
        parts.append(lax.ppermute(lax.slice_in_dim(array, length - before, length, axis=dim), axis, up))
    parts.append(array)
    if after:
        parts.append(lax.ppermute(lax.slice_in_dim(array, 0, after, axis=dim), axis, down))
    return jnp.concatenate(parts, axis=dim)


def exchange(array, before, after, ax_before=None, ax_after=None):
    ax_before = before if ax_before is None else ax_before
    ax_after = after if ax_after is None else ax_after
    widened = with_halo(array, "ax", 2, ax_before, ax_after, False)
    return with_halo(widened, "az", 1, before, after, True)


def win(values, origin, da, dx, na, nx):
    a0, x0 = origin[0] + da, origin[1] + dx
    return values[a0 : a0 + na, x0 : x0 + nx]


def rad_next(values):
    return jnp.concatenate([values[..., 1:], jnp.zeros_like(values[..., :1])], axis=-1)


def rad_prev(values):
    return jnp.concatenate([jnp.zeros_like(values[..., :1]), values[..., :-1]], axis=-1)


def casing_mask(shape):
    return lax.broadcasted_iota(jnp.int32, shape, len(shape) - 1) == shape[-1] - 1


def advect_back(carried_ax, carried_az, na, nx):
    return 0.5 * (carried_ax[..., 1 : 1 + na, 0:nx] - carried_ax[..., 1 : 1 + na, 2 : 2 + nx]) + 0.5 * (
        carried_az[..., 0:na, 1 : 1 + nx] - carried_az[..., 2 : 2 + na, 1 : 1 + nx]
    )


def advect_back4(carried_ax, carried_az, na, nx):
    return 0.5 * (carried_ax[:, 1 : 1 + na, 0:nx, :] - carried_ax[:, 1 : 1 + na, 2 : 2 + nx, :]) + 0.5 * (
        carried_az[:, 0:na, 1 : 1 + nx, :] - carried_az[:, 2 : 2 + na, 1 : 1 + nx, :]
    )


def butterfly_sum(values, axes):
    for axis in axes:
        size = lax.axis_size(axis)
        if size & (size - 1):
            values = lax.psum(values, axis)
            continue
        step = 1
        while step < size:
            values = values + lax.ppermute(values, axis, [(i, i ^ step) for i in range(size)])
            step *= 2
    return values


def shards(
    acoustic,
    mean_flow,
    adjoint_in,
    admittance,
    segment_id,
    noise_code,
    noise_table,
    mic_az,
    mic_ax,
    measured,
):
    na, nx, nr = (acoustic.shape[1], acoustic.shape[2], acoustic.shape[3])
    nseg = admittance.shape[0]
    buoyancy = 1.0 / mean_flow[2]
    stiffness = mean_flow[2] * mean_flow[3] * mean_flow[3]
    axial_flow, swirl_flow = (mean_flow[0], mean_flow[1])

    segment_hot = segment_id[:, :, None] == lax.broadcasted_iota(jnp.int32, (1, 1, nseg), 2)
    wall = jnp.sum(jnp.where(segment_hot, admittance, 0.0), axis=2)
    noise_hot = noise_code[:, :, None] == lax.broadcasted_iota(jnp.int32, (1, 1, noise_table.shape[0]), 2)
    top_profile = (nr - 1 + 0.5) / nr
    source_top = jnp.sum(jnp.where(noise_hot, noise_table, 0.0), axis=2) * top_profile

    a0 = adjoint_in[0]
    push = -step_dt * stiffness * a0
    stack_f = jnp.stack([a0, adjoint_in[1], adjoint_in[2], adjoint_in[3], axial_flow, swirl_flow, buoyancy, push])
    top, below = nr - 1, nr - 2
    planes = [
        acoustic[0, :, :, top],
        acoustic[0, :, :, below],
        acoustic[1, :, :, top],
        acoustic[2, :, :, top],
        acoustic[3, :, :, below],
        axial_flow[:, :, top],
        axial_flow[:, :, below],
        swirl_flow[:, :, top],
        swirl_flow[:, :, below],
        buoyancy[:, :, top],
        buoyancy[:, :, below],
        stiffness[:, :, top],
        wall,
        source_top,
    ]
    stack_c = jnp.stack(planes)
    n_planes = len(planes)
    tile = 8
    reach = 3
    packed = jnp.pad(jnp.transpose(stack_c, (1, 2, 0)), ((0, 0), (0, 0), (0, nr - n_planes)))
    stack_all = jnp.concatenate([stack_f, packed[None]], axis=0)
    n_f = stack_f.shape[0]
    widened = with_halo(stack_all, "ax", 2, tile, tile, False)
    size_az, length_a = (lax.axis_size("az"), widened.shape[1])
    up = [(i, (i + 1) % size_az) for i in range(size_az)]
    down = [(j, i) for i, j in up]
    sent_up = jnp.stack(
        [widened[f, length_a - 1] for f in (0, 1, 2, 3, 5, 6, 7)]
        + [widened[n_f, length_a - reach + k] for k in range(reach)]
    )
    sent_down = jnp.stack(
        [widened[f, 0] for f in (0, 1, 2, 3, 5, 7)] + [widened[7, 1]] + [widened[n_f, k] for k in range(reach)]
    )
    from_below = lax.ppermute(sent_up, "az", up)
    from_above = lax.ppermute(sent_down, "az", down)
    blank = jnp.zeros_like(from_below[0])
    row_before = jnp.stack([from_below[i] for i in (0, 1, 2, 3)] + [blank] + [from_below[i] for i in (4, 5, 6)])
    row_after = jnp.stack([from_above[i] for i in (0, 1, 2, 3)] + [blank, from_above[4], blank, from_above[5]])
    row_after2 = jnp.stack([blank] * 7 + [from_above[6]])
    wide_f = jnp.concatenate(
        [row_before[:, None], widened[:n_f], row_after[:, None], row_after2[:, None]], axis=1
    )
    wide_packed = jnp.concatenate([from_below[7:], widened[n_f], from_above[7:]], axis=0)
    wide_c = jnp.transpose(wide_packed[:, :, :n_planes], (2, 0, 1))

    oc = (reach, tile)
    p_t, p_b, va_t, vx_t, vr_b, u_t, u_b, w_t, w_b, b_t, b_b, s_t, wall_c, src_c = [wide_c[i] for i in range(14)]
    ea, ex = na + 3, nx + 3

    def c(f, da, dx, la, lx):
        return win(f, oc, da, dx, la, lx)

    def advect_c(f, u, w, da, dx, la, lx):
        return c(u, da, dx, la, lx) * (c(f, da, dx + 1, la, lx) - c(f, da, dx - 1, la, lx)) * 0.5 + c(
            w, da, dx, la, lx
        ) * (c(f, da + 1, dx, la, lx) - c(f, da - 1, dx, la, lx)) * 0.5

    new_az = c(va_t, -2, -1, ea + 1, ex) - step_dt * (
        advect_c(va_t, u_t, w_t, -2, -1, ea + 1, ex)
        + c(b_t, -2, -1, ea + 1, ex) * (c(p_t, -1, -1, ea + 1, ex) - c(p_t, -2, -1, ea + 1, ex))
    )
    new_ax = c(vx_t, -1, -2, ea, ex + 1) - step_dt * (
        advect_c(vx_t, u_t, w_t, -1, -2, ea, ex + 1)
        + c(b_t, -1, -2, ea, ex + 1) * (c(p_t, -1, -1, ea, ex + 1) - c(p_t, -1, -2, ea, ex + 1))
    )
    rad_top = c(wall_c, -1, -1, ea, ex) * c(p_t, -1, -1, ea, ex)
    rad_below = c(vr_b, -1, -1, ea, ex) - step_dt * (
        advect_c(vr_b, u_b, w_b, -1, -1, ea, ex)
        + c(b_b, -1, -1, ea, ex) * (c(p_t, -1, -1, ea, ex) - c(p_b, -1, -1, ea, ex))
    )
    spread = (new_az[1:] - new_az[:-1]) + (new_ax[:, 1:] - new_ax[:, :-1]) + (rad_top - rad_below)
    press_ring = (
        c(p_t, -1, -1, ea, ex)
        - step_dt * (advect_c(p_t, u_t, w_t, -1, -1, ea, ex) + c(s_t, -1, -1, ea, ex) * spread)
        + step_dt * c(src_c, -1, -1, ea, ex)
    )

    total_az = na * lax.axis_size("az")
    first_az = lax.axis_index("az") * na
    first_ax = lax.axis_index("ax") * nx
    ring_az = jnp.remainder(mic_az - first_az + 1, total_az)
    ring_ax = mic_ax - first_ax + 1
    on_ring = (ring_az < ea) & (ring_ax >= 0) & (ring_ax < ex)
    owned = (ring_az >= 1) & (ring_az <= na) & (ring_ax >= 1) & (ring_ax <= nx)
    ring_cell = jnp.where(on_ring, ring_az * ex + ring_ax, -1)
    cell_hot = ring_cell[:, None] == lax.broadcasted_iota(jnp.int32, (1, ea * ex), 1)
    heard = jnp.sum(jnp.where(cell_hot, press_ring.reshape(1, ea * ex), 0.0), axis=1)
    misses = heard - measured
    square_sum = jnp.sum(jnp.where(owned, misses * misses, 0.0))
    placed = jnp.sum(jnp.where(cell_hot, misses[:, None], 0.0), axis=0).reshape(ea, ex)

    push_e = -step_dt * c(s_t, -1, -1, ea, ex) * placed
    r1a, r1x = na + 2, nx + 2
    head_az_e = push_e[:r1a, :r1x] - push_e[1 : 1 + r1a, :r1x]
    head_ax_e = push_e[:r1a, :r1x] - push_e[:r1a, 1 : 1 + r1x]
    head_rad_e = -push_e[:r1a, :r1x]
    u_t1, w_t1 = c(u_t, -1, -1, r1a, r1x), c(w_t, -1, -1, r1a, r1x)
    u_b1, w_b1 = c(u_b, -1, -1, r1a, r1x), c(w_b, -1, -1, r1a, r1x)
    b_t1 = c(b_t, -1, -1, r1a, r1x)
    own_e = (slice(1, 1 + na), slice(1, 1 + nx))
    back_press_t = (
        placed[1 : 1 + na, 1 : 1 + nx]
        - step_dt * advect_back(u_t1 * placed[:r1a, :r1x], w_t1 * placed[:r1a, :r1x], na, nx)
    )
    shove_az = step_dt * b_t1 * head_az_e
    shove_ax = step_dt * b_t1 * head_ax_e
    b_b0, wall_0, push_0 = c(b_b, 0, 0, na, nx), c(wall_c, 0, 0, na, nx), push_e[own_e]
    back_press_t = (
        back_press_t
        + (shove_az[own_e] - shove_az[0:na, 1 : 1 + nx])
        + (shove_ax[own_e] - shove_ax[1 : 1 + na, 0:nx])
        + step_dt * b_b0 * push_0
        + wall_0 * push_0
    )
    back_press_b = -step_dt * b_b0 * push_0
    back_az_t = head_az_e[own_e] - step_dt * advect_back(u_t1 * head_az_e, w_t1 * head_az_e, na, nx)
    back_ax_t = head_ax_e[own_e] - step_dt * advect_back(u_t1 * head_ax_e, w_t1 * head_ax_e, na, nx)
    back_rad_b = head_rad_e[own_e] - step_dt * advect_back(u_b1 * head_rad_e, w_b1 * head_rad_e, na, nx)
    zero = jnp.zeros_like(back_press_b)
    extra = jnp.stack(
        [
            jnp.stack([back_press_b, back_press_t], axis=-1),
            jnp.stack([zero, back_az_t], axis=-1),
            jnp.stack([zero, back_ax_t], axis=-1),
            jnp.stack([back_rad_b, zero], axis=-1),
        ]
    )

    of = (1, tile)
    g_a0, g_a1, g_a2, g_a3, g_u, g_w, g_b, g_push = [wide_f[i] for i in range(8)]

    def at(field, da, dx):
        return win(field, of, da, dx, na, nx)

    def head_az(da, dx):
        return at(g_a1, da, dx) + at(g_push, da, dx) - at(g_push, da + 1, dx)

    def head_ax(da, dx):
        return at(g_a2, da, dx) + at(g_push, da, dx) - at(g_push, da, dx + 1)

    casing = casing_mask((na, nx, nr))

    def head_rad(da, dx):
        push_here = at(g_push, da, dx)
        return at(g_a3, da, dx) + push_here - rad_next(push_here)

    def head_masked(da, dx):
        return jnp.where(casing, 0.0, head_rad(da, dx))

    def back_advect(head):
        return 0.5 * (at(g_u, 0, -1) * head(0, -1) - at(g_u, 0, 1) * head(0, 1)) + 0.5 * (
            at(g_w, -1, 0) * head(-1, 0) - at(g_w, 1, 0) * head(1, 0)
        )

    def seed(da, dx):
        return at(g_a0, da, dx)

    backs = [head(0, 0) - step_dt * back_advect(head) for head in (head_az, head_ax, head_masked)]
    shove_r = step_dt * at(g_b, 0, 0) * head_masked(0, 0)
    head_rad_own = head_rad(0, 0)
    back_press = (
        seed(0, 0)
        - step_dt * back_advect(seed)
        + (step_dt * at(g_b, 0, 0) * head_az(0, 0) - step_dt * at(g_b, -1, 0) * head_az(-1, 0))
        + (step_dt * at(g_b, 0, 0) * head_ax(0, 0) - step_dt * at(g_b, 0, -1) * head_ax(0, -1))
        + (shove_r - rad_prev(shove_r))
        + jnp.where(casing, wall[:, :, None] * head_rad_own, 0.0)
    )
    base = jnp.stack([back_press] + backs)

    late_rad, late_push, late_press, _ = lax.optimization_barrier((adjoint_in[3], push, acoustic[0], widened))
    press_top = late_press[:, :, top]
    sens_base = press_top * (late_rad[:, :, top] + late_push[:, :, top])
    sens_placed = press_top * push_0
    slot = lax.broadcasted_iota(jnp.int32, (1, 1, 1 + 2 * nseg), 2)
    first_cell = (lax.broadcasted_iota(jnp.int32, (na, nx, 1), 0) == 0) & (
        lax.broadcasted_iota(jnp.int32, (na, nx, 1), 1) == 0
    )
    seg_here = segment_id[:, :, None]
    payload = jnp.sum(
        jnp.where(
            slot == 0,
            jnp.where(first_cell, square_sum, 0.0),
            jnp.where(
                slot <= nseg,
                jnp.where(seg_here == slot - 1, sens_base[:, :, None], 0.0),
                jnp.where(seg_here == slot - 1 - nseg, sens_placed[:, :, None], 0.0),
            ),
        ),
        axis=(0, 1),
    )

    totals = butterfly_sum(payload, ("az", "ax"))
    mean_sq = totals[0] / mic_az.shape[0] + epsilon
    grad_scale = (na * lax.axis_size("az") * nx * lax.axis_size("ax") / nseg) ** (-0.5)
    liner_grad = (totals[1 : 1 + nseg] + totals[1 + nseg :] / mean_sq) * grad_scale
    misfit = 0.5 * jnp.log(mean_sq)
    lane = lax.broadcasted_iota(jnp.int32, (1, 1, 1, nr), 3)
    extra_scaled = extra / mean_sq
    correction = jnp.where(
        lane == nr - 1,
        extra_scaled[..., 1:2],
        jnp.where(lane == nr - 2, extra_scaled[..., 0:1], 0.0),
    )
    adjoint_out = base + correction
    return (adjoint_out, liner_grad, misfit)


def solution(mesh):
    placed = (
        P(None, "az", "ax", None),
        P(None, "az", "ax", None),
        P(None, "az", "ax", None),
        P(),
        P("az", "ax"),
        P("az", "ax"),
        P(),
        P(),
        P(),
        P(),
    )
    return jax.shard_map(
        shards,
        mesh=mesh,
        in_specs=placed,
        out_specs=(P(None, "az", "ax", None), P(), P()),
        check_vma=False,
    )
```

```python
import jax
import jax.numpy as jnp
from jax import lax
from jax.sharding import PartitionSpec as P

step_dt = 0.25
epsilon = 1e-06


def with_halo(array, axis, dim, before, after, wrap):
    size, length = (lax.axis_size(axis), array.shape[dim])
    up = [(i, (i + 1) % size) for i in range(size if wrap else size - 1)]
    down = [(j, i) for i, j in up]
    parts = []
    if before:
        parts.append(lax.ppermute(lax.slice_in_dim(array, length - before, length, axis=dim), axis, up))
    parts.append(array)
    if after:
        parts.append(lax.ppermute(lax.slice_in_dim(array, 0, after, axis=dim), axis, down))
    return jnp.concatenate(parts, axis=dim)


def exchange(array, before, after, ax_before=None, ax_after=None):
    ax_before = before if ax_before is None else ax_before
    ax_after = after if ax_after is None else ax_after
    widened = with_halo(array, "ax", 2, ax_before, ax_after, False)
    return with_halo(widened, "az", 1, before, after, True)


def win(values, origin, da, dx, na, nx):
    a0, x0 = origin[0] + da, origin[1] + dx
    return values[a0 : a0 + na, x0 : x0 + nx]


def rad_next(values):
    return jnp.concatenate([values[..., 1:], jnp.zeros_like(values[..., :1])], axis=-1)


def rad_prev(values):
    return jnp.concatenate([jnp.zeros_like(values[..., :1]), values[..., :-1]], axis=-1)


def casing_mask(shape):
    return lax.broadcasted_iota(jnp.int32, shape, len(shape) - 1) == shape[-1] - 1


def advect_back(carried_ax, carried_az, na, nx):
    return 0.5 * (carried_ax[..., 1 : 1 + na, 0:nx] - carried_ax[..., 1 : 1 + na, 2 : 2 + nx]) + 0.5 * (
        carried_az[..., 0:na, 1 : 1 + nx] - carried_az[..., 2 : 2 + na, 1 : 1 + nx]
    )


def advect_back4(carried_ax, carried_az, na, nx):
    return 0.5 * (carried_ax[:, 1 : 1 + na, 0:nx, :] - carried_ax[:, 1 : 1 + na, 2 : 2 + nx, :]) + 0.5 * (
        carried_az[:, 0:na, 1 : 1 + nx, :] - carried_az[:, 2 : 2 + na, 1 : 1 + nx, :]
    )


def butterfly_sum(values, axes, skip_first=False):
    for index, axis in enumerate(axes):
        size = lax.axis_size(axis)
        if size & (size - 1):
            values = lax.psum(values, axis)
            continue
        step = 2 if (skip_first and index == 0) else 1
        while step < size:
            values = values + lax.ppermute(values, axis, [(i, i ^ step) for i in range(size)])
            step *= 2
    return values


def shards(
    acoustic,
    mean_flow,
    adjoint_in,
    admittance,
    segment_id,
    noise_code,
    noise_table,
    mic_az,
    mic_ax,
    measured,
):
    na, nx, nr = (acoustic.shape[1], acoustic.shape[2], acoustic.shape[3])
    nseg = admittance.shape[0]
    buoyancy = 1.0 / mean_flow[2]
    stiffness = mean_flow[2] * mean_flow[3] * mean_flow[3]
    axial_flow, swirl_flow = (mean_flow[0], mean_flow[1])

    segment_hot = segment_id[:, :, None] == lax.broadcasted_iota(jnp.int32, (1, 1, nseg), 2)
    wall = jnp.sum(jnp.where(segment_hot, admittance, 0.0), axis=2)
    noise_hot = noise_code[:, :, None] == lax.broadcasted_iota(jnp.int32, (1, 1, noise_table.shape[0]), 2)
    top_profile = (nr - 1 + 0.5) / nr
    source_top = jnp.sum(jnp.where(noise_hot, noise_table, 0.0), axis=2) * top_profile

    a0 = adjoint_in[0]
    push = -step_dt * stiffness * a0
    stack_f = jnp.stack([a0, adjoint_in[1], adjoint_in[2], adjoint_in[3], axial_flow, swirl_flow, buoyancy, push])
    top, below = nr - 1, nr - 2
    planes = [
        acoustic[0, :, :, top],
        acoustic[0, :, :, below],
        acoustic[1, :, :, top],
        acoustic[2, :, :, top],
        acoustic[3, :, :, below],
        axial_flow[:, :, top],
        axial_flow[:, :, below],
        swirl_flow[:, :, top],
        swirl_flow[:, :, below],
        buoyancy[:, :, top],
        buoyancy[:, :, below],
        stiffness[:, :, top],
        wall,
        source_top,
    ]
    stack_c = jnp.stack(planes)
    n_planes = len(planes)
    tile = 8
    reach = 3
    packed = jnp.pad(jnp.transpose(stack_c, (1, 2, 0)), ((0, 0), (0, 0), (0, nr - n_planes)))
    stack_all = jnp.concatenate([stack_f, packed[None]], axis=0)
    n_f = stack_f.shape[0]
    widened = with_halo(stack_all, "ax", 2, tile, tile, False)
    size_az, length_a = (lax.axis_size("az"), widened.shape[1])
    up = [(i, (i + 1) % size_az) for i in range(size_az)]
    down = [(j, i) for i, j in up]
    sent_up = jnp.stack(
        [widened[f, length_a - 1] for f in (0, 1, 2, 3, 5, 6, 7)]
        + [widened[n_f, length_a - reach + k] for k in range(reach)]
    )
    sent_down = jnp.stack(
        [widened[f, 0] for f in (0, 1, 2, 3, 5, 7)] + [widened[7, 1]] + [widened[n_f, k] for k in range(reach)]
    )
    from_below = lax.ppermute(sent_up, "az", up)
    from_above = lax.ppermute(sent_down, "az", down)
    blank = jnp.zeros_like(from_below[0])
    row_before = jnp.stack([from_below[i] for i in (0, 1, 2, 3)] + [blank] + [from_below[i] for i in (4, 5, 6)])
    row_after = jnp.stack([from_above[i] for i in (0, 1, 2, 3)] + [blank, from_above[4], blank, from_above[5]])
    row_after2 = jnp.stack([blank] * 7 + [from_above[6]])
    wide_f = jnp.concatenate(
        [row_before[:, None], widened[:n_f], row_after[:, None], row_after2[:, None]], axis=1
    )
    wide_packed = jnp.concatenate([from_below[7:], widened[n_f], from_above[7:]], axis=0)
    wide_c = jnp.transpose(wide_packed[:, :, :n_planes], (2, 0, 1))

    oc = (reach, tile)
    p_t, p_b, va_t, vx_t, vr_b, u_t, u_b, w_t, w_b, b_t, b_b, s_t, wall_c, src_c = [wide_c[i] for i in range(14)]
    ea, ex = na + 3, nx + 3

    def c(f, da, dx, la, lx):
        return win(f, oc, da, dx, la, lx)

    def advect_c(f, u, w, da, dx, la, lx):
        return c(u, da, dx, la, lx) * (c(f, da, dx + 1, la, lx) - c(f, da, dx - 1, la, lx)) * 0.5 + c(
            w, da, dx, la, lx
        ) * (c(f, da + 1, dx, la, lx) - c(f, da - 1, dx, la, lx)) * 0.5

    new_az = c(va_t, -2, -1, ea + 1, ex) - step_dt * (
        advect_c(va_t, u_t, w_t, -2, -1, ea + 1, ex)
        + c(b_t, -2, -1, ea + 1, ex) * (c(p_t, -1, -1, ea + 1, ex) - c(p_t, -2, -1, ea + 1, ex))
    )
    new_ax = c(vx_t, -1, -2, ea, ex + 1) - step_dt * (
        advect_c(vx_t, u_t, w_t, -1, -2, ea, ex + 1)
        + c(b_t, -1, -2, ea, ex + 1) * (c(p_t, -1, -1, ea, ex + 1) - c(p_t, -1, -2, ea, ex + 1))
    )
    rad_top = c(wall_c, -1, -1, ea, ex) * c(p_t, -1, -1, ea, ex)
    rad_below = c(vr_b, -1, -1, ea, ex) - step_dt * (
        advect_c(vr_b, u_b, w_b, -1, -1, ea, ex)
        + c(b_b, -1, -1, ea, ex) * (c(p_t, -1, -1, ea, ex) - c(p_b, -1, -1, ea, ex))
    )
    spread = (new_az[1:] - new_az[:-1]) + (new_ax[:, 1:] - new_ax[:, :-1]) + (rad_top - rad_below)
    press_ring = (
        c(p_t, -1, -1, ea, ex)
        - step_dt * (advect_c(p_t, u_t, w_t, -1, -1, ea, ex) + c(s_t, -1, -1, ea, ex) * spread)
        + step_dt * c(src_c, -1, -1, ea, ex)
    )

    total_az = na * lax.axis_size("az")
    first_az = lax.axis_index("az") * na
    first_ax = lax.axis_index("ax") * nx
    ring_az = jnp.remainder(mic_az - first_az + 1, total_az)
    ring_ax = mic_ax - first_ax + 1
    on_ring = (ring_az < ea) & (ring_ax >= 0) & (ring_ax < ex)
    owned = (ring_az >= 1) & (ring_az <= na) & (ring_ax >= 1) & (ring_ax <= nx)
    ring_cell = jnp.where(on_ring, ring_az * ex + ring_ax, -1)
    cell_hot = ring_cell[:, None] == lax.broadcasted_iota(jnp.int32, (1, ea * ex), 1)
    heard = jnp.sum(jnp.where(cell_hot, press_ring.reshape(1, ea * ex), 0.0), axis=1)
    misses = heard - measured
    square_sum = jnp.sum(jnp.where(owned, misses * misses, 0.0))
    placed = jnp.sum(jnp.where(cell_hot, misses[:, None], 0.0), axis=0).reshape(ea, ex)

    of = (1, tile)
    g_a0, g_a1, g_a2, g_a3, g_u, g_w, g_b, g_push = [wide_f[i] for i in range(8)]

    def at(field, da, dx):
        return win(field, of, da, dx, na, nx)

    def head_az(da, dx):
        return at(g_a1, da, dx) + at(g_push, da, dx) - at(g_push, da + 1, dx)

    def head_ax(da, dx):
        return at(g_a2, da, dx) + at(g_push, da, dx) - at(g_push, da, dx + 1)

    casing = casing_mask((na, nx, nr))

    def head_rad(da, dx):
        push_here = at(g_push, da, dx)
        return at(g_a3, da, dx) + push_here - rad_next(push_here)

    def head_masked(da, dx):
        return jnp.where(casing, 0.0, head_rad(da, dx))

    def back_advect(head):
        return 0.5 * (at(g_u, 0, -1) * head(0, -1) - at(g_u, 0, 1) * head(0, 1)) + 0.5 * (
            at(g_w, -1, 0) * head(-1, 0) - at(g_w, 1, 0) * head(1, 0)
        )

    def seed(da, dx):
        return at(g_a0, da, dx)

    backs = [head(0, 0) - step_dt * back_advect(head) for head in (head_az, head_ax, head_masked)]
    shove_r = step_dt * at(g_b, 0, 0) * head_masked(0, 0)
    head_rad_own = head_rad(0, 0)
    back_press = (
        seed(0, 0)
        - step_dt * back_advect(seed)
        + (step_dt * at(g_b, 0, 0) * head_az(0, 0) - step_dt * at(g_b, -1, 0) * head_az(-1, 0))
        + (step_dt * at(g_b, 0, 0) * head_ax(0, 0) - step_dt * at(g_b, 0, -1) * head_ax(0, -1))
        + (shove_r - rad_prev(shove_r))
        + jnp.where(casing, wall[:, :, None] * head_rad_own, 0.0)
    )
    base = jnp.stack([back_press] + backs)

    late_rad, late_push, late_press, _ = lax.optimization_barrier((adjoint_in[3], push, acoustic[0], widened))
    press_top = late_press[:, :, top]
    sens_base = press_top * (late_rad[:, :, top] + late_push[:, :, top])
    sens_placed = press_top * (-step_dt * c(s_t, 0, 0, na, nx) * placed[1 : 1 + na, 1 : 1 + nx])
    slot = lax.broadcasted_iota(jnp.int32, (1, 1, 1 + 2 * nseg), 2)
    first_cell = (lax.broadcasted_iota(jnp.int32, (na, nx, 1), 0) == 0) & (
        lax.broadcasted_iota(jnp.int32, (na, nx, 1), 1) == 0
    )
    seg_here = segment_id[:, :, None]
    payload = jnp.sum(
        jnp.where(
            slot == 0,
            jnp.where(first_cell, square_sum, 0.0),
            jnp.where(
                slot <= nseg,
                jnp.where(seg_here == slot - 1, sens_base[:, :, None], 0.0),
                jnp.where(seg_here == slot - 1 - nseg, sens_placed[:, :, None], 0.0),
            ),
        ),
        axis=(0, 1),
    )

    size_az = lax.axis_size("az")
    first_round = payload + lax.ppermute(payload, "az", [(i, i ^ 1) for i in range(size_az)])
    placed, _ = lax.optimization_barrier((placed, first_round))
    push_e = -step_dt * c(s_t, -1, -1, ea, ex) * placed
    r1a, r1x = na + 2, nx + 2
    head_az_e = push_e[:r1a, :r1x] - push_e[1 : 1 + r1a, :r1x]
    head_ax_e = push_e[:r1a, :r1x] - push_e[:r1a, 1 : 1 + r1x]
    head_rad_e = -push_e[:r1a, :r1x]
    u_t1, w_t1 = c(u_t, -1, -1, r1a, r1x), c(w_t, -1, -1, r1a, r1x)
    u_b1, w_b1 = c(u_b, -1, -1, r1a, r1x), c(w_b, -1, -1, r1a, r1x)
    b_t1 = c(b_t, -1, -1, r1a, r1x)
    own_e = (slice(1, 1 + na), slice(1, 1 + nx))
    back_press_t = (
        placed[1 : 1 + na, 1 : 1 + nx]
        - step_dt * advect_back(u_t1 * placed[:r1a, :r1x], w_t1 * placed[:r1a, :r1x], na, nx)
    )
    shove_az = step_dt * b_t1 * head_az_e
    shove_ax = step_dt * b_t1 * head_ax_e
    b_b0, wall_0, push_0 = c(b_b, 0, 0, na, nx), c(wall_c, 0, 0, na, nx), push_e[own_e]
    back_press_t = (
        back_press_t
        + (shove_az[own_e] - shove_az[0:na, 1 : 1 + nx])
        + (shove_ax[own_e] - shove_ax[1 : 1 + na, 0:nx])
        + step_dt * b_b0 * push_0
        + wall_0 * push_0
    )
    back_press_b = -step_dt * b_b0 * push_0
    back_az_t = head_az_e[own_e] - step_dt * advect_back(u_t1 * head_az_e, w_t1 * head_az_e, na, nx)
    back_ax_t = head_ax_e[own_e] - step_dt * advect_back(u_t1 * head_ax_e, w_t1 * head_ax_e, na, nx)
    back_rad_b = head_rad_e[own_e] - step_dt * advect_back(u_b1 * head_rad_e, w_b1 * head_rad_e, na, nx)
    zero = jnp.zeros_like(back_press_b)
    extra = jnp.stack(
        [
            jnp.stack([back_press_b, back_press_t], axis=-1),
            jnp.stack([zero, back_az_t], axis=-1),
            jnp.stack([zero, back_ax_t], axis=-1),
            jnp.stack([back_rad_b, zero], axis=-1),
        ]
    )

    totals = butterfly_sum(first_round, ("az", "ax"), skip_first=True)
    mean_sq = totals[0] / mic_az.shape[0] + epsilon
    grad_scale = (na * lax.axis_size("az") * nx * lax.axis_size("ax") / nseg) ** (-0.5)
    liner_grad = (totals[1 : 1 + nseg] + totals[1 + nseg :] / mean_sq) * grad_scale
    misfit = 0.5 * jnp.log(mean_sq)
    lane = lax.broadcasted_iota(jnp.int32, (1, 1, 1, nr), 3)
    extra_scaled = extra / mean_sq
    correction = jnp.where(
        lane == nr - 1,
        extra_scaled[..., 1:2],
        jnp.where(lane == nr - 2, extra_scaled[..., 0:1], 0.0),
    )
    adjoint_out = base + correction
    return (adjoint_out, liner_grad, misfit)


def solution(mesh):
    placed = (
        P(None, "az", "ax", None),
        P(None, "az", "ax", None),
        P(None, "az", "ax", None),
        P(),
        P("az", "ax"),
        P("az", "ax"),
        P(),
        P(),
        P(),
        P(),
    )
    return jax.shard_map(
        shards,
        mesh=mesh,
        in_specs=placed,
        out_specs=(P(None, "az", "ax", None), P(), P()),
        check_vma=False,
    )
```

```python
import jax
import jax.numpy as jnp
from jax import lax
from jax.sharding import PartitionSpec as P

step_dt = 0.25
epsilon = 1e-06


def with_halo(array, axis, dim, before, after, wrap):
    size, length = (lax.axis_size(axis), array.shape[dim])
    up = [(i, (i + 1) % size) for i in range(size if wrap else size - 1)]
    down = [(j, i) for i, j in up]
    parts = []
    if before:
        parts.append(lax.ppermute(lax.slice_in_dim(array, length - before, length, axis=dim), axis, up))
    parts.append(array)
    if after:
        parts.append(lax.ppermute(lax.slice_in_dim(array, 0, after, axis=dim), axis, down))
    return jnp.concatenate(parts, axis=dim)


def exchange(array, before, after, ax_before=None, ax_after=None):
    ax_before = before if ax_before is None else ax_before
    ax_after = after if ax_after is None else ax_after
    widened = with_halo(array, "ax", 2, ax_before, ax_after, False)
    return with_halo(widened, "az", 1, before, after, True)


def win(values, origin, da, dx, na, nx):
    a0, x0 = origin[0] + da, origin[1] + dx
    return values[a0 : a0 + na, x0 : x0 + nx]


def rad_next(values):
    return jnp.concatenate([values[..., 1:], jnp.zeros_like(values[..., :1])], axis=-1)


def rad_prev(values):
    return jnp.concatenate([jnp.zeros_like(values[..., :1]), values[..., :-1]], axis=-1)


def casing_mask(shape):
    return lax.broadcasted_iota(jnp.int32, shape, len(shape) - 1) == shape[-1] - 1


def advect_back(carried_ax, carried_az, na, nx):
    return 0.5 * (carried_ax[..., 1 : 1 + na, 0:nx] - carried_ax[..., 1 : 1 + na, 2 : 2 + nx]) + 0.5 * (
        carried_az[..., 0:na, 1 : 1 + nx] - carried_az[..., 2 : 2 + na, 1 : 1 + nx]
    )


def advect_back4(carried_ax, carried_az, na, nx):
    return 0.5 * (carried_ax[:, 1 : 1 + na, 0:nx, :] - carried_ax[:, 1 : 1 + na, 2 : 2 + nx, :]) + 0.5 * (
        carried_az[:, 0:na, 1 : 1 + nx, :] - carried_az[:, 2 : 2 + na, 1 : 1 + nx, :]
    )


def butterfly_sum(values, axes, skip_first=False):
    for index, axis in enumerate(axes):
        size = lax.axis_size(axis)
        if size & (size - 1):
            values = lax.psum(values, axis)
            continue
        step = 2 if (skip_first and index == 0) else 1
        while step < size:
            values = values + lax.ppermute(values, axis, [(i, i ^ step) for i in range(size)])
            step *= 2
    return values


def shards(
    acoustic,
    mean_flow,
    adjoint_in,
    admittance,
    segment_id,
    noise_code,
    noise_table,
    mic_az,
    mic_ax,
    measured,
):
    na, nx, nr = (acoustic.shape[1], acoustic.shape[2], acoustic.shape[3])
    nseg = admittance.shape[0]
    buoyancy = 1.0 / mean_flow[2]
    stiffness = mean_flow[2] * mean_flow[3] * mean_flow[3]
    axial_flow, swirl_flow = (mean_flow[0], mean_flow[1])

    segment_hot = segment_id[:, :, None] == lax.broadcasted_iota(jnp.int32, (1, 1, nseg), 2)
    wall = jnp.sum(jnp.where(segment_hot, admittance, 0.0), axis=2)
    noise_hot = noise_code[:, :, None] == lax.broadcasted_iota(jnp.int32, (1, 1, noise_table.shape[0]), 2)
    top_profile = (nr - 1 + 0.5) / nr
    source_top = jnp.sum(jnp.where(noise_hot, noise_table, 0.0), axis=2) * top_profile

    a0 = adjoint_in[0]
    push = -step_dt * stiffness * a0
    stack_f = jnp.stack([a0, adjoint_in[1], adjoint_in[2], adjoint_in[3], axial_flow, swirl_flow, buoyancy, push])
    top, below = nr - 1, nr - 2
    planes = [
        acoustic[0, :, :, top],
        acoustic[0, :, :, below],
        acoustic[1, :, :, top],
        acoustic[2, :, :, top],
        acoustic[3, :, :, below],
        axial_flow[:, :, top],
        axial_flow[:, :, below],
        swirl_flow[:, :, top],
        swirl_flow[:, :, below],
        buoyancy[:, :, top],
        buoyancy[:, :, below],
        stiffness[:, :, top],
        wall,
        source_top,
    ]
    stack_c = jnp.stack(planes)
    n_planes = len(planes)
    tile = 8
    reach = 3
    packed = jnp.pad(jnp.transpose(stack_c, (1, 2, 0)), ((0, 0), (0, 0), (0, nr - n_planes)))
    stack_all = jnp.concatenate([stack_f, packed[None]], axis=0)
    n_f = stack_f.shape[0]
    sent_x = jnp.concatenate([stack_all[:5], stack_all[6:]], axis=0)
    size_ax = lax.axis_size("ax")
    right = [(i, i + 1) for i in range(size_ax - 1)]
    left = [(j, i) for i, j in right]
    length_x = stack_all.shape[2]
    x_before = lax.ppermute(sent_x[:, :, length_x - tile :], "ax", right)
    x_after = lax.ppermute(sent_x[:, :, :tile], "ax", left)
    no_w = jnp.zeros_like(x_before[:1])
    x_before = jnp.concatenate([x_before[:5], no_w, x_before[5:]], axis=0)
    x_after = jnp.concatenate([x_after[:5], no_w, x_after[5:]], axis=0)
    widened = jnp.concatenate([x_before, stack_all, x_after], axis=2)
    size_az, length_a = (lax.axis_size("az"), widened.shape[1])
    up = [(i, (i + 1) % size_az) for i in range(size_az)]
    down = [(j, i) for i, j in up]
    sent_up = jnp.stack(
        [widened[f, length_a - 1] for f in (0, 1, 2, 3, 5, 6, 7)]
        + [widened[n_f, length_a - reach + k] for k in range(reach)]
    )
    sent_down = jnp.stack(
        [widened[f, 0] for f in (0, 1, 2, 3, 5, 7)] + [widened[7, 1]] + [widened[n_f, k] for k in range(reach)]
    )
    from_below = lax.ppermute(sent_up, "az", up)
    from_above = lax.ppermute(sent_down, "az", down)
    blank = jnp.zeros_like(from_below[0])
    row_before = jnp.stack([from_below[i] for i in (0, 1, 2, 3)] + [blank] + [from_below[i] for i in (4, 5, 6)])
    row_after = jnp.stack([from_above[i] for i in (0, 1, 2, 3)] + [blank, from_above[4], blank, from_above[5]])
    row_after2 = jnp.stack([blank] * 7 + [from_above[6]])
    wide_f = jnp.concatenate(
        [row_before[:, None], widened[:n_f], row_after[:, None], row_after2[:, None]], axis=1
    )
    wide_packed = jnp.concatenate([from_below[7:], widened[n_f], from_above[7:]], axis=0)
    wide_c = jnp.transpose(wide_packed[:, :, :n_planes], (2, 0, 1))

    oc = (reach, tile)
    p_t, p_b, va_t, vx_t, vr_b, u_t, u_b, w_t, w_b, b_t, b_b, s_t, wall_c, src_c = [wide_c[i] for i in range(14)]
    ea, ex = na + 3, nx + 3

    def c(f, da, dx, la, lx):
        return win(f, oc, da, dx, la, lx)

    def advect_c(f, u, w, da, dx, la, lx):
        return c(u, da, dx, la, lx) * (c(f, da, dx + 1, la, lx) - c(f, da, dx - 1, la, lx)) * 0.5 + c(
            w, da, dx, la, lx
        ) * (c(f, da + 1, dx, la, lx) - c(f, da - 1, dx, la, lx)) * 0.5

    new_az = c(va_t, -2, -1, ea + 1, ex) - step_dt * (
        advect_c(va_t, u_t, w_t, -2, -1, ea + 1, ex)
        + c(b_t, -2, -1, ea + 1, ex) * (c(p_t, -1, -1, ea + 1, ex) - c(p_t, -2, -1, ea + 1, ex))
    )
    new_ax = c(vx_t, -1, -2, ea, ex + 1) - step_dt * (
        advect_c(vx_t, u_t, w_t, -1, -2, ea, ex + 1)
        + c(b_t, -1, -2, ea, ex + 1) * (c(p_t, -1, -1, ea, ex + 1) - c(p_t, -1, -2, ea, ex + 1))
    )
    rad_top = c(wall_c, -1, -1, ea, ex) * c(p_t, -1, -1, ea, ex)
    rad_below = c(vr_b, -1, -1, ea, ex) - step_dt * (
        advect_c(vr_b, u_b, w_b, -1, -1, ea, ex)
        + c(b_b, -1, -1, ea, ex) * (c(p_t, -1, -1, ea, ex) - c(p_b, -1, -1, ea, ex))
    )
    spread = (new_az[1:] - new_az[:-1]) + (new_ax[:, 1:] - new_ax[:, :-1]) + (rad_top - rad_below)
    press_ring = (
        c(p_t, -1, -1, ea, ex)
        - step_dt * (advect_c(p_t, u_t, w_t, -1, -1, ea, ex) + c(s_t, -1, -1, ea, ex) * spread)
        + step_dt * c(src_c, -1, -1, ea, ex)
    )

    total_az = na * lax.axis_size("az")
    first_az = lax.axis_index("az") * na
    first_ax = lax.axis_index("ax") * nx
    ring_az = jnp.remainder(mic_az - first_az + 1, total_az)
    ring_ax = mic_ax - first_ax + 1
    on_ring = (ring_az < ea) & (ring_ax >= 0) & (ring_ax < ex)
    owned = (ring_az >= 1) & (ring_az <= na) & (ring_ax >= 1) & (ring_ax <= nx)
    ring_cell = jnp.where(on_ring, ring_az * ex + ring_ax, -1)
    cell_hot = ring_cell[:, None] == lax.broadcasted_iota(jnp.int32, (1, ea * ex), 1)
    heard = jnp.sum(jnp.where(cell_hot, press_ring.reshape(1, ea * ex), 0.0), axis=1)
    misses = heard - measured
    square_sum = jnp.sum(jnp.where(owned, misses * misses, 0.0))
    placed = jnp.sum(jnp.where(cell_hot, misses[:, None], 0.0), axis=0).reshape(ea, ex)

    of = (1, tile)
    g_a0, g_a1, g_a2, g_a3, g_u, g_w, g_b, g_push = [wide_f[i] for i in range(8)]

    def at(field, da, dx):
        return win(field, of, da, dx, na, nx)

    def head_az(da, dx):
        return at(g_a1, da, dx) + at(g_push, da, dx) - at(g_push, da + 1, dx)

    def head_ax(da, dx):
        return at(g_a2, da, dx) + at(g_push, da, dx) - at(g_push, da, dx + 1)

    casing = casing_mask((na, nx, nr))

    def head_rad(da, dx):
        push_here = at(g_push, da, dx)
        return at(g_a3, da, dx) + push_here - rad_next(push_here)

    def head_masked(da, dx):
        return jnp.where(casing, 0.0, head_rad(da, dx))

    def back_advect(head):
        return 0.5 * (at(g_u, 0, -1) * head(0, -1) - at(g_u, 0, 1) * head(0, 1)) + 0.5 * (
            at(g_w, -1, 0) * head(-1, 0) - at(g_w, 1, 0) * head(1, 0)
        )

    def seed(da, dx):
        return at(g_a0, da, dx)

    backs = [head(0, 0) - step_dt * back_advect(head) for head in (head_az, head_ax, head_masked)]
    shove_r = step_dt * at(g_b, 0, 0) * head_masked(0, 0)
    head_rad_own = head_rad(0, 0)
    back_press = (
        seed(0, 0)
        - step_dt * back_advect(seed)
        + (step_dt * at(g_b, 0, 0) * head_az(0, 0) - step_dt * at(g_b, -1, 0) * head_az(-1, 0))
        + (step_dt * at(g_b, 0, 0) * head_ax(0, 0) - step_dt * at(g_b, 0, -1) * head_ax(0, -1))
        + (shove_r - rad_prev(shove_r))
        + jnp.where(casing, wall[:, :, None] * head_rad_own, 0.0)
    )
    base = jnp.stack([back_press] + backs)

    late_rad, late_push, late_press, _ = lax.optimization_barrier((adjoint_in[3], push, acoustic[0], widened))
    press_top = late_press[:, :, top]
    sens_base = press_top * (late_rad[:, :, top] + late_push[:, :, top])
    sens_placed = press_top * (-step_dt * c(s_t, 0, 0, na, nx) * placed[1 : 1 + na, 1 : 1 + nx])
    slot = lax.broadcasted_iota(jnp.int32, (1, 1, 1 + 2 * nseg), 2)
    first_cell = (lax.broadcasted_iota(jnp.int32, (na, nx, 1), 0) == 0) & (
        lax.broadcasted_iota(jnp.int32, (na, nx, 1), 1) == 0
    )
    seg_here = segment_id[:, :, None]
    payload = jnp.sum(
        jnp.where(
            slot == 0,
            jnp.where(first_cell, square_sum, 0.0),
            jnp.where(
                slot <= nseg,
                jnp.where(seg_here == slot - 1, sens_base[:, :, None], 0.0),
                jnp.where(seg_here == slot - 1 - nseg, sens_placed[:, :, None], 0.0),
            ),
        ),
        axis=(0, 1),
    )

    size_az = lax.axis_size("az")
    first_round = payload + lax.ppermute(payload, "az", [(i, i ^ 1) for i in range(size_az)])
    placed, _ = lax.optimization_barrier((placed, first_round))
    push_e = -step_dt * c(s_t, -1, -1, ea, ex) * placed
    r1a, r1x = na + 2, nx + 2
    head_az_e = push_e[:r1a, :r1x] - push_e[1 : 1 + r1a, :r1x]
    head_ax_e = push_e[:r1a, :r1x] - push_e[:r1a, 1 : 1 + r1x]
    head_rad_e = -push_e[:r1a, :r1x]
    u_t1, w_t1 = c(u_t, -1, -1, r1a, r1x), c(w_t, -1, -1, r1a, r1x)
    u_b1, w_b1 = c(u_b, -1, -1, r1a, r1x), c(w_b, -1, -1, r1a, r1x)
    b_t1 = c(b_t, -1, -1, r1a, r1x)
    own_e = (slice(1, 1 + na), slice(1, 1 + nx))
    back_press_t = (
        placed[1 : 1 + na, 1 : 1 + nx]
        - step_dt * advect_back(u_t1 * placed[:r1a, :r1x], w_t1 * placed[:r1a, :r1x], na, nx)
    )
    shove_az = step_dt * b_t1 * head_az_e
    shove_ax = step_dt * b_t1 * head_ax_e
    b_b0, wall_0, push_0 = c(b_b, 0, 0, na, nx), c(wall_c, 0, 0, na, nx), push_e[own_e]
    back_press_t = (
        back_press_t
        + (shove_az[own_e] - shove_az[0:na, 1 : 1 + nx])
        + (shove_ax[own_e] - shove_ax[1 : 1 + na, 0:nx])
        + step_dt * b_b0 * push_0
        + wall_0 * push_0
    )
    back_press_b = -step_dt * b_b0 * push_0
    back_az_t = head_az_e[own_e] - step_dt * advect_back(u_t1 * head_az_e, w_t1 * head_az_e, na, nx)
    back_ax_t = head_ax_e[own_e] - step_dt * advect_back(u_t1 * head_ax_e, w_t1 * head_ax_e, na, nx)
    back_rad_b = head_rad_e[own_e] - step_dt * advect_back(u_b1 * head_rad_e, w_b1 * head_rad_e, na, nx)
    zero = jnp.zeros_like(back_press_b)
    extra = jnp.stack(
        [
            jnp.stack([back_press_b, back_press_t], axis=-1),
            jnp.stack([zero, back_az_t], axis=-1),
            jnp.stack([zero, back_ax_t], axis=-1),
            jnp.stack([back_rad_b, zero], axis=-1),
        ]
    )

    totals = butterfly_sum(first_round, ("az", "ax"), skip_first=True)
    mean_sq = totals[0] / mic_az.shape[0] + epsilon
    grad_scale = (na * lax.axis_size("az") * nx * lax.axis_size("ax") / nseg) ** (-0.5)
    liner_grad = (totals[1 : 1 + nseg] + totals[1 + nseg :] / mean_sq) * grad_scale
    misfit = 0.5 * jnp.log(mean_sq)
    lane = lax.broadcasted_iota(jnp.int32, (1, 1, 1, nr), 3)
    extra_scaled = extra / mean_sq
    correction = jnp.where(
        lane == nr - 1,
        extra_scaled[..., 1:2],
        jnp.where(lane == nr - 2, extra_scaled[..., 0:1], 0.0),
    )
    adjoint_out = base + correction
    return (adjoint_out, liner_grad, misfit)


def solution(mesh):
    placed = (
        P(None, "az", "ax", None),
        P(None, "az", "ax", None),
        P(None, "az", "ax", None),
        P(),
        P("az", "ax"),
        P("az", "ax"),
        P(),
        P(),
        P(),
        P(),
    )
    return jax.shard_map(
        shards,
        mesh=mesh,
        in_specs=placed,
        out_specs=(P(None, "az", "ax", None), P(), P()),
        check_vma=False,
    )
```

```python
import jax
import jax.numpy as jnp
from jax import lax
from jax.sharding import PartitionSpec as P

step_dt = 0.25
epsilon = 1e-06


def with_halo(array, axis, dim, before, after, wrap):
    size, length = (lax.axis_size(axis), array.shape[dim])
    up = [(i, (i + 1) % size) for i in range(size if wrap else size - 1)]
    down = [(j, i) for i, j in up]
    parts = []
    if before:
        parts.append(lax.ppermute(lax.slice_in_dim(array, length - before, length, axis=dim), axis, up))
    parts.append(array)
    if after:
        parts.append(lax.ppermute(lax.slice_in_dim(array, 0, after, axis=dim), axis, down))
    return jnp.concatenate(parts, axis=dim)


def exchange(array, before, after, ax_before=None, ax_after=None):
    ax_before = before if ax_before is None else ax_before
    ax_after = after if ax_after is None else ax_after
    widened = with_halo(array, "ax", 2, ax_before, ax_after, False)
    return with_halo(widened, "az", 1, before, after, True)


def win(values, origin, da, dx, na, nx):
    a0, x0 = origin[0] + da, origin[1] + dx
    return values[a0 : a0 + na, x0 : x0 + nx]


def rad_next(values):
    return jnp.concatenate([values[..., 1:], jnp.zeros_like(values[..., :1])], axis=-1)


def rad_prev(values):
    return jnp.concatenate([jnp.zeros_like(values[..., :1]), values[..., :-1]], axis=-1)


def casing_mask(shape):
    return lax.broadcasted_iota(jnp.int32, shape, len(shape) - 1) == shape[-1] - 1


def advect_back(carried_ax, carried_az, na, nx):
    return 0.5 * (carried_ax[..., 1 : 1 + na, 0:nx] - carried_ax[..., 1 : 1 + na, 2 : 2 + nx]) + 0.5 * (
        carried_az[..., 0:na, 1 : 1 + nx] - carried_az[..., 2 : 2 + na, 1 : 1 + nx]
    )


def advect_back4(carried_ax, carried_az, na, nx):
    return 0.5 * (carried_ax[:, 1 : 1 + na, 0:nx, :] - carried_ax[:, 1 : 1 + na, 2 : 2 + nx, :]) + 0.5 * (
        carried_az[:, 0:na, 1 : 1 + nx, :] - carried_az[:, 2 : 2 + na, 1 : 1 + nx, :]
    )


def butterfly_sum(values, axes, skip_first=False):
    for index, axis in enumerate(axes):
        size = lax.axis_size(axis)
        if size & (size - 1):
            values = lax.psum(values, axis)
            continue
        step = 2 if (skip_first and index == 0) else 1
        while step < size:
            values = values + lax.ppermute(values, axis, [(i, i ^ step) for i in range(size)])
            step *= 2
    return values


def shards(
    acoustic,
    mean_flow,
    adjoint_in,
    admittance,
    segment_id,
    noise_code,
    noise_table,
    mic_az,
    mic_ax,
    measured,
):
    na, nx, nr = (acoustic.shape[1], acoustic.shape[2], acoustic.shape[3])
    nseg = admittance.shape[0]
    buoyancy = 1.0 / mean_flow[2]
    stiffness = mean_flow[2] * mean_flow[3] * mean_flow[3]
    axial_flow, swirl_flow = (mean_flow[0], mean_flow[1])

    segment_hot = segment_id[:, :, None] == lax.broadcasted_iota(jnp.int32, (1, 1, nseg), 2)
    wall = jnp.sum(jnp.where(segment_hot, admittance, 0.0), axis=2)
    noise_hot = noise_code[:, :, None] == lax.broadcasted_iota(jnp.int32, (1, 1, noise_table.shape[0]), 2)
    top_profile = (nr - 1 + 0.5) / nr
    source_top = jnp.sum(jnp.where(noise_hot, noise_table, 0.0), axis=2) * top_profile

    a0 = adjoint_in[0]
    push = -step_dt * stiffness * a0
    stack_f = jnp.stack([a0, adjoint_in[1], adjoint_in[2], adjoint_in[3], axial_flow, swirl_flow, buoyancy, push])
    top, below = nr - 1, nr - 2
    planes = [
        acoustic[0, :, :, top],
        acoustic[0, :, :, below],
        acoustic[1, :, :, top],
        acoustic[2, :, :, top],
        acoustic[3, :, :, below],
        axial_flow[:, :, top],
        axial_flow[:, :, below],
        swirl_flow[:, :, top],
        swirl_flow[:, :, below],
        buoyancy[:, :, top],
        buoyancy[:, :, below],
        stiffness[:, :, top],
        wall,
        source_top,
    ]
    stack_c = jnp.stack(planes)
    n_planes = len(planes)
    tile = 8
    reach = 3
    packed = jnp.pad(jnp.transpose(stack_c, (1, 2, 0)), ((0, 0), (0, 0), (0, nr - n_planes)))
    stack_all = jnp.concatenate([stack_f, packed[None]], axis=0)
    n_f = stack_f.shape[0]
    sent_x = jnp.concatenate([stack_all[:5], stack_all[6:]], axis=0)
    size_ax = lax.axis_size("ax")
    right = [(i, i + 1) for i in range(size_ax - 1)]
    left = [(j, i) for i, j in right]
    length_x = stack_all.shape[2]
    x_before = lax.ppermute(sent_x[:, :, length_x - tile :], "ax", right)
    x_after = lax.ppermute(jnp.concatenate([sent_x[:5, :, :tile], sent_x[6:, :, :tile]]), "ax", left)
    no_w = jnp.zeros_like(x_before[:1])
    x_before = jnp.concatenate([x_before[:5], no_w, x_before[5:]], axis=0)
    x_after = jnp.concatenate([x_after[:5], no_w, no_w, x_after[5:]], axis=0)
    widened = jnp.concatenate([x_before, stack_all, x_after], axis=2)
    size_az, length_a = (lax.axis_size("az"), widened.shape[1])
    up = [(i, (i + 1) % size_az) for i in range(size_az)]
    down = [(j, i) for i, j in up]
    sent_up = jnp.stack(
        [widened[f, length_a - 1] for f in (0, 1, 2, 3, 5, 6, 7)]
        + [widened[n_f, length_a - reach + k] for k in range(reach)]
    )
    sent_down = jnp.stack(
        [widened[f, 0] for f in (0, 1, 2, 3, 5, 7)] + [widened[7, 1]] + [widened[n_f, k] for k in range(reach)]
    )
    from_below = lax.ppermute(sent_up, "az", up)
    from_above = lax.ppermute(sent_down, "az", down)
    blank = jnp.zeros_like(from_below[0])
    row_before = jnp.stack([from_below[i] for i in (0, 1, 2, 3)] + [blank] + [from_below[i] for i in (4, 5, 6)])
    row_after = jnp.stack([from_above[i] for i in (0, 1, 2, 3)] + [blank, from_above[4], blank, from_above[5]])
    row_after2 = jnp.stack([blank] * 7 + [from_above[6]])
    wide_f = jnp.concatenate(
        [row_before[:, None], widened[:n_f], row_after[:, None], row_after2[:, None]], axis=1
    )
    wide_packed = jnp.concatenate([from_below[7:], widened[n_f], from_above[7:]], axis=0)
    wide_c = jnp.transpose(wide_packed[:, :, :n_planes], (2, 0, 1))

    oc = (reach, tile)
    p_t, p_b, va_t, vx_t, vr_b, u_t, u_b, w_t, w_b, b_t, b_b, s_t, wall_c, src_c = [wide_c[i] for i in range(14)]
    ea, ex = na + 3, nx + 3

    def c(f, da, dx, la, lx):
        return win(f, oc, da, dx, la, lx)

    def advect_c(f, u, w, da, dx, la, lx):
        return c(u, da, dx, la, lx) * (c(f, da, dx + 1, la, lx) - c(f, da, dx - 1, la, lx)) * 0.5 + c(
            w, da, dx, la, lx
        ) * (c(f, da + 1, dx, la, lx) - c(f, da - 1, dx, la, lx)) * 0.5

    new_az = c(va_t, -2, -1, ea + 1, ex) - step_dt * (
        advect_c(va_t, u_t, w_t, -2, -1, ea + 1, ex)
        + c(b_t, -2, -1, ea + 1, ex) * (c(p_t, -1, -1, ea + 1, ex) - c(p_t, -2, -1, ea + 1, ex))
    )
    new_ax = c(vx_t, -1, -2, ea, ex + 1) - step_dt * (
        advect_c(vx_t, u_t, w_t, -1, -2, ea, ex + 1)
        + c(b_t, -1, -2, ea, ex + 1) * (c(p_t, -1, -1, ea, ex + 1) - c(p_t, -1, -2, ea, ex + 1))
    )
    rad_top = c(wall_c, -1, -1, ea, ex) * c(p_t, -1, -1, ea, ex)
    rad_below = c(vr_b, -1, -1, ea, ex) - step_dt * (
        advect_c(vr_b, u_b, w_b, -1, -1, ea, ex)
        + c(b_b, -1, -1, ea, ex) * (c(p_t, -1, -1, ea, ex) - c(p_b, -1, -1, ea, ex))
    )
    spread = (new_az[1:] - new_az[:-1]) + (new_ax[:, 1:] - new_ax[:, :-1]) + (rad_top - rad_below)
    press_ring = (
        c(p_t, -1, -1, ea, ex)
        - step_dt * (advect_c(p_t, u_t, w_t, -1, -1, ea, ex) + c(s_t, -1, -1, ea, ex) * spread)
        + step_dt * c(src_c, -1, -1, ea, ex)
    )

    total_az = na * lax.axis_size("az")
    first_az = lax.axis_index("az") * na
    first_ax = lax.axis_index("ax") * nx
    ring_az = jnp.remainder(mic_az - first_az + 1, total_az)
    ring_ax = mic_ax - first_ax + 1
    on_ring = (ring_az < ea) & (ring_ax >= 0) & (ring_ax < ex)
    owned = (ring_az >= 1) & (ring_az <= na) & (ring_ax >= 1) & (ring_ax <= nx)
    ring_cell = jnp.where(on_ring, ring_az * ex + ring_ax, -1)
    cell_hot = ring_cell[:, None] == lax.broadcasted_iota(jnp.int32, (1, ea * ex), 1)
    heard = jnp.sum(jnp.where(cell_hot, press_ring.reshape(1, ea * ex), 0.0), axis=1)
    misses = heard - measured
    square_sum = jnp.sum(jnp.where(owned, misses * misses, 0.0))
    placed = jnp.sum(jnp.where(cell_hot, misses[:, None], 0.0), axis=0).reshape(ea, ex)

    of = (1, tile)
    g_a0, g_a1, g_a2, g_a3, g_u, g_w, g_b, g_push = [wide_f[i] for i in range(8)]

    def at(field, da, dx):
        return win(field, of, da, dx, na, nx)

    def head_az(da, dx):
        return at(g_a1, da, dx) + at(g_push, da, dx) - at(g_push, da + 1, dx)

    def head_ax(da, dx):
        return at(g_a2, da, dx) + at(g_push, da, dx) - at(g_push, da, dx + 1)

    casing = casing_mask((na, nx, nr))

    def head_rad(da, dx):
        push_here = at(g_push, da, dx)
        return at(g_a3, da, dx) + push_here - rad_next(push_here)

    def head_masked(da, dx):
        return jnp.where(casing, 0.0, head_rad(da, dx))

    def back_advect(head):
        return 0.5 * (at(g_u, 0, -1) * head(0, -1) - at(g_u, 0, 1) * head(0, 1)) + 0.5 * (
            at(g_w, -1, 0) * head(-1, 0) - at(g_w, 1, 0) * head(1, 0)
        )

    def seed(da, dx):
        return at(g_a0, da, dx)

    backs = [head(0, 0) - step_dt * back_advect(head) for head in (head_az, head_ax, head_masked)]
    shove_r = step_dt * at(g_b, 0, 0) * head_masked(0, 0)
    head_rad_own = head_rad(0, 0)
    back_press = (
        seed(0, 0)
        - step_dt * back_advect(seed)
        + (step_dt * at(g_b, 0, 0) * head_az(0, 0) - step_dt * at(g_b, -1, 0) * head_az(-1, 0))
        + (step_dt * at(g_b, 0, 0) * head_ax(0, 0) - step_dt * at(g_b, 0, -1) * head_ax(0, -1))
        + (shove_r - rad_prev(shove_r))
        + jnp.where(casing, wall[:, :, None] * head_rad_own, 0.0)
    )
    base = jnp.stack([back_press] + backs)

    late_rad, late_push, late_press, _ = lax.optimization_barrier((adjoint_in[3], push, acoustic[0], widened))
    press_top = late_press[:, :, top]
    sens_base = press_top * (late_rad[:, :, top] + late_push[:, :, top])
    sens_placed = press_top * (-step_dt * c(s_t, 0, 0, na, nx) * placed[1 : 1 + na, 1 : 1 + nx])
    slot = lax.broadcasted_iota(jnp.int32, (1, 1, 1 + 2 * nseg), 2)
    first_cell = (lax.broadcasted_iota(jnp.int32, (na, nx, 1), 0) == 0) & (
        lax.broadcasted_iota(jnp.int32, (na, nx, 1), 1) == 0
    )
    seg_here = segment_id[:, :, None]
    payload = jnp.sum(
        jnp.where(
            slot == 0,
            jnp.where(first_cell, square_sum, 0.0),
            jnp.where(
                slot <= nseg,
                jnp.where(seg_here == slot - 1, sens_base[:, :, None], 0.0),
                jnp.where(seg_here == slot - 1 - nseg, sens_placed[:, :, None], 0.0),
            ),
        ),
        axis=(0, 1),
    )

    size_az = lax.axis_size("az")
    first_round = payload + lax.ppermute(payload, "az", [(i, i ^ 1) for i in range(size_az)])
    placed, _ = lax.optimization_barrier((placed, first_round))
    push_e = -step_dt * c(s_t, -1, -1, ea, ex) * placed
    r1a, r1x = na + 2, nx + 2
    head_az_e = push_e[:r1a, :r1x] - push_e[1 : 1 + r1a, :r1x]
    head_ax_e = push_e[:r1a, :r1x] - push_e[:r1a, 1 : 1 + r1x]
    head_rad_e = -push_e[:r1a, :r1x]
    u_t1, w_t1 = c(u_t, -1, -1, r1a, r1x), c(w_t, -1, -1, r1a, r1x)
    u_b1, w_b1 = c(u_b, -1, -1, r1a, r1x), c(w_b, -1, -1, r1a, r1x)
    b_t1 = c(b_t, -1, -1, r1a, r1x)
    own_e = (slice(1, 1 + na), slice(1, 1 + nx))
    back_press_t = (
        placed[1 : 1 + na, 1 : 1 + nx]
        - step_dt * advect_back(u_t1 * placed[:r1a, :r1x], w_t1 * placed[:r1a, :r1x], na, nx)
    )
    shove_az = step_dt * b_t1 * head_az_e
    shove_ax = step_dt * b_t1 * head_ax_e
    b_b0, wall_0, push_0 = c(b_b, 0, 0, na, nx), c(wall_c, 0, 0, na, nx), push_e[own_e]
    back_press_t = (
        back_press_t
        + (shove_az[own_e] - shove_az[0:na, 1 : 1 + nx])
        + (shove_ax[own_e] - shove_ax[1 : 1 + na, 0:nx])
        + step_dt * b_b0 * push_0
        + wall_0 * push_0
    )
    back_press_b = -step_dt * b_b0 * push_0
    back_az_t = head_az_e[own_e] - step_dt * advect_back(u_t1 * head_az_e, w_t1 * head_az_e, na, nx)
    back_ax_t = head_ax_e[own_e] - step_dt * advect_back(u_t1 * head_ax_e, w_t1 * head_ax_e, na, nx)
    back_rad_b = head_rad_e[own_e] - step_dt * advect_back(u_b1 * head_rad_e, w_b1 * head_rad_e, na, nx)
    zero = jnp.zeros_like(back_press_b)
    extra = jnp.stack(
        [
            jnp.stack([back_press_b, back_press_t], axis=-1),
            jnp.stack([zero, back_az_t], axis=-1),
            jnp.stack([zero, back_ax_t], axis=-1),
            jnp.stack([back_rad_b, zero], axis=-1),
        ]
    )

    totals = butterfly_sum(first_round, ("az", "ax"), skip_first=True)
    mean_sq = totals[0] / mic_az.shape[0] + epsilon
    grad_scale = (na * lax.axis_size("az") * nx * lax.axis_size("ax") / nseg) ** (-0.5)
    liner_grad = (totals[1 : 1 + nseg] + totals[1 + nseg :] / mean_sq) * grad_scale
    misfit = 0.5 * jnp.log(mean_sq)
    lane = lax.broadcasted_iota(jnp.int32, (1, 1, 1, nr), 3)
    extra_scaled = extra / mean_sq
    correction = jnp.where(
        lane == nr - 1,
        extra_scaled[..., 1:2],
        jnp.where(lane == nr - 2, extra_scaled[..., 0:1], 0.0),
    )
    adjoint_out = base + correction
    return (adjoint_out, liner_grad, misfit)


def solution(mesh):
    placed = (
        P(None, "az", "ax", None),
        P(None, "az", "ax", None),
        P(None, "az", "ax", None),
        P(),
        P("az", "ax"),
        P("az", "ax"),
        P(),
        P(),
        P(),
        P(),
    )
    return jax.shard_map(
        shards,
        mesh=mesh,
        in_specs=placed,
        out_specs=(P(None, "az", "ax", None), P(), P()),
        check_vma=False,
    )
```

```python
import jax
import jax.numpy as jnp
from jax import lax
from jax.sharding import PartitionSpec as P

step_dt = 0.25
epsilon = 1e-06


def with_halo(array, axis, dim, before, after, wrap):
    size, length = (lax.axis_size(axis), array.shape[dim])
    up = [(i, (i + 1) % size) for i in range(size if wrap else size - 1)]
    down = [(j, i) for i, j in up]
    parts = []
    if before:
        parts.append(lax.ppermute(lax.slice_in_dim(array, length - before, length, axis=dim), axis, up))
    parts.append(array)
    if after:
        parts.append(lax.ppermute(lax.slice_in_dim(array, 0, after, axis=dim), axis, down))
    return jnp.concatenate(parts, axis=dim)


def exchange(array, before, after, ax_before=None, ax_after=None):
    ax_before = before if ax_before is None else ax_before
    ax_after = after if ax_after is None else ax_after
    widened = with_halo(array, "ax", 2, ax_before, ax_after, False)
    return with_halo(widened, "az", 1, before, after, True)


def win(values, origin, da, dx, na, nx):
    a0, x0 = origin[0] + da, origin[1] + dx
    return values[a0 : a0 + na, x0 : x0 + nx]


def rad_next(values):
    return jnp.concatenate([values[..., 1:], jnp.zeros_like(values[..., :1])], axis=-1)


def rad_prev(values):
    return jnp.concatenate([jnp.zeros_like(values[..., :1]), values[..., :-1]], axis=-1)


def casing_mask(shape):
    return lax.broadcasted_iota(jnp.int32, shape, len(shape) - 1) == shape[-1] - 1


def advect_back(carried_ax, carried_az, na, nx):
    return 0.5 * (carried_ax[..., 1 : 1 + na, 0:nx] - carried_ax[..., 1 : 1 + na, 2 : 2 + nx]) + 0.5 * (
        carried_az[..., 0:na, 1 : 1 + nx] - carried_az[..., 2 : 2 + na, 1 : 1 + nx]
    )


def advect_back4(carried_ax, carried_az, na, nx):
    return 0.5 * (carried_ax[:, 1 : 1 + na, 0:nx, :] - carried_ax[:, 1 : 1 + na, 2 : 2 + nx, :]) + 0.5 * (
        carried_az[:, 0:na, 1 : 1 + nx, :] - carried_az[:, 2 : 2 + na, 1 : 1 + nx, :]
    )


def butterfly_sum(values, axes, skip_first=False):
    for index, axis in enumerate(axes):
        size = lax.axis_size(axis)
        if size & (size - 1):
            values = lax.psum(values, axis)
            continue
        step = 2 if (skip_first and axis == "az") else 1
        while step < size:
            values = values + lax.ppermute(values, axis, [(i, i ^ step) for i in range(size)])
            step *= 2
    return values


def shards(
    acoustic,
    mean_flow,
    adjoint_in,
    admittance,
    segment_id,
    noise_code,
    noise_table,
    mic_az,
    mic_ax,
    measured,
):
    na, nx, nr = (acoustic.shape[1], acoustic.shape[2], acoustic.shape[3])
    nseg = admittance.shape[0]
    buoyancy = 1.0 / mean_flow[2]
    stiffness = mean_flow[2] * mean_flow[3] * mean_flow[3]
    axial_flow, swirl_flow = (mean_flow[0], mean_flow[1])

    segment_hot = segment_id[:, :, None] == lax.broadcasted_iota(jnp.int32, (1, 1, nseg), 2)
    wall = jnp.sum(jnp.where(segment_hot, admittance, 0.0), axis=2)
    noise_hot = noise_code[:, :, None] == lax.broadcasted_iota(jnp.int32, (1, 1, noise_table.shape[0]), 2)
    top_profile = (nr - 1 + 0.5) / nr
    source_top = jnp.sum(jnp.where(noise_hot, noise_table, 0.0), axis=2) * top_profile

    a0 = adjoint_in[0]
    push = -step_dt * stiffness * a0
    stack_f = jnp.stack([a0, adjoint_in[1], adjoint_in[2], adjoint_in[3], axial_flow, swirl_flow, buoyancy, push])
    top, below = nr - 1, nr - 2
    planes = [
        acoustic[0, :, :, top],
        acoustic[0, :, :, below],
        acoustic[1, :, :, top],
        acoustic[2, :, :, top],
        acoustic[3, :, :, below],
        axial_flow[:, :, top],
        axial_flow[:, :, below],
        swirl_flow[:, :, top],
        swirl_flow[:, :, below],
        buoyancy[:, :, top],
        buoyancy[:, :, below],
        stiffness[:, :, top],
        wall,
        source_top,
    ]
    stack_c = jnp.stack(planes)
    n_planes = len(planes)
    tile = 8
    reach = 3
    packed = jnp.pad(jnp.transpose(stack_c, (1, 2, 0)), ((0, 0), (0, 0), (0, nr - n_planes)))
    stack_all = jnp.concatenate([stack_f, packed[None]], axis=0)
    n_f = stack_f.shape[0]
    sent_x = jnp.concatenate([stack_all[:5], stack_all[6:]], axis=0)
    size_ax = lax.axis_size("ax")
    right = [(i, i + 1) for i in range(size_ax - 1)]
    left = [(j, i) for i, j in right]
    length_x = stack_all.shape[2]
    x_before = lax.ppermute(sent_x[:, :, length_x - tile :], "ax", right)
    x_after = lax.ppermute(jnp.concatenate([sent_x[:5, :, :tile], sent_x[6:, :, :tile]]), "ax", left)
    no_w = jnp.zeros_like(x_before[:1])
    x_before = jnp.concatenate([x_before[:5], no_w, x_before[5:]], axis=0)
    x_after = jnp.concatenate([x_after[:5], no_w, no_w, x_after[5:]], axis=0)
    widened = jnp.concatenate([x_before, stack_all, x_after], axis=2)
    size_az, length_a = (lax.axis_size("az"), widened.shape[1])
    up = [(i, (i + 1) % size_az) for i in range(size_az)]
    down = [(j, i) for i, j in up]
    sent_up = jnp.stack(
        [widened[f, length_a - 1] for f in (0, 1, 2, 3, 5, 6, 7)]
        + [widened[n_f, length_a - reach + k] for k in range(reach)]
    )
    sent_down = jnp.stack(
        [widened[f, 0] for f in (0, 1, 2, 3, 5, 7)] + [widened[7, 1]] + [widened[n_f, k] for k in range(reach)]
    )
    from_below = lax.ppermute(sent_up, "az", up)
    from_above = lax.ppermute(sent_down, "az", down)
    blank = jnp.zeros_like(from_below[0])
    row_before = jnp.stack([from_below[i] for i in (0, 1, 2, 3)] + [blank] + [from_below[i] for i in (4, 5, 6)])
    row_after = jnp.stack([from_above[i] for i in (0, 1, 2, 3)] + [blank, from_above[4], blank, from_above[5]])
    row_after2 = jnp.stack([blank] * 7 + [from_above[6]])
    wide_f = jnp.concatenate(
        [row_before[:, None], widened[:n_f], row_after[:, None], row_after2[:, None]], axis=1
    )
    wide_packed = jnp.concatenate([from_below[7:], widened[n_f], from_above[7:]], axis=0)
    wide_c = jnp.transpose(wide_packed[:, :, :n_planes], (2, 0, 1))

    oc = (reach, tile)
    p_t, p_b, va_t, vx_t, vr_b, u_t, u_b, w_t, w_b, b_t, b_b, s_t, wall_c, src_c = [wide_c[i] for i in range(14)]
    ea, ex = na + 3, nx + 3

    def c(f, da, dx, la, lx):
        return win(f, oc, da, dx, la, lx)

    def advect_c(f, u, w, da, dx, la, lx):
        return c(u, da, dx, la, lx) * (c(f, da, dx + 1, la, lx) - c(f, da, dx - 1, la, lx)) * 0.5 + c(
            w, da, dx, la, lx
        ) * (c(f, da + 1, dx, la, lx) - c(f, da - 1, dx, la, lx)) * 0.5

    new_az = c(va_t, -2, -1, ea + 1, ex) - step_dt * (
        advect_c(va_t, u_t, w_t, -2, -1, ea + 1, ex)
        + c(b_t, -2, -1, ea + 1, ex) * (c(p_t, -1, -1, ea + 1, ex) - c(p_t, -2, -1, ea + 1, ex))
    )
    new_ax = c(vx_t, -1, -2, ea, ex + 1) - step_dt * (
        advect_c(vx_t, u_t, w_t, -1, -2, ea, ex + 1)
        + c(b_t, -1, -2, ea, ex + 1) * (c(p_t, -1, -1, ea, ex + 1) - c(p_t, -1, -2, ea, ex + 1))
    )
    rad_top = c(wall_c, -1, -1, ea, ex) * c(p_t, -1, -1, ea, ex)
    rad_below = c(vr_b, -1, -1, ea, ex) - step_dt * (
        advect_c(vr_b, u_b, w_b, -1, -1, ea, ex)
        + c(b_b, -1, -1, ea, ex) * (c(p_t, -1, -1, ea, ex) - c(p_b, -1, -1, ea, ex))
    )
    spread = (new_az[1:] - new_az[:-1]) + (new_ax[:, 1:] - new_ax[:, :-1]) + (rad_top - rad_below)
    press_ring = (
        c(p_t, -1, -1, ea, ex)
        - step_dt * (advect_c(p_t, u_t, w_t, -1, -1, ea, ex) + c(s_t, -1, -1, ea, ex) * spread)
        + step_dt * c(src_c, -1, -1, ea, ex)
    )

    total_az = na * lax.axis_size("az")
    first_az = lax.axis_index("az") * na
    first_ax = lax.axis_index("ax") * nx
    ring_az = jnp.remainder(mic_az - first_az + 1, total_az)
    ring_ax = mic_ax - first_ax + 1
    on_ring = (ring_az < ea) & (ring_ax >= 0) & (ring_ax < ex)
    owned = (ring_az >= 1) & (ring_az <= na) & (ring_ax >= 1) & (ring_ax <= nx)
    ring_cell = jnp.where(on_ring, ring_az * ex + ring_ax, -1)
    cell_hot = ring_cell[:, None] == lax.broadcasted_iota(jnp.int32, (1, ea * ex), 1)
    heard = jnp.sum(jnp.where(cell_hot, press_ring.reshape(1, ea * ex), 0.0), axis=1)
    misses = heard - measured
    square_sum = jnp.sum(jnp.where(owned, misses * misses, 0.0))
    placed = jnp.sum(jnp.where(cell_hot, misses[:, None], 0.0), axis=0).reshape(ea, ex)

    of = (1, tile)
    g_a0, g_a1, g_a2, g_a3, g_u, g_w, g_b, g_push = [wide_f[i] for i in range(8)]

    def at(field, da, dx):
        return win(field, of, da, dx, na, nx)

    def head_az(da, dx):
        return at(g_a1, da, dx) + at(g_push, da, dx) - at(g_push, da + 1, dx)

    def head_ax(da, dx):
        return at(g_a2, da, dx) + at(g_push, da, dx) - at(g_push, da, dx + 1)

    casing = casing_mask((na, nx, nr))

    def head_rad(da, dx):
        push_here = at(g_push, da, dx)
        return at(g_a3, da, dx) + push_here - rad_next(push_here)

    def head_masked(da, dx):
        return jnp.where(casing, 0.0, head_rad(da, dx))

    def back_advect(head):
        return 0.5 * (at(g_u, 0, -1) * head(0, -1) - at(g_u, 0, 1) * head(0, 1)) + 0.5 * (
            at(g_w, -1, 0) * head(-1, 0) - at(g_w, 1, 0) * head(1, 0)
        )

    def seed(da, dx):
        return at(g_a0, da, dx)

    backs = [head(0, 0) - step_dt * back_advect(head) for head in (head_az, head_ax, head_masked)]
    shove_r = step_dt * at(g_b, 0, 0) * head_masked(0, 0)
    head_rad_own = head_rad(0, 0)
    back_press = (
        seed(0, 0)
        - step_dt * back_advect(seed)
        + (step_dt * at(g_b, 0, 0) * head_az(0, 0) - step_dt * at(g_b, -1, 0) * head_az(-1, 0))
        + (step_dt * at(g_b, 0, 0) * head_ax(0, 0) - step_dt * at(g_b, 0, -1) * head_ax(0, -1))
        + (shove_r - rad_prev(shove_r))
        + jnp.where(casing, wall[:, :, None] * head_rad_own, 0.0)
    )
    base = jnp.stack([back_press] + backs)

    late_rad, late_push, late_press, _ = lax.optimization_barrier((adjoint_in[3], push, acoustic[0], widened))
    press_top = late_press[:, :, top]
    sens_base = press_top * (late_rad[:, :, top] + late_push[:, :, top])
    sens_placed = press_top * (-step_dt * c(s_t, 0, 0, na, nx) * placed[1 : 1 + na, 1 : 1 + nx])
    slot = lax.broadcasted_iota(jnp.int32, (1, 1, 1 + 2 * nseg), 2)
    first_cell = (lax.broadcasted_iota(jnp.int32, (na, nx, 1), 0) == 0) & (
        lax.broadcasted_iota(jnp.int32, (na, nx, 1), 1) == 0
    )
    seg_here = segment_id[:, :, None]
    payload = jnp.sum(
        jnp.where(
            slot == 0,
            jnp.where(first_cell, square_sum, 0.0),
            jnp.where(
                slot <= nseg,
                jnp.where(seg_here == slot - 1, sens_base[:, :, None], 0.0),
                jnp.where(seg_here == slot - 1 - nseg, sens_placed[:, :, None], 0.0),
            ),
        ),
        axis=(0, 1),
    )

    size_az = lax.axis_size("az")
    first_round = payload + lax.ppermute(payload, "az", [(i, i ^ 1) for i in range(size_az)])
    placed, _ = lax.optimization_barrier((placed, first_round))
    push_e = -step_dt * c(s_t, -1, -1, ea, ex) * placed
    r1a, r1x = na + 2, nx + 2
    head_az_e = push_e[:r1a, :r1x] - push_e[1 : 1 + r1a, :r1x]
    head_ax_e = push_e[:r1a, :r1x] - push_e[:r1a, 1 : 1 + r1x]
    head_rad_e = -push_e[:r1a, :r1x]
    u_t1, w_t1 = c(u_t, -1, -1, r1a, r1x), c(w_t, -1, -1, r1a, r1x)
    u_b1, w_b1 = c(u_b, -1, -1, r1a, r1x), c(w_b, -1, -1, r1a, r1x)
    b_t1 = c(b_t, -1, -1, r1a, r1x)
    own_e = (slice(1, 1 + na), slice(1, 1 + nx))
    back_press_t = (
        placed[1 : 1 + na, 1 : 1 + nx]
        - step_dt * advect_back(u_t1 * placed[:r1a, :r1x], w_t1 * placed[:r1a, :r1x], na, nx)
    )
    shove_az = step_dt * b_t1 * head_az_e
    shove_ax = step_dt * b_t1 * head_ax_e
    b_b0, wall_0, push_0 = c(b_b, 0, 0, na, nx), c(wall_c, 0, 0, na, nx), push_e[own_e]
    back_press_t = (
        back_press_t
        + (shove_az[own_e] - shove_az[0:na, 1 : 1 + nx])
        + (shove_ax[own_e] - shove_ax[1 : 1 + na, 0:nx])
        + step_dt * b_b0 * push_0
        + wall_0 * push_0
    )
    back_press_b = -step_dt * b_b0 * push_0
    back_az_t = head_az_e[own_e] - step_dt * advect_back(u_t1 * head_az_e, w_t1 * head_az_e, na, nx)
    back_ax_t = head_ax_e[own_e] - step_dt * advect_back(u_t1 * head_ax_e, w_t1 * head_ax_e, na, nx)
    back_rad_b = head_rad_e[own_e] - step_dt * advect_back(u_b1 * head_rad_e, w_b1 * head_rad_e, na, nx)
    zero = jnp.zeros_like(back_press_b)
    extra = jnp.stack(
        [
            jnp.stack([back_press_b, back_press_t], axis=-1),
            jnp.stack([zero, back_az_t], axis=-1),
            jnp.stack([zero, back_ax_t], axis=-1),
            jnp.stack([back_rad_b, zero], axis=-1),
        ]
    )

    totals = butterfly_sum(first_round, ("ax", "az"), skip_first=True)
    mean_sq = totals[0] / mic_az.shape[0] + epsilon
    grad_scale = (na * lax.axis_size("az") * nx * lax.axis_size("ax") / nseg) ** (-0.5)
    liner_grad = (totals[1 : 1 + nseg] + totals[1 + nseg :] / mean_sq) * grad_scale
    misfit = 0.5 * jnp.log(mean_sq)
    lane = lax.broadcasted_iota(jnp.int32, (1, 1, 1, nr), 3)
    extra_scaled = extra / mean_sq
    correction = jnp.where(
        lane == nr - 1,
        extra_scaled[..., 1:2],
        jnp.where(lane == nr - 2, extra_scaled[..., 0:1], 0.0),
    )
    adjoint_out = base + correction
    return (adjoint_out, liner_grad, misfit)


def solution(mesh):
    placed = (
        P(None, "az", "ax", None),
        P(None, "az", "ax", None),
        P(None, "az", "ax", None),
        P(),
        P("az", "ax"),
        P("az", "ax"),
        P(),
        P(),
        P(),
        P(),
    )
    return jax.shard_map(
        shards,
        mesh=mesh,
        in_specs=placed,
        out_specs=(P(None, "az", "ax", None), P(), P()),
        check_vma=False,
    )
```

```python
import jax
import jax.numpy as jnp
from jax import lax
from jax.sharding import PartitionSpec as P

step_dt = 0.25
epsilon = 1e-06


def with_halo(array, axis, dim, before, after, wrap):
    size, length = (lax.axis_size(axis), array.shape[dim])
    up = [(i, (i + 1) % size) for i in range(size if wrap else size - 1)]
    down = [(j, i) for i, j in up]
    parts = []
    if before:
        parts.append(lax.ppermute(lax.slice_in_dim(array, length - before, length, axis=dim), axis, up))
    parts.append(array)
    if after:
        parts.append(lax.ppermute(lax.slice_in_dim(array, 0, after, axis=dim), axis, down))
    return jnp.concatenate(parts, axis=dim)


def exchange(array, before, after, ax_before=None, ax_after=None):
    ax_before = before if ax_before is None else ax_before
    ax_after = after if ax_after is None else ax_after
    widened = with_halo(array, "ax", 2, ax_before, ax_after, False)
    return with_halo(widened, "az", 1, before, after, True)


def win(values, origin, da, dx, na, nx):
    a0, x0 = origin[0] + da, origin[1] + dx
    return values[a0 : a0 + na, x0 : x0 + nx]


def rad_next(values):
    return jnp.concatenate([values[..., 1:], jnp.zeros_like(values[..., :1])], axis=-1)


def rad_prev(values):
    return jnp.concatenate([jnp.zeros_like(values[..., :1]), values[..., :-1]], axis=-1)


def casing_mask(shape):
    return lax.broadcasted_iota(jnp.int32, shape, len(shape) - 1) == shape[-1] - 1


def advect_back(carried_ax, carried_az, na, nx):
    return 0.5 * (carried_ax[..., 1 : 1 + na, 0:nx] - carried_ax[..., 1 : 1 + na, 2 : 2 + nx]) + 0.5 * (
        carried_az[..., 0:na, 1 : 1 + nx] - carried_az[..., 2 : 2 + na, 1 : 1 + nx]
    )


def advect_back4(carried_ax, carried_az, na, nx):
    return 0.5 * (carried_ax[:, 1 : 1 + na, 0:nx, :] - carried_ax[:, 1 : 1 + na, 2 : 2 + nx, :]) + 0.5 * (
        carried_az[:, 0:na, 1 : 1 + nx, :] - carried_az[:, 2 : 2 + na, 1 : 1 + nx, :]
    )


def butterfly_sum(values, axes, skip_first=False):
    for index, axis in enumerate(axes):
        size = lax.axis_size(axis)
        if size & (size - 1):
            values = lax.psum(values, axis)
            continue
        step = 2 if (skip_first and axis == "ax") else 1
        while step < size:
            values = values + lax.ppermute(values, axis, [(i, i ^ step) for i in range(size)])
            step *= 2
    return values


def shards(
    acoustic,
    mean_flow,
    adjoint_in,
    admittance,
    segment_id,
    noise_code,
    noise_table,
    mic_az,
    mic_ax,
    measured,
):
    na, nx, nr = (acoustic.shape[1], acoustic.shape[2], acoustic.shape[3])
    nseg = admittance.shape[0]
    buoyancy = 1.0 / mean_flow[2]
    stiffness = mean_flow[2] * mean_flow[3] * mean_flow[3]
    axial_flow, swirl_flow = (mean_flow[0], mean_flow[1])

    segment_hot = segment_id[:, :, None] == lax.broadcasted_iota(jnp.int32, (1, 1, nseg), 2)
    wall = jnp.sum(jnp.where(segment_hot, admittance, 0.0), axis=2)
    noise_hot = noise_code[:, :, None] == lax.broadcasted_iota(jnp.int32, (1, 1, noise_table.shape[0]), 2)
    top_profile = (nr - 1 + 0.5) / nr
    source_top = jnp.sum(jnp.where(noise_hot, noise_table, 0.0), axis=2) * top_profile

    a0 = adjoint_in[0]
    push = -step_dt * stiffness * a0
    stack_f = jnp.stack([a0, adjoint_in[1], adjoint_in[2], adjoint_in[3], axial_flow, swirl_flow, buoyancy, push])
    top, below = nr - 1, nr - 2
    planes = [
        acoustic[0, :, :, top],
        acoustic[0, :, :, below],
        acoustic[1, :, :, top],
        acoustic[2, :, :, top],
        acoustic[3, :, :, below],
        axial_flow[:, :, top],
        axial_flow[:, :, below],
        swirl_flow[:, :, top],
        swirl_flow[:, :, below],
        buoyancy[:, :, top],
        buoyancy[:, :, below],
        stiffness[:, :, top],
        wall,
        source_top,
    ]
    stack_c = jnp.stack(planes)
    n_planes = len(planes)
    tile = 8
    reach = 3
    packed = jnp.pad(jnp.transpose(stack_c, (1, 2, 0)), ((0, 0), (0, 0), (0, nr - n_planes)))
    stack_all = jnp.concatenate([stack_f, packed[None]], axis=0)
    n_f = stack_f.shape[0]
    sent_x = jnp.concatenate([stack_all[:5], stack_all[6:]], axis=0)
    size_ax = lax.axis_size("ax")
    right = [(i, i + 1) for i in range(size_ax - 1)]
    left = [(j, i) for i, j in right]
    length_x = stack_all.shape[2]
    x_before = lax.ppermute(sent_x[:, :, length_x - tile :], "ax", right)
    x_after = lax.ppermute(jnp.concatenate([sent_x[:5, :, :tile], sent_x[6:, :, :tile]]), "ax", left)
    no_w = jnp.zeros_like(x_before[:1])
    x_before = jnp.concatenate([x_before[:5], no_w, x_before[5:]], axis=0)
    x_after = jnp.concatenate([x_after[:5], no_w, no_w, x_after[5:]], axis=0)
    widened = jnp.concatenate([x_before, stack_all, x_after], axis=2)
    size_az, length_a = (lax.axis_size("az"), widened.shape[1])
    up = [(i, (i + 1) % size_az) for i in range(size_az)]
    down = [(j, i) for i, j in up]
    sent_up = jnp.stack(
        [widened[f, length_a - 1] for f in (0, 1, 2, 3, 5, 6, 7)]
        + [widened[n_f, length_a - reach + k] for k in range(reach)]
    )
    sent_down = jnp.stack(
        [widened[f, 0] for f in (0, 1, 2, 3, 5, 7)] + [widened[7, 1]] + [widened[n_f, k] for k in range(reach)]
    )
    from_below = lax.ppermute(sent_up, "az", up)
    from_above = lax.ppermute(sent_down, "az", down)
    blank = jnp.zeros_like(from_below[0])
    row_before = jnp.stack([from_below[i] for i in (0, 1, 2, 3)] + [blank] + [from_below[i] for i in (4, 5, 6)])
    row_after = jnp.stack([from_above[i] for i in (0, 1, 2, 3)] + [blank, from_above[4], blank, from_above[5]])
    row_after2 = jnp.stack([blank] * 7 + [from_above[6]])
    wide_f = jnp.concatenate(
        [row_before[:, None], widened[:n_f], row_after[:, None], row_after2[:, None]], axis=1
    )
    wide_packed = jnp.concatenate([from_below[7:], widened[n_f], from_above[7:]], axis=0)
    wide_c = jnp.transpose(wide_packed[:, :, :n_planes], (2, 0, 1))

    oc = (reach, tile)
    p_t, p_b, va_t, vx_t, vr_b, u_t, u_b, w_t, w_b, b_t, b_b, s_t, wall_c, src_c = [wide_c[i] for i in range(14)]
    ea, ex = na + 3, nx + 3

    def c(f, da, dx, la, lx):
        return win(f, oc, da, dx, la, lx)

    def advect_c(f, u, w, da, dx, la, lx):
        return c(u, da, dx, la, lx) * (c(f, da, dx + 1, la, lx) - c(f, da, dx - 1, la, lx)) * 0.5 + c(
            w, da, dx, la, lx
        ) * (c(f, da + 1, dx, la, lx) - c(f, da - 1, dx, la, lx)) * 0.5

    new_az = c(va_t, -2, -1, ea + 1, ex) - step_dt * (
        advect_c(va_t, u_t, w_t, -2, -1, ea + 1, ex)
        + c(b_t, -2, -1, ea + 1, ex) * (c(p_t, -1, -1, ea + 1, ex) - c(p_t, -2, -1, ea + 1, ex))
    )
    new_ax = c(vx_t, -1, -2, ea, ex + 1) - step_dt * (
        advect_c(vx_t, u_t, w_t, -1, -2, ea, ex + 1)
        + c(b_t, -1, -2, ea, ex + 1) * (c(p_t, -1, -1, ea, ex + 1) - c(p_t, -1, -2, ea, ex + 1))
    )
    rad_top = c(wall_c, -1, -1, ea, ex) * c(p_t, -1, -1, ea, ex)
    rad_below = c(vr_b, -1, -1, ea, ex) - step_dt * (
        advect_c(vr_b, u_b, w_b, -1, -1, ea, ex)
        + c(b_b, -1, -1, ea, ex) * (c(p_t, -1, -1, ea, ex) - c(p_b, -1, -1, ea, ex))
    )
    spread = (new_az[1:] - new_az[:-1]) + (new_ax[:, 1:] - new_ax[:, :-1]) + (rad_top - rad_below)
    press_ring = (
        c(p_t, -1, -1, ea, ex)
        - step_dt * (advect_c(p_t, u_t, w_t, -1, -1, ea, ex) + c(s_t, -1, -1, ea, ex) * spread)
        + step_dt * c(src_c, -1, -1, ea, ex)
    )

    total_az = na * lax.axis_size("az")
    first_az = lax.axis_index("az") * na
    first_ax = lax.axis_index("ax") * nx
    ring_az = jnp.remainder(mic_az - first_az + 1, total_az)
    ring_ax = mic_ax - first_ax + 1
    on_ring = (ring_az < ea) & (ring_ax >= 0) & (ring_ax < ex)
    owned = (ring_az >= 1) & (ring_az <= na) & (ring_ax >= 1) & (ring_ax <= nx)
    ring_cell = jnp.where(on_ring, ring_az * ex + ring_ax, -1)
    cell_hot = ring_cell[:, None] == lax.broadcasted_iota(jnp.int32, (1, ea * ex), 1)
    heard = jnp.sum(jnp.where(cell_hot, press_ring.reshape(1, ea * ex), 0.0), axis=1)
    misses = heard - measured
    square_sum = jnp.sum(jnp.where(owned, misses * misses, 0.0))
    placed = jnp.sum(jnp.where(cell_hot, misses[:, None], 0.0), axis=0).reshape(ea, ex)

    of = (1, tile)
    g_a0, g_a1, g_a2, g_a3, g_u, g_w, g_b, g_push = [wide_f[i] for i in range(8)]

    def at(field, da, dx):
        return win(field, of, da, dx, na, nx)

    def head_az(da, dx):
        return at(g_a1, da, dx) + at(g_push, da, dx) - at(g_push, da + 1, dx)

    def head_ax(da, dx):
        return at(g_a2, da, dx) + at(g_push, da, dx) - at(g_push, da, dx + 1)

    casing = casing_mask((na, nx, nr))

    def head_rad(da, dx):
        push_here = at(g_push, da, dx)
        return at(g_a3, da, dx) + push_here - rad_next(push_here)

    def head_masked(da, dx):
        return jnp.where(casing, 0.0, head_rad(da, dx))

    def back_advect(head):
        return 0.5 * (at(g_u, 0, -1) * head(0, -1) - at(g_u, 0, 1) * head(0, 1)) + 0.5 * (
            at(g_w, -1, 0) * head(-1, 0) - at(g_w, 1, 0) * head(1, 0)
        )

    def seed(da, dx):
        return at(g_a0, da, dx)

    backs = [head(0, 0) - step_dt * back_advect(head) for head in (head_az, head_ax, head_masked)]
    shove_r = step_dt * at(g_b, 0, 0) * head_masked(0, 0)
    head_rad_own = head_rad(0, 0)
    back_press = (
        seed(0, 0)
        - step_dt * back_advect(seed)
        + (step_dt * at(g_b, 0, 0) * head_az(0, 0) - step_dt * at(g_b, -1, 0) * head_az(-1, 0))
        + (step_dt * at(g_b, 0, 0) * head_ax(0, 0) - step_dt * at(g_b, 0, -1) * head_ax(0, -1))
        + (shove_r - rad_prev(shove_r))
        + jnp.where(casing, wall[:, :, None] * head_rad_own, 0.0)
    )
    base = jnp.stack([back_press] + backs)

    late_rad, late_push, late_press, _ = lax.optimization_barrier((adjoint_in[3], push, acoustic[0], widened))
    press_top = late_press[:, :, top]
    sens_base = press_top * (late_rad[:, :, top] + late_push[:, :, top])
    sens_placed = press_top * (-step_dt * c(s_t, 0, 0, na, nx) * placed[1 : 1 + na, 1 : 1 + nx])
    slot = lax.broadcasted_iota(jnp.int32, (1, 1, 1 + 2 * nseg), 2)
    first_cell = (lax.broadcasted_iota(jnp.int32, (na, nx, 1), 0) == 0) & (
        lax.broadcasted_iota(jnp.int32, (na, nx, 1), 1) == 0
    )
    seg_here = segment_id[:, :, None]
    payload = jnp.sum(
        jnp.where(
            slot == 0,
            jnp.where(first_cell, square_sum, 0.0),
            jnp.where(
                slot <= nseg,
                jnp.where(seg_here == slot - 1, sens_base[:, :, None], 0.0),
                jnp.where(seg_here == slot - 1 - nseg, sens_placed[:, :, None], 0.0),
            ),
        ),
        axis=(0, 1),
    )

    size_ax_first = lax.axis_size("ax")
    first_round = payload + lax.ppermute(payload, "ax", [(i, i ^ 1) for i in range(size_ax_first)])
    placed, _ = lax.optimization_barrier((placed, first_round))
    push_e = -step_dt * c(s_t, -1, -1, ea, ex) * placed
    r1a, r1x = na + 2, nx + 2
    head_az_e = push_e[:r1a, :r1x] - push_e[1 : 1 + r1a, :r1x]
    head_ax_e = push_e[:r1a, :r1x] - push_e[:r1a, 1 : 1 + r1x]
    head_rad_e = -push_e[:r1a, :r1x]
    u_t1, w_t1 = c(u_t, -1, -1, r1a, r1x), c(w_t, -1, -1, r1a, r1x)
    u_b1, w_b1 = c(u_b, -1, -1, r1a, r1x), c(w_b, -1, -1, r1a, r1x)
    b_t1 = c(b_t, -1, -1, r1a, r1x)
    own_e = (slice(1, 1 + na), slice(1, 1 + nx))
    back_press_t = (
        placed[1 : 1 + na, 1 : 1 + nx]
        - step_dt * advect_back(u_t1 * placed[:r1a, :r1x], w_t1 * placed[:r1a, :r1x], na, nx)
    )
    shove_az = step_dt * b_t1 * head_az_e
    shove_ax = step_dt * b_t1 * head_ax_e
    b_b0, wall_0, push_0 = c(b_b, 0, 0, na, nx), c(wall_c, 0, 0, na, nx), push_e[own_e]
    back_press_t = (
        back_press_t
        + (shove_az[own_e] - shove_az[0:na, 1 : 1 + nx])
        + (shove_ax[own_e] - shove_ax[1 : 1 + na, 0:nx])
        + step_dt * b_b0 * push_0
        + wall_0 * push_0
    )
    back_press_b = -step_dt * b_b0 * push_0
    back_az_t = head_az_e[own_e] - step_dt * advect_back(u_t1 * head_az_e, w_t1 * head_az_e, na, nx)
    back_ax_t = head_ax_e[own_e] - step_dt * advect_back(u_t1 * head_ax_e, w_t1 * head_ax_e, na, nx)
    back_rad_b = head_rad_e[own_e] - step_dt * advect_back(u_b1 * head_rad_e, w_b1 * head_rad_e, na, nx)
    zero = jnp.zeros_like(back_press_b)
    extra = jnp.stack(
        [
            jnp.stack([back_press_b, back_press_t], axis=-1),
            jnp.stack([zero, back_az_t], axis=-1),
            jnp.stack([zero, back_ax_t], axis=-1),
            jnp.stack([back_rad_b, zero], axis=-1),
        ]
    )

    totals = butterfly_sum(first_round, ("az", "ax"), skip_first=True)
    mean_sq = totals[0] / mic_az.shape[0] + epsilon
    grad_scale = (na * lax.axis_size("az") * nx * lax.axis_size("ax") / nseg) ** (-0.5)
    liner_grad = (totals[1 : 1 + nseg] + totals[1 + nseg :] / mean_sq) * grad_scale
    misfit = 0.5 * jnp.log(mean_sq)
    lane = lax.broadcasted_iota(jnp.int32, (1, 1, 1, nr), 3)
    extra_scaled = extra / mean_sq
    correction = jnp.where(
        lane == nr - 1,
        extra_scaled[..., 1:2],
        jnp.where(lane == nr - 2, extra_scaled[..., 0:1], 0.0),
    )
    adjoint_out = base + correction
    return (adjoint_out, liner_grad, misfit)


def solution(mesh):
    placed = (
        P(None, "az", "ax", None),
        P(None, "az", "ax", None),
        P(None, "az", "ax", None),
        P(),
        P("az", "ax"),
        P("az", "ax"),
        P(),
        P(),
        P(),
        P(),
    )
    return jax.shard_map(
        shards,
        mesh=mesh,
        in_specs=placed,
        out_specs=(P(None, "az", "ax", None), P(), P()),
        check_vma=False,
    )
```
